32 devices in a mesh: depth: 4 (over y, x), row: 4 (over z), col: 2 (over core).
Axes of the slice: x: 2, y: 2, z: 4, core: 2. Of those that a mesh axis runs over, the one named last changes fastest.
Arguments:
- phase: float32 [4, 1024, 512], P('depth', 'row', 'col'), may hold values from -4 to 4
- absorption: float32 [4, 1024, 512], P('depth', 'row', 'col'), may hold values from 0 to 0.5
- probe: float32 [2, 256, 256], replicated, may hold values from -4 to 4
- measured: float32 [4, 2, 4, 256, 256], P('row', 'col'), may hold values from 0 to 3
- offsets: int32 [4, 2, 4, 2], P('row', 'col'), may hold values from -128 to 896, as said below
Outputs:
- grad_phase: float32 [4, 1024, 512], P('depth', 'row', 'col')
- grad_absorption: float32 [4, 1024, 512], P('depth', 'row', 'col')
The draws below stay inside these ranges and needn't reach their ends.
Inputs may be any that keep to these rules, and one draw needn't show every extreme that they name: `offsets`: probe k of tile (i, j) has row i * 256 + s, with s in -128 .. -1 when k mod 4 is 0 or 1 and in 1 .. 128 otherwise; its column is j * 256 + t, with t in -128 .. -1 for even k and in 1 .. 128 for odd k.
All inputs are finite; a program needn't handle non-finite values.
Results may differ from the reference program's by a relative error of at most 0.0003.
Values sent between devices are 32-bit elements; how exact they have to be, the bound alone decides.
No kernel may reach another device: no remote copies, remote signals or barrier semaphores. Data moves between devices by JAX's collectives and lax.ppermute only.
A program may use at most 128 MiB of HBM per device.

```python
import math
import jax
import jax.numpy as jnp
from jax import lax

W = 256
HALO = 128
PROBES_DEV = 4
TR = 256
TC = 256
SLICES = 4
TILES_R = 4
TILES_C = 2
NR = 1024
NC = 512


def draw_offsets(key, part):
    rows_key, cols_key = jax.random.split(key)
    shape = (TILES_R, TILES_C, PROBES_DEV)
    probe_index = jnp.arange(PROBES_DEV, dtype=jnp.int32)
    row_side = probe_index % 4 // 2
    col_side = probe_index % 2
    row_draw = jax.random.randint(rows_key, shape, 0, HALO, dtype=jnp.int32)
    col_draw = jax.random.randint(cols_key, shape, 0, HALO, dtype=jnp.int32)
    row_local = jnp.where(row_side[None, None, :] == 1, TR - W + 1 + row_draw, row_draw - HALO)
    col_local = jnp.where(col_side[None, None, :] == 1, TC - W + 1 + col_draw, col_draw - HALO)
    row_global = jnp.arange(TILES_R, dtype=jnp.int32)[:, None, None] * TR + row_local
    col_global = jnp.arange(TILES_C, dtype=jnp.int32)[None, :, None] * TC + col_local
    row_global = row_global.at[0, 0, 0].set(-HALO)
    col_global = col_global.at[0, 0, 0].set(-HALO)
    row_global = row_global.at[TILES_R - 1, 0, 2].set(TILES_R * TR - W + HALO)
    col_global = col_global.at[0, TILES_C - 1, 1].set(TILES_C * TC - W + HALO)
    return jnp.stack((row_global, col_global), axis=-1).astype(jnp.int32)


def steps_of(key, dims, shards, least, largest):
    loudness = 1.0
    for axis_at, parts in shards:
        draws = jax.random.uniform(jax.random.fold_in(jax.random.fold_in(key, 6), axis_at), (parts,), jnp.float32, least / len(shards), largest / len(shards))
        loudness = loudness * jnp.repeat(jnp.exp(draws), dims[axis_at] // parts).reshape((-1,) + (1,) * (len(dims) - 1 - axis_at))
    return loudness


def normal_values(own_key, dims, scale, reach, cuts=(), kind=jnp.bfloat16):
    values = jax.random.normal(own_key, dims, jnp.float32) * scale
    if len(cuts) > 0:
        values = steps_of(own_key, dims, cuts, -0.22, 0.18) * values
    return jnp.clip(values, min=-reach, max=reach).astype(kind)


def setup_inputs(seed: int = 0) -> dict:
    keys = jax.random.split(jax.random.key(seed), 6)
    return {
        "phase": normal_values(keys[0], (SLICES, NR, NC), 1.0, 4.0, ((0, 4), (1, 4), (2, 2)), jnp.float32),
        "absorption": jnp.clip(0.5 * jax.random.uniform(keys[1], (SLICES, NR, NC), jnp.float32) ** steps_of(keys[1], (SLICES, NR, NC), ((0, 4), (1, 4), (2, 2)), -0.2, 0.2), 0.0, 0.5),
        "probe": normal_values(keys[2], (2, W, W), 0.7, 4.0, (), jnp.float32),
        "measured": jnp.clip(3.0 * jax.random.uniform(keys[3], (TILES_R, TILES_C, PROBES_DEV, W, W), jnp.float32) ** steps_of(keys[3], (TILES_R, TILES_C, PROBES_DEV, W, W), ((0, 4), (1, 2)), -0.2, 0.2), 0.0, 3.0),
        "offsets": draw_offsets(jax.random.fold_in(keys[5], 71), 0),
    }


def chirp_factor():
    index = jnp.arange(W, dtype=jnp.int32)
    signed = jnp.where(index < W // 2, index, index - W)
    angle = -(signed * signed % (4 * W)).astype(jnp.float32) * (2.0 * math.pi / (4 * W))
    line = lax.complex(jnp.cos(angle), jnp.sin(angle))
    return line[:, None] * line[None, :]

def probe_loss(win_phase, win_absorb, probe, measured, chirp):
    damping = jnp.exp(-win_absorb)
    transmit = lax.complex(damping * jnp.cos(win_phase), damping * jnp.sin(win_phase))
    wave = lax.complex(probe[0], probe[1])
    far = wave
    for layer in range(SLICES):
        moved = transmit[layer] * wave
        if layer < SLICES - 1:
            wave = jnp.fft.ifft2(jnp.fft.fft2(moved) * chirp)
        else:
            far = jnp.fft.fft2(moved, norm='ortho')
    power = jnp.real(far) ** 2 + jnp.imag(far) ** 2
    return jnp.sum((power - measured) ** 2) / 16.0

def reference(phase, absorption, probe, measured, offsets):
    widths = ((0, 0), (HALO, HALO), (HALO, HALO))
    phase_pad = jnp.pad(phase, widths)
    absorb_pad = jnp.pad(absorption, widths)
    chirp = chirp_factor()
    flat_offsets = offsets.reshape(-1, 2)
    flat_measured = measured.reshape(-1, W, W)
    grad_fn = jax.grad(probe_loss, argnums=(0, 1))

    def visit(carry, item):
        grad_phase, grad_absorb = carry
        corner, target = item
        start = (jnp.zeros((), jnp.int32), (corner[0] + HALO).astype(jnp.int32), (corner[1] + HALO).astype(jnp.int32))
        win_phase = lax.dynamic_slice(phase_pad, start, (SLICES, W, W))
        win_absorb = lax.dynamic_slice(absorb_pad, start, (SLICES, W, W))
        part_phase, part_absorb = grad_fn(win_phase, win_absorb, probe, target, chirp)
        grad_phase = lax.dynamic_update_slice(grad_phase, lax.dynamic_slice(grad_phase, start, (SLICES, W, W)) + part_phase, start)
        grad_absorb = lax.dynamic_update_slice(grad_absorb, lax.dynamic_slice(grad_absorb, start, (SLICES, W, W)) + part_absorb, start)
        return ((grad_phase, grad_absorb), None)
    initial = (jnp.zeros_like(phase_pad), jnp.zeros_like(absorb_pad))
    (grad_phase, grad_absorb), _ = lax.scan(visit, initial, (flat_offsets, flat_measured))
    return (grad_phase[:, HALO:HALO + NR, HALO:HALO + NC], grad_absorb[:, HALO:HALO + NR, HALO:HALO + NC])
```

```python
import math

import jax
import jax.numpy as jnp
from jax import lax
from jax.sharding import PartitionSpec as P

exact_mode = lax.Precision.HIGHEST


def from_behind(value, axis, steps):
    count = lax.axis_size(axis)
    leading, last = (max(0, -steps), min(count, count - steps))
    return lax.ppermute(value, axis, [(source, source + steps) for source in range(leading, last)])


def with_halo(block, sides, width):
    for axis, dim in sides:
        count = lax.axis_size(axis)
        forward = [(i, i + 1) for i in range(count - 1)]
        backward = [(target, source) for source, target in forward]
        low = lax.ppermute(
            lax.slice_in_dim(block, block.shape[dim] - width, None, axis=dim), axis, forward
        )
        high = lax.ppermute(lax.slice_in_dim(block, 0, width, axis=dim), axis, backward)
        block = jnp.concatenate([low, block, high], axis=dim)
    return block


def matmul_exact(first, second):
    return jnp.dot(first, second, precision=exact_mode, preferred_element_type=jnp.float32)


def build_tables(width):
    index = jnp.arange(width, dtype=jnp.int32)
    product = index[:, None] * index[None, :] % width
    angle = product.astype(jnp.float32) * (2.0 * math.pi / width)
    cosine = jnp.cos(angle)
    sine = jnp.sin(angle)
    signed = jnp.where(index < width // 2, index, index - width)
    chirp = -(signed * signed % (4 * width)).astype(jnp.float32) * (2.0 * math.pi / (4 * width))
    chirp_re = jnp.cos(chirp)[None, :]
    chirp_im = jnp.sin(chirp)[None, :]
    scaled_re = cosine * chirp_re - sine * chirp_im
    scaled_im = cosine * chirp_im + sine * chirp_re
    fresnel_re = matmul_exact(scaled_re, cosine) + matmul_exact(scaled_im, sine)
    fresnel_im = matmul_exact(scaled_im, cosine) - matmul_exact(scaled_re, sine)
    fresnel = jnp.stack((fresnel_re, fresnel_im)) / width
    far_field = jnp.stack((cosine, -sine)) / math.sqrt(width)
    return (fresnel, far_field)


def adjoint_of(matrix):
    return jnp.stack((matrix[0].T, -matrix[1].T))


def left_product(matrix, waves):
    return jnp.einsum(
        "ij,bjk->bik", matrix, waves, precision=exact_mode, preferred_element_type=jnp.float32
    )


def right_product(waves, matrix):
    return jnp.einsum(
        "bij,kj->bik", waves, matrix, precision=exact_mode, preferred_element_type=jnp.float32
    )


def propagate(matrix, waves):
    width = matrix.shape[1]
    tall = matrix.reshape(2 * width, width)
    from_real = left_product(tall, waves[0])
    from_imag = left_product(tall, waves[1])
    inner_re = from_real[:, :width] - from_imag[:, width:]
    inner_im = from_real[:, width:] + from_imag[:, :width]
    right_re = right_product(inner_re, tall)
    right_im = right_product(inner_im, tall)
    outer_re = right_re[:, :, :width] - right_im[:, :, width:]
    outer_im = right_re[:, :, width:] + right_im[:, :, :width]
    return jnp.stack((outer_re, outer_im))


def forward_layers(wave, slab, matrices):
    moved_list = []
    for layer in range(slab.shape[1]):
        trans_re = slab[0, layer]
        trans_im = slab[1, layer]
        moved = jnp.stack(
            (trans_re * wave[0] - trans_im * wave[1], trans_re * wave[1] + trans_im * wave[0])
        )
        moved_list.append(moved)
        wave = propagate(matrices[layer], moved)
    return (wave, jnp.stack(moved_list, axis=1))


def backward_layers(grad, slab, moved, adjoints):
    layers = slab.shape[1]
    phase_parts = [None] * layers
    absorb_parts = [None] * layers
    for layer in reversed(range(layers)):
        grad_moved = propagate(adjoints[layer], grad)
        moved_re = moved[0, layer]
        moved_im = moved[1, layer]
        phase_parts[layer] = grad_moved[1] * moved_re - grad_moved[0] * moved_im
        absorb_parts[layer] = -(grad_moved[0] * moved_re + grad_moved[1] * moved_im)
        trans_re = slab[0, layer]
        trans_im = slab[1, layer]
        grad = jnp.stack(
            (
                trans_re * grad_moved[0] + trans_im * grad_moved[1],
                trans_re * grad_moved[1] - trans_im * grad_moved[0],
            )
        )
    return (grad, jnp.stack(phase_parts), jnp.stack(absorb_parts))


def pass_rows_all(strip, steps):
    return from_behind(strip, "row", steps)


def pass_cols_all(strip, steps):
    return from_behind(strip, "col", steps)


def fold_rows(grid, rim, mover):
    inner = grid.shape[2] - 2 * rim
    from_above = mover(grid[:, :, inner + rim :], 1)
    from_below = mover(grid[:, :, :rim], -1)
    core = grid[:, :, rim : rim + inner]
    core = core.at[:, :, :rim].add(from_above)
    return core.at[:, :, inner - rim :].add(from_below)


def fold_cols(grid, rim, mover):
    inner = grid.shape[3] - 2 * rim
    from_left = mover(grid[:, :, :, inner + rim :], 1)
    from_right = mover(grid[:, :, :, :rim], -1)
    core = grid[:, :, :, rim : rim + inner]
    core = core.at[:, :, :, :rim].add(from_left)
    return core.at[:, :, :, inner - rim :].add(from_right)


def fold_both(grid, rim, row_mover, col_mover):
    return fold_cols(fold_rows(grid, rim, row_mover), rim, col_mover)


def to_transmit(extended):
    damping = jnp.exp(-extended[1])
    return jnp.stack((damping * jnp.cos(extended[0]), damping * jnp.sin(extended[0])))


def place(patch, row, col, frame):
    height, span = frame
    extra_rows = height - patch.shape[-2]
    extra_cols = span - patch.shape[-1]
    padded = jnp.pad(patch, ((0, 0), (0, 0), (extra_rows, extra_rows), (extra_cols, extra_cols)))
    anchor = jnp.zeros((), jnp.int32)
    start = (anchor, anchor, extra_rows - row, extra_cols - col)
    return lax.dynamic_slice(padded, start, patch.shape[:2] + (height, span))


def per_device(phase, absorption, probe, measured, offsets):
    layers, tile_rows, tile_cols = phase.shape
    width = probe.shape[1]
    rim = width // 2
    probes = offsets.shape[2]
    depth_count = lax.axis_size("depth")
    depth_index = lax.axis_index("depth")
    row_index = lax.axis_index("row")
    col_index = lax.axis_index("col")
    stacked = jnp.stack((phase, absorption))
    extended = with_halo(stacked, (("row", 2), ("col", 3)), rim)
    corners = offsets[0, 0]
    row_starts = corners[:, 0] - row_index * tile_rows + rim
    col_starts = corners[:, 1] - col_index * tile_cols + rim
    anchor = jnp.zeros((), jnp.int32)
    fresnel, far_field = build_tables(width)
    share = probes // depth_count
    first = depth_index * share
    cut = jnp.stack(
        [
            lax.dynamic_slice(
                extended, (anchor, anchor, row_starts[k], col_starts[k]), (2, layers, width, width)
            )
            for k in range(probes)
        ],
        axis=2,
    )
    gathered = lax.all_to_all(cut, "depth", 2, 1, tiled=True)
    windows = to_transmit(gathered)
    total_layers = windows.shape[1]
    matrices = [fresnel] * (total_layers - 1) + [far_field]
    adjoints = [adjoint_of(matrix) for matrix in matrices]
    start_wave = probe[:, None]
    far_wave, moved = forward_layers(start_wave, windows, matrices)
    target = lax.dynamic_slice_in_dim(measured[0, 0], first, share)
    power = far_wave[0] ** 2 + far_wave[1] ** 2
    detector = far_wave * (0.25 * (power - target))[None]
    unused, phase_grad, absorb_grad = backward_layers(detector, windows, moved, adjoints)
    parts = jnp.stack((phase_grad, absorb_grad))
    returned = lax.all_to_all(parts, "depth", 1, 2, tiled=True)
    grid = jnp.zeros((2, layers) + extended.shape[2:], jnp.float32)
    for k in range(probes):
        grid = grid + place(returned[:, :, k], row_starts[k], col_starts[k], extended.shape[2:])
    owned = fold_both(grid, rim, pass_rows_all, pass_cols_all)
    return (owned[0], owned[1])


def solution(mesh):
    return jax.shard_map(
        per_device,
        mesh=mesh,
        in_specs=(
            P("depth", "row", "col"),
            P("depth", "row", "col"),
            P(),
            P("row", "col", None, None, None),
            P("row", "col", None, None),
        ),
        out_specs=(P("depth", "row", "col"), P("depth", "row", "col")),
        check_vma=False,
    )
```

```python
import math

import jax
import jax.numpy as jnp
from jax import lax
from jax.sharding import PartitionSpec as P

exact_mode = lax.Precision.HIGHEST


def from_behind(value, axis, steps):
    count = lax.axis_size(axis)
    leading, last = (max(0, -steps), min(count, count - steps))
    return lax.ppermute(value, axis, [(source, source + steps) for source in range(leading, last)])


def with_halo(block, sides, width):
    for axis, dim in sides:
        count = lax.axis_size(axis)
        forward = [(i, i + 1) for i in range(count - 1)]
        backward = [(target, source) for source, target in forward]
        low = lax.ppermute(
            lax.slice_in_dim(block, block.shape[dim] - width, None, axis=dim), axis, forward
        )
        high = lax.ppermute(lax.slice_in_dim(block, 0, width, axis=dim), axis, backward)
        block = jnp.concatenate([low, block, high], axis=dim)
    return block


def matmul_exact(first, second):
    return jnp.dot(first, second, precision=exact_mode, preferred_element_type=jnp.float32)


def build_tables(width):
    index = jnp.arange(width, dtype=jnp.int32)
    product = index[:, None] * index[None, :] % width
    angle = product.astype(jnp.float32) * (2.0 * math.pi / width)
    cosine = jnp.cos(angle)
    sine = jnp.sin(angle)
    signed = jnp.where(index < width // 2, index, index - width)
    chirp = -(signed * signed % (4 * width)).astype(jnp.float32) * (2.0 * math.pi / (4 * width))
    chirp_re = jnp.cos(chirp)[None, :]
    chirp_im = jnp.sin(chirp)[None, :]
    scaled_re = cosine * chirp_re - sine * chirp_im
    scaled_im = cosine * chirp_im + sine * chirp_re
    fresnel_re = matmul_exact(scaled_re, cosine) + matmul_exact(scaled_im, sine)
    fresnel_im = matmul_exact(scaled_im, cosine) - matmul_exact(scaled_re, sine)
    fresnel = jnp.stack((fresnel_re, fresnel_im)) / width
    far_field = jnp.stack((cosine, -sine)) / math.sqrt(width)
    return (fresnel, far_field)


def adjoint_of(matrix):
    return jnp.stack((matrix[0].T, -matrix[1].T))


def left_product(matrix, waves):
    return jnp.einsum(
        "ij,bjk->bik", matrix, waves, precision=exact_mode, preferred_element_type=jnp.float32
    )


def right_product(waves, matrix):
    return jnp.einsum(
        "bij,kj->bik", waves, matrix, precision=exact_mode, preferred_element_type=jnp.float32
    )


def propagate(matrix, waves):
    width = matrix.shape[1]
    tall = matrix.reshape(2 * width, width)
    from_real = left_product(tall, waves[0])
    from_imag = left_product(tall, waves[1])
    inner_re = from_real[:, :width] - from_imag[:, width:]
    inner_im = from_real[:, width:] + from_imag[:, :width]
    right_re = right_product(inner_re, tall)
    right_im = right_product(inner_im, tall)
    outer_re = right_re[:, :, :width] - right_im[:, :, width:]
    outer_im = right_re[:, :, width:] + right_im[:, :, :width]
    return jnp.stack((outer_re, outer_im))


def forward_layers(wave, slab, matrices):
    moved_list = []
    for layer in range(slab.shape[1]):
        trans_re = slab[0, layer]
        trans_im = slab[1, layer]
        moved = jnp.stack(
            (trans_re * wave[0] - trans_im * wave[1], trans_re * wave[1] + trans_im * wave[0])
        )
        moved_list.append(moved)
        wave = propagate(matrices[layer], moved)
    return (wave, jnp.stack(moved_list, axis=1))


def backward_layers(grad, slab, moved, adjoints):
    layers = slab.shape[1]
    phase_parts = [None] * layers
    absorb_parts = [None] * layers
    for layer in reversed(range(layers)):
        grad_moved = propagate(adjoints[layer], grad)
        moved_re = moved[0, layer]
        moved_im = moved[1, layer]
        phase_parts[layer] = grad_moved[1] * moved_re - grad_moved[0] * moved_im
        absorb_parts[layer] = -(grad_moved[0] * moved_re + grad_moved[1] * moved_im)
        trans_re = slab[0, layer]
        trans_im = slab[1, layer]
        grad = jnp.stack(
            (
                trans_re * grad_moved[0] + trans_im * grad_moved[1],
                trans_re * grad_moved[1] - trans_im * grad_moved[0],
            )
        )
    return (grad, jnp.stack(phase_parts), jnp.stack(absorb_parts))


def pass_rows_all(strip, steps):
    return from_behind(strip, "row", steps)


def pass_cols_all(strip, steps):
    return from_behind(strip, "col", steps)


def fold_rows(grid, rim, mover):
    inner = grid.shape[2] - 2 * rim
    from_above = mover(grid[:, :, inner + rim :], 1)
    from_below = mover(grid[:, :, :rim], -1)
    core = grid[:, :, rim : rim + inner]
    core = core.at[:, :, :rim].add(from_above)
    return core.at[:, :, inner - rim :].add(from_below)


def fold_cols(grid, rim, mover):
    inner = grid.shape[3] - 2 * rim
    from_left = mover(grid[:, :, :, inner + rim :], 1)
    from_right = mover(grid[:, :, :, :rim], -1)
    core = grid[:, :, :, rim : rim + inner]
    core = core.at[:, :, :, :rim].add(from_left)
    return core.at[:, :, :, inner - rim :].add(from_right)


def fold_both(grid, rim, row_mover, col_mover):
    return fold_cols(fold_rows(grid, rim, row_mover), rim, col_mover)


def to_transmit(extended):
    damping = jnp.exp(-extended[1])
    return jnp.stack((damping * jnp.cos(extended[0]), damping * jnp.sin(extended[0])))


def place(patch, row, col, frame):
    height, span = frame
    extra_rows = height - patch.shape[-2]
    extra_cols = span - patch.shape[-1]
    padded = jnp.pad(patch, ((0, 0), (0, 0), (extra_rows, extra_rows), (extra_cols, extra_cols)))
    anchor = jnp.zeros((), jnp.int32)
    start = (anchor, anchor, extra_rows - row, extra_cols - col)
    return lax.dynamic_slice(padded, start, patch.shape[:2] + (height, span))


def per_device(phase, absorption, probe, measured, offsets):
    layers, tile_rows, tile_cols = phase.shape
    width = probe.shape[1]
    rim = width // 2
    probes = offsets.shape[2]
    depth_count = lax.axis_size("depth")
    depth_index = lax.axis_index("depth")
    row_index = lax.axis_index("row")
    col_index = lax.axis_index("col")
    corners = offsets[0, 0]
    row_starts = corners[:, 0] - row_index * tile_rows + rim
    col_starts = corners[:, 1] - col_index * tile_cols + rim
    row_starts = [jnp.clip(row_starts[k], 0, 2 * rim + tile_rows - width) for k in range(probes)]
    col_starts = [jnp.clip(col_starts[k], 0, 2 * rim + tile_cols - width) for k in range(probes)]
    stacked = jnp.stack((phase, absorption))
    row_starts, col_starts, stacked = lax.optimization_barrier((row_starts, col_starts, stacked))
    extended = with_halo(stacked, (("row", 2), ("col", 3)), rim)
    anchor = jnp.zeros((), jnp.int32)
    fresnel, far_field = build_tables(width)
    share = probes // depth_count
    first = depth_index * share
    cut = jnp.stack(
        [
            lax.dynamic_slice(
                extended, (anchor, anchor, row_starts[k], col_starts[k]), (2, layers, width, width)
            )
            for k in range(probes)
        ],
        axis=2,
    )
    gathered = lax.all_to_all(cut, "depth", 2, 1, tiled=True)
    windows = to_transmit(gathered)
    total_layers = windows.shape[1]
    matrices = [fresnel] * (total_layers - 1) + [far_field]
    adjoints = [adjoint_of(matrix) for matrix in matrices]
    start_wave = probe[:, None]
    far_wave, moved = forward_layers(start_wave, windows, matrices)
    target = lax.dynamic_slice_in_dim(measured[0, 0], first, share)
    power = far_wave[0] ** 2 + far_wave[1] ** 2
    detector = far_wave * (0.25 * (power - target))[None]
    unused, phase_grad, absorb_grad = backward_layers(detector, windows, moved, adjoints)
    parts = jnp.stack((phase_grad, absorb_grad))
    returned = lax.all_to_all(parts, "depth", 1, 2, tiled=True)
    grid = jnp.zeros((2, layers) + extended.shape[2:], jnp.float32)
    for k in range(probes):
        grid = grid + place(returned[:, :, k], row_starts[k], col_starts[k], extended.shape[2:])
    owned = fold_both(grid, rim, pass_rows_all, pass_cols_all)
    return (owned[0], owned[1])


def solution(mesh):
    return jax.shard_map(
        per_device,
        mesh=mesh,
        in_specs=(
            P("depth", "row", "col"),
            P("depth", "row", "col"),
            P(),
            P("row", "col", None, None, None),
            P("row", "col", None, None),
        ),
        out_specs=(P("depth", "row", "col"), P("depth", "row", "col")),
        check_vma=False,
    )
```

```python
import math

import jax
import jax.numpy as jnp
from jax import lax
from jax.sharding import PartitionSpec as P

exact_mode = lax.Precision.HIGHEST
wave_mode = lax.Precision.HIGH


def from_behind(value, axis, steps):
    count = lax.axis_size(axis)
    leading, last = (max(0, -steps), min(count, count - steps))
    return lax.ppermute(value, axis, [(source, source + steps) for source in range(leading, last)])


def with_halo(block, sides, width):
    for axis, dim in sides:
        count = lax.axis_size(axis)
        forward = [(i, i + 1) for i in range(count - 1)]
        backward = [(target, source) for source, target in forward]
        low = lax.ppermute(
            lax.slice_in_dim(block, block.shape[dim] - width, None, axis=dim), axis, forward
        )
        high = lax.ppermute(lax.slice_in_dim(block, 0, width, axis=dim), axis, backward)
        block = jnp.concatenate([low, block, high], axis=dim)
    return block


def matmul_exact(first, second):
    return jnp.dot(first, second, precision=exact_mode, preferred_element_type=jnp.float32)


def build_tables(width):
    index = jnp.arange(width, dtype=jnp.int32)
    product = index[:, None] * index[None, :] % width
    angle = product.astype(jnp.float32) * (2.0 * math.pi / width)
    cosine = jnp.cos(angle)
    sine = jnp.sin(angle)
    signed = jnp.where(index < width // 2, index, index - width)
    chirp = -(signed * signed % (4 * width)).astype(jnp.float32) * (2.0 * math.pi / (4 * width))
    chirp_re = jnp.cos(chirp)[None, :]
    chirp_im = jnp.sin(chirp)[None, :]
    scaled_re = cosine * chirp_re - sine * chirp_im
    scaled_im = cosine * chirp_im + sine * chirp_re
    fresnel_re = matmul_exact(scaled_re, cosine) + matmul_exact(scaled_im, sine)
    fresnel_im = matmul_exact(scaled_im, cosine) - matmul_exact(scaled_re, sine)
    fresnel = jnp.stack((fresnel_re, fresnel_im)) / width
    far_field = jnp.stack((cosine, -sine)) / math.sqrt(width)
    return (fresnel, far_field)


def adjoint_of(matrix):
    return jnp.stack((matrix[0].T, -matrix[1].T))


def left_product(matrix, waves):
    return jnp.einsum(
        "ij,bjk->bik", matrix, waves, precision=wave_mode, preferred_element_type=jnp.float32
    )


def right_product(waves, matrix):
    return jnp.einsum(
        "bij,kj->bik", waves, matrix, precision=wave_mode, preferred_element_type=jnp.float32
    )


def propagate(matrix, waves):
    width = matrix.shape[1]
    tall = matrix.reshape(2 * width, width)
    from_real = left_product(tall, waves[0])
    from_imag = left_product(tall, waves[1])
    inner_re = from_real[:, :width] - from_imag[:, width:]
    inner_im = from_real[:, width:] + from_imag[:, :width]
    right_re = right_product(inner_re, tall)
    right_im = right_product(inner_im, tall)
    outer_re = right_re[:, :, :width] - right_im[:, :, width:]
    outer_im = right_re[:, :, width:] + right_im[:, :, :width]
    return jnp.stack((outer_re, outer_im))


def forward_layers(wave, slab, matrices):
    moved_list = []
    for layer in range(slab.shape[1]):
        trans_re = slab[0, layer]
        trans_im = slab[1, layer]
        moved = jnp.stack(
            (trans_re * wave[0] - trans_im * wave[1], trans_re * wave[1] + trans_im * wave[0])
        )
        moved_list.append(moved)
        wave = propagate(matrices[layer], moved)
    return (wave, jnp.stack(moved_list, axis=1))


def backward_layers(grad, slab, moved, adjoints):
    layers = slab.shape[1]
    phase_parts = [None] * layers
    absorb_parts = [None] * layers
    for layer in reversed(range(layers)):
        grad_moved = propagate(adjoints[layer], grad)
        moved_re = moved[0, layer]
        moved_im = moved[1, layer]
        phase_parts[layer] = grad_moved[1] * moved_re - grad_moved[0] * moved_im
        absorb_parts[layer] = -(grad_moved[0] * moved_re + grad_moved[1] * moved_im)
        trans_re = slab[0, layer]
        trans_im = slab[1, layer]
        grad = jnp.stack(
            (
                trans_re * grad_moved[0] + trans_im * grad_moved[1],
                trans_re * grad_moved[1] - trans_im * grad_moved[0],
            )
        )
    return (grad, jnp.stack(phase_parts), jnp.stack(absorb_parts))


def pass_rows_all(strip, steps):
    return from_behind(strip, "row", steps)


def pass_cols_all(strip, steps):
    return from_behind(strip, "col", steps)


def fold_rows(grid, rim, mover):
    inner = grid.shape[2] - 2 * rim
    from_above = mover(grid[:, :, inner + rim :], 1)
    from_below = mover(grid[:, :, :rim], -1)
    core = grid[:, :, rim : rim + inner]
    core = core.at[:, :, :rim].add(from_above)
    return core.at[:, :, inner - rim :].add(from_below)


def fold_cols(grid, rim, mover):
    inner = grid.shape[3] - 2 * rim
    from_left = mover(grid[:, :, :, inner + rim :], 1)
    from_right = mover(grid[:, :, :, :rim], -1)
    core = grid[:, :, :, rim : rim + inner]
    core = core.at[:, :, :, :rim].add(from_left)
    return core.at[:, :, :, inner - rim :].add(from_right)


def fold_both(grid, rim, row_mover, col_mover):
    return fold_cols(fold_rows(grid, rim, row_mover), rim, col_mover)


def to_transmit(extended):
    damping = jnp.exp(-extended[1])
    return jnp.stack((damping * jnp.cos(extended[0]), damping * jnp.sin(extended[0])))


def place(patch, row, col, frame):
    height, span = frame
    extra_rows = height - patch.shape[-2]
    extra_cols = span - patch.shape[-1]
    padded = jnp.pad(patch, ((0, 0), (0, 0), (extra_rows, extra_rows), (extra_cols, extra_cols)))
    anchor = jnp.zeros((), jnp.int32)
    start = (anchor, anchor, extra_rows - row, extra_cols - col)
    return lax.dynamic_slice(padded, start, patch.shape[:2] + (height, span))


def per_device(phase, absorption, probe, measured, offsets):
    layers, tile_rows, tile_cols = phase.shape
    width = probe.shape[1]
    rim = width // 2
    probes = offsets.shape[2]
    depth_count = lax.axis_size("depth")
    depth_index = lax.axis_index("depth")
    row_index = lax.axis_index("row")
    col_index = lax.axis_index("col")
    corners = offsets[0, 0]
    row_starts = corners[:, 0] - row_index * tile_rows + rim
    col_starts = corners[:, 1] - col_index * tile_cols + rim
    row_starts = [jnp.clip(row_starts[k], 0, 2 * rim + tile_rows - width) for k in range(probes)]
    col_starts = [jnp.clip(col_starts[k], 0, 2 * rim + tile_cols - width) for k in range(probes)]
    stacked = jnp.stack((phase, absorption))
    row_starts, col_starts, stacked = lax.optimization_barrier((row_starts, col_starts, stacked))
    extended = with_halo(stacked, (("row", 2), ("col", 3)), rim)
    anchor = jnp.zeros((), jnp.int32)
    fresnel, far_field = build_tables(width)
    share = probes // depth_count
    first = depth_index * share
    cut = jnp.stack(
        [
            lax.dynamic_slice(
                extended, (anchor, anchor, row_starts[k], col_starts[k]), (2, layers, width, width)
            )
            for k in range(probes)
        ],
        axis=2,
    )
    gathered = lax.all_to_all(cut, "depth", 2, 1, tiled=True)
    windows = to_transmit(gathered)
    total_layers = windows.shape[1]
    matrices = [fresnel] * (total_layers - 1) + [far_field]
    adjoints = [adjoint_of(matrix) for matrix in matrices]
    start_wave = probe[:, None]
    far_wave, moved = forward_layers(start_wave, windows, matrices)
    target = lax.dynamic_slice_in_dim(measured[0, 0], first, share)
    power = far_wave[0] ** 2 + far_wave[1] ** 2
    detector = far_wave * (0.25 * (power - target))[None]
    unused, phase_grad, absorb_grad = backward_layers(detector, windows, moved, adjoints)
    parts = jnp.stack((phase_grad, absorb_grad))
    returned = lax.all_to_all(parts, "depth", 1, 2, tiled=True)
    grid = jnp.zeros((2, layers) + extended.shape[2:], jnp.float32)
    for k in range(probes):
        grid = grid + place(returned[:, :, k], row_starts[k], col_starts[k], extended.shape[2:])
    owned = fold_both(grid, rim, pass_rows_all, pass_cols_all)
    return (owned[0], owned[1])


def solution(mesh):
    return jax.shard_map(
        per_device,
        mesh=mesh,
        in_specs=(
            P("depth", "row", "col"),
            P("depth", "row", "col"),
            P(),
            P("row", "col", None, None, None),
            P("row", "col", None, None),
        ),
        out_specs=(P("depth", "row", "col"), P("depth", "row", "col")),
        check_vma=False,
    )
```

```python
import math

import jax
import jax.numpy as jnp
from jax import lax
from jax.sharding import PartitionSpec as P

exact_mode = lax.Precision.HIGHEST
wave_mode = lax.Precision.HIGH


def from_behind(value, axis, steps):
    count = lax.axis_size(axis)
    leading, last = (max(0, -steps), min(count, count - steps))
    return lax.ppermute(value, axis, [(source, source + steps) for source in range(leading, last)])


def with_halo(block, sides, width):
    for axis, dim in sides:
        count = lax.axis_size(axis)
        forward = [(i, i + 1) for i in range(count - 1)]
        backward = [(target, source) for source, target in forward]
        low = lax.ppermute(
            lax.slice_in_dim(block, block.shape[dim] - width, None, axis=dim), axis, forward
        )
        high = lax.ppermute(lax.slice_in_dim(block, 0, width, axis=dim), axis, backward)
        block = jnp.concatenate([low, block, high], axis=dim)
    return block


def matmul_exact(first, second):
    return jnp.dot(first, second, precision=exact_mode, preferred_element_type=jnp.float32)


def build_tables(width):
    index = jnp.arange(width, dtype=jnp.int32)
    product = index[:, None] * index[None, :] % width
    angle = product.astype(jnp.float32) * (2.0 * math.pi / width)
    cosine = jnp.cos(angle)
    sine = jnp.sin(angle)
    signed = jnp.where(index < width // 2, index, index - width)
    chirp = -(signed * signed % (4 * width)).astype(jnp.float32) * (2.0 * math.pi / (4 * width))
    chirp_re = jnp.cos(chirp)[None, :]
    chirp_im = jnp.sin(chirp)[None, :]
    scaled_re = cosine * chirp_re - sine * chirp_im
    scaled_im = cosine * chirp_im + sine * chirp_re
    fresnel_re = matmul_exact(scaled_re, cosine) + matmul_exact(scaled_im, sine)
    fresnel_im = matmul_exact(scaled_im, cosine) - matmul_exact(scaled_re, sine)
    fresnel = jnp.stack((fresnel_re, fresnel_im)) / width
    far_field = jnp.stack((cosine, -sine)) / math.sqrt(width)
    return (fresnel, far_field)


def adjoint_of(matrix):
    return jnp.stack((matrix[0].T, -matrix[1].T))


def left_product(matrix, waves, mode):
    return jnp.einsum(
        "ij,bjk->bik", matrix, waves, precision=mode, preferred_element_type=jnp.float32
    )


def right_product(waves, matrix, mode):
    return jnp.einsum(
        "bij,kj->bik", waves, matrix, precision=mode, preferred_element_type=jnp.float32
    )


def propagate(matrix, waves, mode):
    width = matrix.shape[1]
    tall = matrix.reshape(2 * width, width)
    from_real = left_product(tall, waves[0], mode)
    from_imag = left_product(tall, waves[1], mode)
    inner_re = from_real[:, :width] - from_imag[:, width:]
    inner_im = from_real[:, width:] + from_imag[:, :width]
    right_re = right_product(inner_re, tall, mode)
    right_im = right_product(inner_im, tall, mode)
    outer_re = right_re[:, :, :width] - right_im[:, :, width:]
    outer_im = right_re[:, :, width:] + right_im[:, :, :width]
    return jnp.stack((outer_re, outer_im))


def forward_layers(wave, slab, matrices):
    moved_list = []
    for layer in range(slab.shape[1]):
        trans_re = slab[0, layer]
        trans_im = slab[1, layer]
        moved = jnp.stack(
            (trans_re * wave[0] - trans_im * wave[1], trans_re * wave[1] + trans_im * wave[0])
        )
        moved_list.append(moved)
        wave = propagate(matrices[layer], moved, exact_mode)
    return (wave, jnp.stack(moved_list, axis=1))


def backward_layers(grad, slab, moved, adjoints):
    layers = slab.shape[1]
    phase_parts = [None] * layers
    absorb_parts = [None] * layers
    for layer in reversed(range(layers)):
        grad_moved = propagate(adjoints[layer], grad, wave_mode)
        moved_re = moved[0, layer]
        moved_im = moved[1, layer]
        phase_parts[layer] = grad_moved[1] * moved_re - grad_moved[0] * moved_im
        absorb_parts[layer] = -(grad_moved[0] * moved_re + grad_moved[1] * moved_im)
        trans_re = slab[0, layer]
        trans_im = slab[1, layer]
        grad = jnp.stack(
            (
                trans_re * grad_moved[0] + trans_im * grad_moved[1],
                trans_re * grad_moved[1] - trans_im * grad_moved[0],
            )
        )
    return (grad, jnp.stack(phase_parts), jnp.stack(absorb_parts))


def pass_rows_all(strip, steps):
    return from_behind(strip, "row", steps)


def pass_cols_all(strip, steps):
    return from_behind(strip, "col", steps)


def fold_rows(grid, rim, mover):
    inner = grid.shape[2] - 2 * rim
    from_above = mover(grid[:, :, inner + rim :], 1)
    from_below = mover(grid[:, :, :rim], -1)
    core = grid[:, :, rim : rim + inner]
    core = core.at[:, :, :rim].add(from_above)
    return core.at[:, :, inner - rim :].add(from_below)


def fold_cols(grid, rim, mover):
    inner = grid.shape[3] - 2 * rim
    from_left = mover(grid[:, :, :, inner + rim :], 1)
    from_right = mover(grid[:, :, :, :rim], -1)
    core = grid[:, :, :, rim : rim + inner]
    core = core.at[:, :, :, :rim].add(from_left)
    return core.at[:, :, :, inner - rim :].add(from_right)


def fold_both(grid, rim, row_mover, col_mover):
    return fold_cols(fold_rows(grid, rim, row_mover), rim, col_mover)


def to_transmit(extended):
    damping = jnp.exp(-extended[1])
    return jnp.stack((damping * jnp.cos(extended[0]), damping * jnp.sin(extended[0])))


def place(patch, row, col, frame):
    height, span = frame
    extra_rows = height - patch.shape[-2]
    extra_cols = span - patch.shape[-1]
    padded = jnp.pad(patch, ((0, 0), (0, 0), (extra_rows, extra_rows), (extra_cols, extra_cols)))
    anchor = jnp.zeros((), jnp.int32)
    start = (anchor, anchor, extra_rows - row, extra_cols - col)
    return lax.dynamic_slice(padded, start, patch.shape[:2] + (height, span))


def per_device(phase, absorption, probe, measured, offsets):
    layers, tile_rows, tile_cols = phase.shape
    width = probe.shape[1]
    rim = width // 2
    probes = offsets.shape[2]
    depth_count = lax.axis_size("depth")
    depth_index = lax.axis_index("depth")
    row_index = lax.axis_index("row")
    col_index = lax.axis_index("col")
    corners = offsets[0, 0]
    row_starts = corners[:, 0] - row_index * tile_rows + rim
    col_starts = corners[:, 1] - col_index * tile_cols + rim
    row_starts = [jnp.clip(row_starts[k], 0, 2 * rim + tile_rows - width) for k in range(probes)]
    col_starts = [jnp.clip(col_starts[k], 0, 2 * rim + tile_cols - width) for k in range(probes)]
    stacked = jnp.stack((phase, absorption))
    row_starts, col_starts, stacked = lax.optimization_barrier((row_starts, col_starts, stacked))
    extended = with_halo(stacked, (("row", 2), ("col", 3)), rim)
    anchor = jnp.zeros((), jnp.int32)
    fresnel, far_field = build_tables(width)
    share = probes // depth_count
    first = depth_index * share
    cut = jnp.stack(
        [
            lax.dynamic_slice(
                extended, (anchor, anchor, row_starts[k], col_starts[k]), (2, layers, width, width)
            )
            for k in range(probes)
        ],
        axis=2,
    )
    gathered = lax.all_to_all(cut, "depth", 2, 1, tiled=True)
    windows = to_transmit(gathered)
    total_layers = windows.shape[1]
    matrices = [fresnel] * (total_layers - 1) + [far_field]
    adjoints = [adjoint_of(matrix) for matrix in matrices]
    start_wave = probe[:, None]
    far_wave, moved = forward_layers(start_wave, windows, matrices)
    target = lax.dynamic_slice_in_dim(measured[0, 0], first, share)
    power = far_wave[0] ** 2 + far_wave[1] ** 2
    detector = far_wave * (0.25 * (power - target))[None]
    unused, phase_grad, absorb_grad = backward_layers(detector, windows, moved, adjoints)
    parts = jnp.stack((phase_grad, absorb_grad))
    returned = lax.all_to_all(parts, "depth", 1, 2, tiled=True)
    grid = jnp.zeros((2, layers) + extended.shape[2:], jnp.float32)
    for k in range(probes):
        grid = grid + place(returned[:, :, k], row_starts[k], col_starts[k], extended.shape[2:])
    owned = fold_both(grid, rim, pass_rows_all, pass_cols_all)
    return (owned[0], owned[1])


def solution(mesh):
    return jax.shard_map(
        per_device,
        mesh=mesh,
        in_specs=(
            P("depth", "row", "col"),
            P("depth", "row", "col"),
            P(),
            P("row", "col", None, None, None),
            P("row", "col", None, None),
        ),
        out_specs=(P("depth", "row", "col"), P("depth", "row", "col")),
        check_vma=False,
    )
```

```python
import math

import jax
import jax.numpy as jnp
from jax import lax
from jax.sharding import PartitionSpec as P

exact_mode = lax.Precision.HIGHEST
wave_mode = lax.Precision.HIGH


def from_behind(value, axis, steps):
    count = lax.axis_size(axis)
    leading, last = (max(0, -steps), min(count, count - steps))
    return lax.ppermute(value, axis, [(source, source + steps) for source in range(leading, last)])


def with_halo(block, sides, width):
    for axis, dim in sides:
        count = lax.axis_size(axis)
        forward = [(i, i + 1) for i in range(count - 1)]
        backward = [(target, source) for source, target in forward]
        low = lax.ppermute(
            lax.slice_in_dim(block, block.shape[dim] - width, None, axis=dim), axis, forward
        )
        high = lax.ppermute(lax.slice_in_dim(block, 0, width, axis=dim), axis, backward)
        block = jnp.concatenate([low, block, high], axis=dim)
    return block


def matmul_exact(first, second):
    return jnp.dot(first, second, precision=exact_mode, preferred_element_type=jnp.float32)


def build_tables(width):
    index = jnp.arange(width, dtype=jnp.int32)
    product = index[:, None] * index[None, :] % width
    angle = product.astype(jnp.float32) * (2.0 * math.pi / width)
    cosine = jnp.cos(angle)
    sine = jnp.sin(angle)
    signed = jnp.where(index < width // 2, index, index - width)
    chirp = -(signed * signed % (4 * width)).astype(jnp.float32) * (2.0 * math.pi / (4 * width))
    chirp_re = jnp.cos(chirp)[None, :]
    chirp_im = jnp.sin(chirp)[None, :]
    scaled_re = cosine * chirp_re - sine * chirp_im
    scaled_im = cosine * chirp_im + sine * chirp_re
    fresnel_re = matmul_exact(scaled_re, cosine) + matmul_exact(scaled_im, sine)
    fresnel_im = matmul_exact(scaled_im, cosine) - matmul_exact(scaled_re, sine)
    fresnel = jnp.stack((fresnel_re, fresnel_im)) / width
    far_field = jnp.stack((cosine, -sine)) / math.sqrt(width)
    return (fresnel, far_field)


def adjoint_of(matrix):
    return jnp.stack((matrix[0].T, -matrix[1].T))


def left_product(matrix, waves, mode):
    return jnp.einsum(
        "ij,bjk->bik", matrix, waves, precision=mode, preferred_element_type=jnp.float32
    )


def right_product(waves, matrix, mode):
    return jnp.einsum(
        "bij,kj->bik", waves, matrix, precision=mode, preferred_element_type=jnp.float32
    )


def propagate(matrix, waves, mode):
    width = matrix.shape[1]
    tall = matrix.reshape(2 * width, width)
    from_real = left_product(tall, waves[0], mode)
    from_imag = left_product(tall, waves[1], mode)
    inner_re = from_real[:, :width] - from_imag[:, width:]
    inner_im = from_real[:, width:] + from_imag[:, :width]
    right_re = right_product(inner_re, tall, mode)
    right_im = right_product(inner_im, tall, mode)
    outer_re = right_re[:, :, :width] - right_im[:, :, width:]
    outer_im = right_re[:, :, width:] + right_im[:, :, :width]
    return jnp.stack((outer_re, outer_im))


def forward_layers(wave, slab, matrices):
    moved_list = []
    for layer in range(slab.shape[1]):
        trans_re = slab[0, layer]
        trans_im = slab[1, layer]
        moved = jnp.stack(
            (trans_re * wave[0] - trans_im * wave[1], trans_re * wave[1] + trans_im * wave[0])
        )
        moved_list.append(moved)
        wave = propagate(matrices[layer], moved, exact_mode)
    return (wave, jnp.stack(moved_list, axis=1))


def backward_layers(grad, slab, moved, adjoints):
    layers = slab.shape[1]
    phase_parts = [None] * layers
    absorb_parts = [None] * layers
    for layer in reversed(range(layers)):
        grad_moved = propagate(adjoints[layer], grad, wave_mode)
        moved_re = moved[0, layer]
        moved_im = moved[1, layer]
        phase_parts[layer] = grad_moved[1] * moved_re - grad_moved[0] * moved_im
        absorb_parts[layer] = -(grad_moved[0] * moved_re + grad_moved[1] * moved_im)
        trans_re = slab[0, layer]
        trans_im = slab[1, layer]
        grad = jnp.stack(
            (
                trans_re * grad_moved[0] + trans_im * grad_moved[1],
                trans_re * grad_moved[1] - trans_im * grad_moved[0],
            )
        )
    return (grad, jnp.stack(phase_parts), jnp.stack(absorb_parts))


def pass_rows_all(strip, steps):
    return from_behind(strip, "row", steps)


def pass_cols_all(strip, steps):
    return from_behind(strip, "col", steps)


def fold_rows(grid, rim, mover):
    inner = grid.shape[2] - 2 * rim
    from_above = mover(grid[:, :, inner + rim :], 1)
    from_below = mover(grid[:, :, :rim], -1)
    core = grid[:, :, rim : rim + inner]
    core = core.at[:, :, :rim].add(from_above)
    return core.at[:, :, inner - rim :].add(from_below)


def fold_cols(grid, rim, mover):
    inner = grid.shape[3] - 2 * rim
    from_left = mover(grid[:, :, :, inner + rim :], 1)
    from_right = mover(grid[:, :, :, :rim], -1)
    core = grid[:, :, :, rim : rim + inner]
    core = core.at[:, :, :, :rim].add(from_left)
    return core.at[:, :, :, inner - rim :].add(from_right)


def fold_both(grid, rim, row_mover, col_mover):
    return fold_rows(fold_cols(grid, rim, col_mover), rim, row_mover)


def to_transmit(extended):
    damping = jnp.exp(-extended[1])
    return jnp.stack((damping * jnp.cos(extended[0]), damping * jnp.sin(extended[0])))


def place(patch, row, col, frame):
    height, span = frame
    extra_rows = height - patch.shape[-2]
    extra_cols = span - patch.shape[-1]
    padded = jnp.pad(patch, ((0, 0), (0, 0), (extra_rows, extra_rows), (extra_cols, extra_cols)))
    anchor = jnp.zeros((), jnp.int32)
    start = (anchor, anchor, extra_rows - row, extra_cols - col)
    return lax.dynamic_slice(padded, start, patch.shape[:2] + (height, span))


def per_device(phase, absorption, probe, measured, offsets):
    layers, tile_rows, tile_cols = phase.shape
    width = probe.shape[1]
    rim = width // 2
    probes = offsets.shape[2]
    depth_count = lax.axis_size("depth")
    depth_index = lax.axis_index("depth")
    row_index = lax.axis_index("row")
    col_index = lax.axis_index("col")
    corners = offsets[0, 0]
    row_starts = corners[:, 0] - row_index * tile_rows + rim
    col_starts = corners[:, 1] - col_index * tile_cols + rim
    row_starts = [jnp.clip(row_starts[k], 0, 2 * rim + tile_rows - width) for k in range(probes)]
    col_starts = [jnp.clip(col_starts[k], 0, 2 * rim + tile_cols - width) for k in range(probes)]
    stacked = jnp.stack((phase, absorption))
    row_starts, col_starts, stacked = lax.optimization_barrier((row_starts, col_starts, stacked))
    extended = with_halo(stacked, (("row", 2), ("col", 3)), rim)
    anchor = jnp.zeros((), jnp.int32)
    fresnel, far_field = build_tables(width)
    share = probes // depth_count
    first = depth_index * share
    cut = jnp.stack(
        [
            lax.dynamic_slice(
                extended, (anchor, anchor, row_starts[k], col_starts[k]), (2, layers, width, width)
            )
            for k in range(probes)
        ],
        axis=2,
    )
    gathered = lax.all_to_all(cut, "depth", 2, 1, tiled=True)
    windows = to_transmit(gathered)
    total_layers = windows.shape[1]
    matrices = [fresnel] * (total_layers - 1) + [far_field]
    adjoints = [adjoint_of(matrix) for matrix in matrices]
    start_wave = probe[:, None]
    far_wave, moved = forward_layers(start_wave, windows, matrices)
    target = lax.dynamic_slice_in_dim(measured[0, 0], first, share)
    power = far_wave[0] ** 2 + far_wave[1] ** 2
    detector = far_wave * (0.25 * (power - target))[None]
    unused, phase_grad, absorb_grad = backward_layers(detector, windows, moved, adjoints)
    parts = jnp.stack((phase_grad, absorb_grad))
    returned = lax.all_to_all(parts, "depth", 1, 2, tiled=True)
    grid = jnp.zeros((2, layers) + extended.shape[2:], jnp.float32)
    for k in range(probes):
        grid = grid + place(returned[:, :, k], row_starts[k], col_starts[k], extended.shape[2:])
    owned = fold_both(grid, rim, pass_rows_all, pass_cols_all)
    return (owned[0], owned[1])


def solution(mesh):
    return jax.shard_map(
        per_device,
        mesh=mesh,
        in_specs=(
            P("depth", "row", "col"),
            P("depth", "row", "col"),
            P(),
            P("row", "col", None, None, None),
            P("row", "col", None, None),
        ),
        out_specs=(P("depth", "row", "col"), P("depth", "row", "col")),
        check_vma=False,
    )
```

```python
import math

import jax
import jax.numpy as jnp
from jax import lax
from jax.sharding import PartitionSpec as P

exact_mode = lax.Precision.HIGHEST
wave_mode = lax.Precision.HIGH


def from_behind(value, axis, steps):
    count = lax.axis_size(axis)
    leading, last = (max(0, -steps), min(count, count - steps))
    return lax.ppermute(value, axis, [(source, source + steps) for source in range(leading, last)])


def with_halo(block, sides, width):
    for axis, dim in sides:
        count = lax.axis_size(axis)
        forward = [(i, i + 1) for i in range(count - 1)]
        backward = [(target, source) for source, target in forward]
        low = lax.ppermute(
            lax.slice_in_dim(block, block.shape[dim] - width, None, axis=dim), axis, forward
        )
        high = lax.ppermute(lax.slice_in_dim(block, 0, width, axis=dim), axis, backward)
        block = jnp.concatenate([low, block, high], axis=dim)
    return block


def matmul_exact(first, second):
    return jnp.dot(first, second, precision=exact_mode, preferred_element_type=jnp.float32)


def build_tables(width):
    index = jnp.arange(width, dtype=jnp.int32)
    product = index[:, None] * index[None, :] % width
    angle = product.astype(jnp.float32) * (2.0 * math.pi / width)
    cosine = jnp.cos(angle)
    sine = jnp.sin(angle)
    signed = jnp.where(index < width // 2, index, index - width)
    chirp = -(signed * signed % (4 * width)).astype(jnp.float32) * (2.0 * math.pi / (4 * width))
    chirp_re = jnp.cos(chirp)[None, :]
    chirp_im = jnp.sin(chirp)[None, :]
    scaled_re = cosine * chirp_re - sine * chirp_im
    scaled_im = cosine * chirp_im + sine * chirp_re
    fresnel_re = matmul_exact(scaled_re, cosine) + matmul_exact(scaled_im, sine)
    fresnel_im = matmul_exact(scaled_im, cosine) - matmul_exact(scaled_re, sine)
    fresnel = jnp.stack((fresnel_re, fresnel_im)) / width
    far_field = jnp.stack((cosine, -sine)) / math.sqrt(width)
    return (fresnel, far_field)


def adjoint_of(matrix):
    return jnp.stack((matrix[0].T, -matrix[1].T))


def left_product(matrix, waves, mode):
    return jnp.einsum(
        "ij,bjk->bik", matrix, waves, precision=mode, preferred_element_type=jnp.float32
    )


def right_product(waves, matrix, mode):
    return jnp.einsum(
        "bij,kj->bik", waves, matrix, precision=mode, preferred_element_type=jnp.float32
    )


def propagate(matrix, waves, mode):
    width = matrix.shape[1]
    tall = matrix.reshape(2 * width, width)
    from_real = left_product(tall, waves[0], mode)
    from_imag = left_product(tall, waves[1], mode)
    inner_re = from_real[:, :width] - from_imag[:, width:]
    inner_im = from_real[:, width:] + from_imag[:, :width]
    right_re = right_product(inner_re, tall, mode)
    right_im = right_product(inner_im, tall, mode)
    outer_re = right_re[:, :, :width] - right_im[:, :, width:]
    outer_im = right_re[:, :, width:] + right_im[:, :, :width]
    return jnp.stack((outer_re, outer_im))


def forward_layers(wave, slab, matrices):
    layers = slab.shape[1]

    def step(wave, trans):
        trans_re, trans_im = trans[0], trans[1]
        moved = jnp.stack(
            (trans_re * wave[0] - trans_im * wave[1], trans_re * wave[1] + trans_im * wave[0])
        )
        return (moved, propagate(matrices[0], moved, exact_mode))

    wave = jnp.broadcast_to(wave, (2,) + slab.shape[2:])
    inner = jnp.moveaxis(slab[:, : layers - 1], 1, 0)
    wave, moved_inner = lax.scan(lambda w, t: step(w, t)[::-1], wave, inner)
    last_moved, unused = step(wave, slab[:, layers - 1])
    far = propagate(matrices[-1], last_moved, exact_mode)
    moved = jnp.concatenate((jnp.moveaxis(moved_inner, 0, 1), last_moved[:, None]), axis=1)
    return (far, moved)


def backward_layers(grad, slab, moved, adjoints):
    layers = slab.shape[1]

    def step(grad, adjoint, trans, moved_here):
        grad_moved = propagate(adjoint, grad, wave_mode)
        moved_re = moved_here[0]
        moved_im = moved_here[1]
        phase_part = grad_moved[1] * moved_re - grad_moved[0] * moved_im
        absorb_part = -(grad_moved[0] * moved_re + grad_moved[1] * moved_im)
        trans_re = trans[0]
        trans_im = trans[1]
        grad = jnp.stack(
            (
                trans_re * grad_moved[0] + trans_im * grad_moved[1],
                trans_re * grad_moved[1] - trans_im * grad_moved[0],
            )
        )
        return (grad, jnp.stack((phase_part, absorb_part)))

    grad, last_parts = step(grad, adjoints[-1], slab[:, layers - 1], moved[:, layers - 1])
    inner = (jnp.moveaxis(slab[:, : layers - 1], 1, 0), jnp.moveaxis(moved[:, : layers - 1], 1, 0))
    grad, inner_parts = lax.scan(
        lambda g, x: step(g, adjoints[0], x[0], x[1]), grad, inner, reverse=True
    )
    parts = jnp.concatenate((jnp.moveaxis(inner_parts, 0, 1), last_parts[:, None]), axis=1)
    return (grad, parts[0], parts[1])


def pass_rows_all(strip, steps):
    return from_behind(strip, "row", steps)


def pass_cols_all(strip, steps):
    return from_behind(strip, "col", steps)


def fold_rows(grid, rim, mover):
    inner = grid.shape[2] - 2 * rim
    from_above = mover(grid[:, :, inner + rim :], 1)
    from_below = mover(grid[:, :, :rim], -1)
    core = grid[:, :, rim : rim + inner]
    core = core.at[:, :, :rim].add(from_above)
    return core.at[:, :, inner - rim :].add(from_below)


def fold_cols(grid, rim, mover):
    inner = grid.shape[3] - 2 * rim
    from_left = mover(grid[:, :, :, inner + rim :], 1)
    from_right = mover(grid[:, :, :, :rim], -1)
    core = grid[:, :, :, rim : rim + inner]
    core = core.at[:, :, :, :rim].add(from_left)
    return core.at[:, :, :, inner - rim :].add(from_right)


def fold_both(grid, rim, row_mover, col_mover):
    return fold_rows(fold_cols(grid, rim, col_mover), rim, row_mover)


def to_transmit(extended):
    damping = jnp.exp(-extended[1])
    return jnp.stack((damping * jnp.cos(extended[0]), damping * jnp.sin(extended[0])))


def place(patch, row, col, frame):
    height, span = frame
    extra_rows = height - patch.shape[-2]
    extra_cols = span - patch.shape[-1]
    padded = jnp.pad(patch, ((0, 0), (0, 0), (extra_rows, extra_rows), (extra_cols, extra_cols)))
    anchor = jnp.zeros((), jnp.int32)
    start = (anchor, anchor, extra_rows - row, extra_cols - col)
    return lax.dynamic_slice(padded, start, patch.shape[:2] + (height, span))


def per_device(phase, absorption, probe, measured, offsets):
    layers, tile_rows, tile_cols = phase.shape
    width = probe.shape[1]
    rim = width // 2
    probes = offsets.shape[2]
    depth_count = lax.axis_size("depth")
    depth_index = lax.axis_index("depth")
    row_index = lax.axis_index("row")
    col_index = lax.axis_index("col")
    corners = offsets[0, 0]
    row_starts = corners[:, 0] - row_index * tile_rows + rim
    col_starts = corners[:, 1] - col_index * tile_cols + rim
    row_starts = [jnp.clip(row_starts[k], 0, 2 * rim + tile_rows - width) for k in range(probes)]
    col_starts = [jnp.clip(col_starts[k], 0, 2 * rim + tile_cols - width) for k in range(probes)]
    stacked = jnp.stack((phase, absorption))
    row_starts, col_starts, stacked = lax.optimization_barrier((row_starts, col_starts, stacked))
    extended = with_halo(stacked, (("row", 2), ("col", 3)), rim)
    anchor = jnp.zeros((), jnp.int32)
    fresnel, far_field = build_tables(width)
    share = probes // depth_count
    first = depth_index * share
    cut = jnp.stack(
        [
            lax.dynamic_slice(
                extended, (anchor, anchor, row_starts[k], col_starts[k]), (2, layers, width, width)
            )
            for k in range(probes)
        ],
        axis=2,
    )
    gathered = lax.all_to_all(cut, "depth", 2, 1, tiled=True)
    windows = to_transmit(gathered)
    total_layers = windows.shape[1]
    matrices = [fresnel] * (total_layers - 1) + [far_field]
    adjoints = [adjoint_of(matrix) for matrix in matrices]
    start_wave = probe[:, None]
    far_wave, moved = forward_layers(start_wave, windows, matrices)
    target = lax.dynamic_slice_in_dim(measured[0, 0], first, share)
    power = far_wave[0] ** 2 + far_wave[1] ** 2
    detector = far_wave * (0.25 * (power - target))[None]
    unused, phase_grad, absorb_grad = backward_layers(detector, windows, moved, adjoints)
    parts = jnp.stack((phase_grad, absorb_grad))
    returned = lax.all_to_all(parts, "depth", 1, 2, tiled=True)
    grid = jnp.zeros((2, layers) + extended.shape[2:], jnp.float32)
    for k in range(probes):
        grid = grid + place(returned[:, :, k], row_starts[k], col_starts[k], extended.shape[2:])
    owned = fold_both(grid, rim, pass_rows_all, pass_cols_all)
    return (owned[0], owned[1])


def solution(mesh):
    return jax.shard_map(
        per_device,
        mesh=mesh,
        in_specs=(
            P("depth", "row", "col"),
            P("depth", "row", "col"),
            P(),
            P("row", "col", None, None, None),
            P("row", "col", None, None),
        ),
        out_specs=(P("depth", "row", "col"), P("depth", "row", "col")),
        check_vma=False,
    )
```

```python
import math

import jax
import jax.numpy as jnp
from jax import lax
from jax.sharding import PartitionSpec as P

exact_mode = lax.Precision.HIGHEST
wave_mode = lax.Precision.HIGH


def from_behind(value, axis, steps):
    count = lax.axis_size(axis)
    leading, last = (max(0, -steps), min(count, count - steps))
    return lax.ppermute(value, axis, [(source, source + steps) for source in range(leading, last)])


def with_halo(block, sides, width):
    for axis, dim in sides:
        count = lax.axis_size(axis)
        forward = [(i, i + 1) for i in range(count - 1)]
        backward = [(target, source) for source, target in forward]
        low = lax.ppermute(
            lax.slice_in_dim(block, block.shape[dim] - width, None, axis=dim), axis, forward
        )
        high = lax.ppermute(lax.slice_in_dim(block, 0, width, axis=dim), axis, backward)
        block = jnp.concatenate([low, block, high], axis=dim)
    return block


def matmul_exact(first, second):
    return jnp.dot(first, second, precision=exact_mode, preferred_element_type=jnp.float32)


def build_tables(width):
    index = jnp.arange(width, dtype=jnp.int32)
    product = index[:, None] * index[None, :] % width
    angle = product.astype(jnp.float32) * (2.0 * math.pi / width)
    cosine = jnp.cos(angle)
    sine = jnp.sin(angle)
    signed = jnp.where(index < width // 2, index, index - width)
    chirp = -(signed * signed % (4 * width)).astype(jnp.float32) * (2.0 * math.pi / (4 * width))
    chirp_re = jnp.cos(chirp)[None, :]
    chirp_im = jnp.sin(chirp)[None, :]
    scaled_re = cosine * chirp_re - sine * chirp_im
    scaled_im = cosine * chirp_im + sine * chirp_re
    fresnel_re = matmul_exact(scaled_re, cosine) + matmul_exact(scaled_im, sine)
    fresnel_im = matmul_exact(scaled_im, cosine) - matmul_exact(scaled_re, sine)
    fresnel = jnp.stack((fresnel_re, fresnel_im)) / width
    far_field = jnp.stack((cosine, -sine)) / math.sqrt(width)
    return (fresnel, far_field)


def adjoint_of(matrix):
    return jnp.stack((matrix[0].T, -matrix[1].T))


def left_product(matrix, waves, mode):
    return jnp.einsum(
        "ij,bjk->bik", matrix, waves, precision=mode, preferred_element_type=jnp.float32
    )


def right_product(waves, matrix, mode):
    return jnp.einsum(
        "bij,kj->bik", waves, matrix, precision=mode, preferred_element_type=jnp.float32
    )


def propagate(matrix, waves, mode):
    width = matrix.shape[1]
    tall = matrix.reshape(2 * width, width)
    batch = waves.shape[1]
    both = left_product(tall, waves.reshape((2 * batch,) + waves.shape[2:]), mode)
    from_real = both[:batch]
    from_imag = both[batch:]
    inner_re = from_real[:, :width] - from_imag[:, width:]
    inner_im = from_real[:, width:] + from_imag[:, :width]
    right = right_product(jnp.concatenate((inner_re, inner_im)), tall, mode)
    right_re = right[:batch]
    right_im = right[batch:]
    outer_re = right_re[:, :, :width] - right_im[:, :, width:]
    outer_im = right_re[:, :, width:] + right_im[:, :, :width]
    return jnp.stack((outer_re, outer_im))


def forward_layers(wave, slab, matrices):
    moved_list = []
    for layer in range(slab.shape[1]):
        trans_re = slab[0, layer]
        trans_im = slab[1, layer]
        moved = jnp.stack(
            (trans_re * wave[0] - trans_im * wave[1], trans_re * wave[1] + trans_im * wave[0])
        )
        moved_list.append(moved)
        wave = propagate(matrices[layer], moved, exact_mode)
    return (wave, jnp.stack(moved_list, axis=1))


def backward_layers(grad, slab, moved, adjoints):
    layers = slab.shape[1]
    phase_parts = [None] * layers
    absorb_parts = [None] * layers
    for layer in reversed(range(layers)):
        grad_moved = propagate(adjoints[layer], grad, wave_mode)
        moved_re = moved[0, layer]
        moved_im = moved[1, layer]
        phase_parts[layer] = grad_moved[1] * moved_re - grad_moved[0] * moved_im
        absorb_parts[layer] = -(grad_moved[0] * moved_re + grad_moved[1] * moved_im)
        trans_re = slab[0, layer]
        trans_im = slab[1, layer]
        grad = jnp.stack(
            (
                trans_re * grad_moved[0] + trans_im * grad_moved[1],
                trans_re * grad_moved[1] - trans_im * grad_moved[0],
            )
        )
    return (grad, jnp.stack(phase_parts), jnp.stack(absorb_parts))


def pass_rows_all(strip, steps):
    return from_behind(strip, "row", steps)


def pass_cols_all(strip, steps):
    return from_behind(strip, "col", steps)


def fold_rows(grid, rim, mover):
    inner = grid.shape[2] - 2 * rim
    from_above = mover(grid[:, :, inner + rim :], 1)
    from_below = mover(grid[:, :, :rim], -1)
    core = grid[:, :, rim : rim + inner]
    core = core.at[:, :, :rim].add(from_above)
    return core.at[:, :, inner - rim :].add(from_below)


def fold_cols(grid, rim, mover):
    inner = grid.shape[3] - 2 * rim
    from_left = mover(grid[:, :, :, inner + rim :], 1)
    from_right = mover(grid[:, :, :, :rim], -1)
    core = grid[:, :, :, rim : rim + inner]
    core = core.at[:, :, :, :rim].add(from_left)
    return core.at[:, :, :, inner - rim :].add(from_right)


def fold_both(grid, rim, row_mover, col_mover):
    return fold_rows(fold_cols(grid, rim, col_mover), rim, row_mover)


def to_transmit(extended):
    damping = jnp.exp(-extended[1])
    return jnp.stack((damping * jnp.cos(extended[0]), damping * jnp.sin(extended[0])))


def place(patch, row, col, frame):
    height, span = frame
    extra_rows = height - patch.shape[-2]
    extra_cols = span - patch.shape[-1]
    padded = jnp.pad(patch, ((0, 0), (0, 0), (extra_rows, extra_rows), (extra_cols, extra_cols)))
    anchor = jnp.zeros((), jnp.int32)
    start = (anchor, anchor, extra_rows - row, extra_cols - col)
    return lax.dynamic_slice(padded, start, patch.shape[:2] + (height, span))


def per_device(phase, absorption, probe, measured, offsets):
    layers, tile_rows, tile_cols = phase.shape
    width = probe.shape[1]
    rim = width // 2
    probes = offsets.shape[2]
    depth_count = lax.axis_size("depth")
    depth_index = lax.axis_index("depth")
    row_index = lax.axis_index("row")
    col_index = lax.axis_index("col")
    corners = offsets[0, 0]
    row_starts = corners[:, 0] - row_index * tile_rows + rim
    col_starts = corners[:, 1] - col_index * tile_cols + rim
    row_starts = [jnp.clip(row_starts[k], 0, 2 * rim + tile_rows - width) for k in range(probes)]
    col_starts = [jnp.clip(col_starts[k], 0, 2 * rim + tile_cols - width) for k in range(probes)]
    stacked = jnp.stack((phase, absorption))
    row_starts, col_starts, stacked = lax.optimization_barrier((row_starts, col_starts, stacked))
    extended = with_halo(stacked, (("row", 2), ("col", 3)), rim)
    anchor = jnp.zeros((), jnp.int32)
    fresnel, far_field = build_tables(width)
    share = probes // depth_count
    first = depth_index * share
    cut = jnp.stack(
        [
            lax.dynamic_slice(
                extended, (anchor, anchor, row_starts[k], col_starts[k]), (2, layers, width, width)
            )
            for k in range(probes)
        ],
        axis=2,
    )
    gathered = lax.all_to_all(cut, "depth", 2, 1, tiled=True)
    windows = to_transmit(gathered)
    total_layers = windows.shape[1]
    matrices = [fresnel] * (total_layers - 1) + [far_field]
    adjoints = [adjoint_of(matrix) for matrix in matrices]
    start_wave = probe[:, None]
    far_wave, moved = forward_layers(start_wave, windows, matrices)
    target = lax.dynamic_slice_in_dim(measured[0, 0], first, share)
    power = far_wave[0] ** 2 + far_wave[1] ** 2
    detector = far_wave * (0.25 * (power - target))[None]
    unused, phase_grad, absorb_grad = backward_layers(detector, windows, moved, adjoints)
    parts = jnp.stack((phase_grad, absorb_grad))
    returned = lax.all_to_all(parts, "depth", 1, 2, tiled=True)
    grid = jnp.zeros((2, layers) + extended.shape[2:], jnp.float32)
    for k in range(probes):
        grid = grid + place(returned[:, :, k], row_starts[k], col_starts[k], extended.shape[2:])
    owned = fold_both(grid, rim, pass_rows_all, pass_cols_all)
    return (owned[0], owned[1])


def solution(mesh):
    return jax.shard_map(
        per_device,
        mesh=mesh,
        in_specs=(
            P("depth", "row", "col"),
            P("depth", "row", "col"),
            P(),
            P("row", "col", None, None, None),
            P("row", "col", None, None),
        ),
        out_specs=(P("depth", "row", "col"), P("depth", "row", "col")),
        check_vma=False,
    )
```

```python
import math

import jax
import jax.numpy as jnp
from jax import lax
from jax.sharding import PartitionSpec as P

exact_mode = lax.Precision.HIGHEST
wave_mode = lax.Precision.HIGH


def from_behind(value, axis, steps):
    count = lax.axis_size(axis)
    leading, last = (max(0, -steps), min(count, count - steps))
    return lax.ppermute(value, axis, [(source, source + steps) for source in range(leading, last)])


def with_halo(block, sides, width):
    for axis, dim in sides:
        count = lax.axis_size(axis)
        forward = [(i, i + 1) for i in range(count - 1)]
        backward = [(target, source) for source, target in forward]
        low = lax.ppermute(
            lax.slice_in_dim(block, block.shape[dim] - width, None, axis=dim), axis, forward
        )
        high = lax.ppermute(lax.slice_in_dim(block, 0, width, axis=dim), axis, backward)
        block = jnp.concatenate([low, block, high], axis=dim)
    return block


def matmul_exact(first, second):
    return jnp.dot(first, second, precision=exact_mode, preferred_element_type=jnp.float32)


def build_tables(width):
    index = jnp.arange(width, dtype=jnp.int32)
    product = index[:, None] * index[None, :] % width
    angle = product.astype(jnp.float32) * (2.0 * math.pi / width)
    cosine = jnp.cos(angle)
    sine = jnp.sin(angle)
    signed = jnp.where(index < width // 2, index, index - width)
    chirp = -(signed * signed % (4 * width)).astype(jnp.float32) * (2.0 * math.pi / (4 * width))
    chirp_re = jnp.cos(chirp)[None, :]
    chirp_im = jnp.sin(chirp)[None, :]
    scaled_re = cosine * chirp_re - sine * chirp_im
    scaled_im = cosine * chirp_im + sine * chirp_re
    fresnel_re = matmul_exact(scaled_re, cosine) + matmul_exact(scaled_im, sine)
    fresnel_im = matmul_exact(scaled_im, cosine) - matmul_exact(scaled_re, sine)
    fresnel = jnp.stack((fresnel_re, fresnel_im)) / width
    far_field = jnp.stack((cosine, -sine)) / math.sqrt(width)
    return (fresnel, far_field)


def adjoint_of(matrix):
    return jnp.stack((matrix[0].T, -matrix[1].T))


def left_product(matrix, waves, mode):
    return jnp.einsum(
        "ij,bjk->bik", matrix, waves, precision=mode, preferred_element_type=jnp.float32
    )


def right_product(waves, matrix, mode):
    return jnp.einsum(
        "bij,kj->bik", waves, matrix, precision=mode, preferred_element_type=jnp.float32
    )


def propagate(matrix, waves, mode):
    width = matrix.shape[1]
    tall = matrix.reshape(2 * width, width)
    batch = waves.shape[1]
    both = left_product(tall, waves.reshape((2 * batch,) + waves.shape[2:]), mode)
    from_real = both[:batch]
    from_imag = both[batch:]
    inner_re = from_real[:, :width] - from_imag[:, width:]
    inner_im = from_real[:, width:] + from_imag[:, :width]
    right = right_product(jnp.concatenate((inner_re, inner_im)), tall, mode)
    right_re = right[:batch]
    right_im = right[batch:]
    outer_re = right_re[:, :, :width] - right_im[:, :, width:]
    outer_im = right_re[:, :, width:] + right_im[:, :, :width]
    return jnp.stack((outer_re, outer_im))


def forward_layers(wave, slab, matrices):
    moved_list = []
    for layer in range(slab.shape[1]):
        trans_re = slab[0, layer]
        trans_im = slab[1, layer]
        moved = jnp.stack(
            (trans_re * wave[0] - trans_im * wave[1], trans_re * wave[1] + trans_im * wave[0])
        )
        moved_list.append(moved)
        wave = propagate(matrices[layer], moved, exact_mode)
    return (wave, jnp.stack(moved_list, axis=1))


def backward_layers(grad, slab, moved, adjoints):
    layers = slab.shape[1]
    phase_parts = [None] * layers
    absorb_parts = [None] * layers
    for layer in reversed(range(layers)):
        grad_moved = propagate(adjoints[layer], grad, wave_mode)
        moved_re = moved[0, layer]
        moved_im = moved[1, layer]
        phase_parts[layer] = grad_moved[1] * moved_re - grad_moved[0] * moved_im
        absorb_parts[layer] = -(grad_moved[0] * moved_re + grad_moved[1] * moved_im)
        trans_re = slab[0, layer]
        trans_im = slab[1, layer]
        grad = jnp.stack(
            (
                trans_re * grad_moved[0] + trans_im * grad_moved[1],
                trans_re * grad_moved[1] - trans_im * grad_moved[0],
            )
        )
    return (grad, jnp.stack(phase_parts), jnp.stack(absorb_parts))


def pass_rows_all(strip, steps):
    return from_behind(strip, "row", steps)


def pass_cols_all(strip, steps):
    return from_behind(strip, "col", steps)


def fold_rows(grid, rim, mover):
    inner = grid.shape[2] - 2 * rim
    from_above = mover(grid[:, :, inner + rim :], 1)
    from_below = mover(grid[:, :, :rim], -1)
    core = grid[:, :, rim : rim + inner]
    core = core.at[:, :, :rim].add(from_above)
    return core.at[:, :, inner - rim :].add(from_below)


def fold_cols(grid, rim, mover):
    inner = grid.shape[3] - 2 * rim
    from_left = mover(grid[:, :, :, inner + rim :], 1)
    from_right = mover(grid[:, :, :, :rim], -1)
    core = grid[:, :, :, rim : rim + inner]
    core = core.at[:, :, :, :rim].add(from_left)
    return core.at[:, :, :, inner - rim :].add(from_right)


def fold_both(grid, rim, row_mover, col_mover):
    return fold_rows(fold_cols(grid, rim, col_mover), rim, row_mover)


def to_transmit(extended):
    damping = jnp.exp(-extended[1])
    return jnp.stack((damping * jnp.cos(extended[0]), damping * jnp.sin(extended[0])))


def place(patch, row, col, frame):
    height, span = frame
    extra_rows = height - patch.shape[-2]
    extra_cols = span - patch.shape[-1]
    padded = jnp.pad(patch, ((0, 0), (0, 0), (extra_rows, extra_rows), (extra_cols, extra_cols)))
    anchor = jnp.zeros((), jnp.int32)
    start = (anchor, anchor, extra_rows - row, extra_cols - col)
    return lax.dynamic_slice(padded, start, patch.shape[:2] + (height, span))


def exchange(chunks, axis, count, index):
    pieces = [chunks[0]]
    for shift in range(1, count):
        pieces.append(
            lax.ppermute(chunks[shift], axis, [(i, (i + shift) % count) for i in range(count)])
        )
    stacked = jnp.stack(pieces)
    return [lax.dynamic_index_in_dim(stacked, (index - j) % count, keepdims=False) for j in range(count)]


def per_device(phase, absorption, probe, measured, offsets):
    layers, tile_rows, tile_cols = phase.shape
    width = probe.shape[1]
    rim = width // 2
    probes = offsets.shape[2]
    depth_count = lax.axis_size("depth")
    depth_index = lax.axis_index("depth")
    row_index = lax.axis_index("row")
    col_index = lax.axis_index("col")
    corners = offsets[0, 0]
    row_starts = corners[:, 0] - row_index * tile_rows + rim
    col_starts = corners[:, 1] - col_index * tile_cols + rim
    row_starts = [jnp.clip(row_starts[k], 0, 2 * rim + tile_rows - width) for k in range(probes)]
    col_starts = [jnp.clip(col_starts[k], 0, 2 * rim + tile_cols - width) for k in range(probes)]
    stacked = jnp.stack((phase, absorption))
    row_starts, col_starts, stacked = lax.optimization_barrier((row_starts, col_starts, stacked))
    extended = with_halo(stacked, (("row", 2), ("col", 3)), rim)
    anchor = jnp.zeros((), jnp.int32)
    fresnel, far_field = build_tables(width)
    share = probes // depth_count
    first = depth_index * share
    cut = jnp.stack(
        [
            lax.dynamic_slice(
                extended, (anchor, anchor, row_starts[k], col_starts[k]), (2, layers, width, width)
            )
            for k in range(probes)
        ],
        axis=2,
    )
    outgoing = [
        lax.dynamic_slice_in_dim(cut, ((depth_index + shift) % depth_count) * share, share, axis=2)
        for shift in range(depth_count)
    ]
    gathered = jnp.concatenate(exchange(outgoing, "depth", depth_count, depth_index), axis=1)
    windows = to_transmit(gathered)
    total_layers = windows.shape[1]
    matrices = [fresnel] * (total_layers - 1) + [far_field]
    adjoints = [adjoint_of(matrix) for matrix in matrices]
    start_wave = probe[:, None]
    far_wave, moved = forward_layers(start_wave, windows, matrices)
    target = lax.dynamic_slice_in_dim(measured[0, 0], first, share)
    power = far_wave[0] ** 2 + far_wave[1] ** 2
    detector = far_wave * (0.25 * (power - target))[None]
    unused, phase_grad, absorb_grad = backward_layers(detector, windows, moved, adjoints)
    parts = jnp.stack((phase_grad, absorb_grad))
    outgoing = [
        lax.dynamic_slice_in_dim(parts, ((depth_index + shift) % depth_count) * layers, layers, axis=1)
        for shift in range(depth_count)
    ]
    returned = jnp.concatenate(exchange(outgoing, "depth", depth_count, depth_index), axis=2)
    grid = jnp.zeros((2, layers) + extended.shape[2:], jnp.float32)
    for k in range(probes):
        grid = grid + place(returned[:, :, k], row_starts[k], col_starts[k], extended.shape[2:])
    owned = fold_both(grid, rim, pass_rows_all, pass_cols_all)
    return (owned[0], owned[1])


def solution(mesh):
    return jax.shard_map(
        per_device,
        mesh=mesh,
        in_specs=(
            P("depth", "row", "col"),
            P("depth", "row", "col"),
            P(),
            P("row", "col", None, None, None),
            P("row", "col", None, None),
        ),
        out_specs=(P("depth", "row", "col"), P("depth", "row", "col")),
        check_vma=False,
    )
```

```python
import math

import jax
import jax.numpy as jnp
from jax import lax
from jax.sharding import PartitionSpec as P

exact_mode = lax.Precision.HIGHEST
wave_mode = lax.Precision.HIGH


def from_behind(value, axis, steps):
    count = lax.axis_size(axis)
    leading, last = (max(0, -steps), min(count, count - steps))
    return lax.ppermute(value, axis, [(source, source + steps) for source in range(leading, last)])


def outside_filled(strip, edge):
    return jnp.stack((jnp.where(edge, 1.0, strip[0]), jnp.where(edge, 0.0, strip[1])))


def with_halo(block, sides, width):
    for axis, dim in sides:
        count = lax.axis_size(axis)
        index = lax.axis_index(axis)
        forward = [(i, i + 1) for i in range(count - 1)]
        backward = [(target, source) for source, target in forward]
        low = lax.ppermute(
            lax.slice_in_dim(block, block.shape[dim] - width, None, axis=dim), axis, forward
        )
        high = lax.ppermute(lax.slice_in_dim(block, 0, width, axis=dim), axis, backward)
        low = outside_filled(low, index == 0)
        high = outside_filled(high, index == count - 1)
        block = jnp.concatenate([low, block, high], axis=dim)
    return block


def matmul_exact(first, second):
    return jnp.dot(first, second, precision=exact_mode, preferred_element_type=jnp.float32)


def build_tables(width):
    index = jnp.arange(width, dtype=jnp.int32)
    product = index[:, None] * index[None, :] % width
    angle = product.astype(jnp.float32) * (2.0 * math.pi / width)
    cosine = jnp.cos(angle)
    sine = jnp.sin(angle)
    signed = jnp.where(index < width // 2, index, index - width)
    chirp = -(signed * signed % (4 * width)).astype(jnp.float32) * (2.0 * math.pi / (4 * width))
    chirp_re = jnp.cos(chirp)[None, :]
    chirp_im = jnp.sin(chirp)[None, :]
    scaled_re = cosine * chirp_re - sine * chirp_im
    scaled_im = cosine * chirp_im + sine * chirp_re
    fresnel_re = matmul_exact(scaled_re, cosine) + matmul_exact(scaled_im, sine)
    fresnel_im = matmul_exact(scaled_im, cosine) - matmul_exact(scaled_re, sine)
    fresnel = jnp.stack((fresnel_re, fresnel_im)) / width
    far_field = jnp.stack((cosine, -sine)) / math.sqrt(width)
    return (fresnel, far_field)


def adjoint_of(matrix):
    return jnp.stack((matrix[0].T, -matrix[1].T))


def left_product(matrix, waves, mode):
    return jnp.einsum(
        "ij,bjk->bik", matrix, waves, precision=mode, preferred_element_type=jnp.float32
    )


def right_product(waves, matrix, mode):
    return jnp.einsum(
        "bij,kj->bik", waves, matrix, precision=mode, preferred_element_type=jnp.float32
    )


def propagate(matrix, waves, mode):
    width = matrix.shape[1]
    tall = matrix.reshape(2 * width, width)
    batch = waves.shape[1]
    both = left_product(tall, waves.reshape((2 * batch,) + waves.shape[2:]), mode)
    from_real = both[:batch]
    from_imag = both[batch:]
    inner_re = from_real[:, :width] - from_imag[:, width:]
    inner_im = from_real[:, width:] + from_imag[:, :width]
    right = right_product(jnp.concatenate((inner_re, inner_im)), tall, mode)
    right_re = right[:batch]
    right_im = right[batch:]
    outer_re = right_re[:, :, :width] - right_im[:, :, width:]
    outer_im = right_re[:, :, width:] + right_im[:, :, :width]
    return jnp.stack((outer_re, outer_im))


def forward_layers(wave, slab, matrices):
    moved_list = []
    for layer in range(slab.shape[1]):
        trans_re = slab[0, layer]
        trans_im = slab[1, layer]
        moved = jnp.stack(
            (trans_re * wave[0] - trans_im * wave[1], trans_re * wave[1] + trans_im * wave[0])
        )
        moved_list.append(moved)
        wave = propagate(matrices[layer], moved, exact_mode)
    return (wave, jnp.stack(moved_list, axis=1))


def backward_layers(grad, slab, moved, adjoints):
    layers = slab.shape[1]
    phase_parts = [None] * layers
    absorb_parts = [None] * layers
    for layer in reversed(range(layers)):
        grad_moved = propagate(adjoints[layer], grad, wave_mode)
        moved_re = moved[0, layer]
        moved_im = moved[1, layer]
        phase_parts[layer] = grad_moved[1] * moved_re - grad_moved[0] * moved_im
        absorb_parts[layer] = -(grad_moved[0] * moved_re + grad_moved[1] * moved_im)
        trans_re = slab[0, layer]
        trans_im = slab[1, layer]
        grad = jnp.stack(
            (
                trans_re * grad_moved[0] + trans_im * grad_moved[1],
                trans_re * grad_moved[1] - trans_im * grad_moved[0],
            )
        )
    return (grad, jnp.stack(phase_parts), jnp.stack(absorb_parts))


def pass_rows_all(strip, steps):
    return from_behind(strip, "row", steps)


def pass_cols_all(strip, steps):
    return from_behind(strip, "col", steps)


def fold_rows(grid, rim, mover):
    inner = grid.shape[2] - 2 * rim
    from_above = mover(grid[:, :, inner + rim :], 1)
    from_below = mover(grid[:, :, :rim], -1)
    core = grid[:, :, rim : rim + inner]
    core = core.at[:, :, :rim].add(from_above)
    return core.at[:, :, inner - rim :].add(from_below)


def fold_cols(grid, rim, mover):
    inner = grid.shape[3] - 2 * rim
    from_left = mover(grid[:, :, :, inner + rim :], 1)
    from_right = mover(grid[:, :, :, :rim], -1)
    core = grid[:, :, :, rim : rim + inner]
    core = core.at[:, :, :, :rim].add(from_left)
    return core.at[:, :, :, inner - rim :].add(from_right)


def fold_both(grid, rim, row_mover, col_mover):
    return fold_rows(fold_cols(grid, rim, col_mover), rim, row_mover)


def to_transmit(extended):
    damping = jnp.exp(-extended[1])
    return jnp.stack((damping * jnp.cos(extended[0]), damping * jnp.sin(extended[0])))


def place(patch, row, col, frame):
    height, span = frame
    extra_rows = height - patch.shape[-2]
    extra_cols = span - patch.shape[-1]
    padded = jnp.pad(patch, ((0, 0), (0, 0), (extra_rows, extra_rows), (extra_cols, extra_cols)))
    anchor = jnp.zeros((), jnp.int32)
    start = (anchor, anchor, extra_rows - row, extra_cols - col)
    return lax.dynamic_slice(padded, start, patch.shape[:2] + (height, span))


def per_device(phase, absorption, probe, measured, offsets):
    layers, tile_rows, tile_cols = phase.shape
    width = probe.shape[1]
    rim = width // 2
    probes = offsets.shape[2]
    depth_count = lax.axis_size("depth")
    depth_index = lax.axis_index("depth")
    row_index = lax.axis_index("row")
    col_index = lax.axis_index("col")
    corners = offsets[0, 0]
    row_starts = corners[:, 0] - row_index * tile_rows + rim
    col_starts = corners[:, 1] - col_index * tile_cols + rim
    row_starts = [jnp.clip(row_starts[k], 0, 2 * rim + tile_rows - width) for k in range(probes)]
    col_starts = [jnp.clip(col_starts[k], 0, 2 * rim + tile_cols - width) for k in range(probes)]
    stacked = to_transmit(jnp.stack((phase, absorption)))
    row_starts, col_starts, stacked = lax.optimization_barrier((row_starts, col_starts, stacked))
    extended = with_halo(stacked, (("row", 2), ("col", 3)), rim)
    anchor = jnp.zeros((), jnp.int32)
    fresnel, far_field = build_tables(width)
    share = probes // depth_count
    first = depth_index * share
    cut = jnp.stack(
        [
            lax.dynamic_slice(
                extended, (anchor, anchor, row_starts[k], col_starts[k]), (2, layers, width, width)
            )
            for k in range(probes)
        ],
        axis=2,
    )
    gathered = lax.all_to_all(cut, "depth", 2, 1, tiled=True)
    windows = gathered
    total_layers = windows.shape[1]
    matrices = [fresnel] * (total_layers - 1) + [far_field]
    adjoints = [adjoint_of(matrix) for matrix in matrices]
    start_wave = probe[:, None]
    far_wave, moved = forward_layers(start_wave, windows, matrices)
    target = lax.dynamic_slice_in_dim(measured[0, 0], first, share)
    power = far_wave[0] ** 2 + far_wave[1] ** 2
    detector = far_wave * (0.25 * (power - target))[None]
    unused, phase_grad, absorb_grad = backward_layers(detector, windows, moved, adjoints)
    parts = jnp.stack((phase_grad, absorb_grad))
    returned = lax.all_to_all(parts, "depth", 1, 2, tiled=True)
    grid = jnp.zeros((2, layers) + extended.shape[2:], jnp.float32)
    for k in range(probes):
        grid = grid + place(returned[:, :, k], row_starts[k], col_starts[k], extended.shape[2:])
    owned = fold_both(grid, rim, pass_rows_all, pass_cols_all)
    return (owned[0], owned[1])


def solution(mesh):
    return jax.shard_map(
        per_device,
        mesh=mesh,
        in_specs=(
            P("depth", "row", "col"),
            P("depth", "row", "col"),
            P(),
            P("row", "col", None, None, None),
            P("row", "col", None, None),
        ),
        out_specs=(P("depth", "row", "col"), P("depth", "row", "col")),
        check_vma=False,
    )
```

```python
import math

import jax
import jax.numpy as jnp
from jax import lax
from jax.sharding import PartitionSpec as P

exact_mode = lax.Precision.HIGHEST
wave_mode = lax.Precision.HIGH


def from_behind(value, axis, steps):
    count = lax.axis_size(axis)
    leading, last = (max(0, -steps), min(count, count - steps))
    return lax.ppermute(value, axis, [(source, source + steps) for source in range(leading, last)])


def outside_filled(strip, edge):
    return jnp.stack((jnp.where(edge, 1.0, strip[0]), jnp.where(edge, 0.0, strip[1])))


def with_halo(block, sides, width):
    for axis, dim in sides:
        count = lax.axis_size(axis)
        index = lax.axis_index(axis)
        forward = [(i, i + 1) for i in range(count - 1)]
        backward = [(target, source) for source, target in forward]
        low = lax.ppermute(
            lax.slice_in_dim(block, block.shape[dim] - width, None, axis=dim), axis, forward
        )
        high = lax.ppermute(lax.slice_in_dim(block, 0, width, axis=dim), axis, backward)
        low = outside_filled(low, index == 0)
        high = outside_filled(high, index == count - 1)
        block = jnp.concatenate([low, block, high], axis=dim)
    return block


def matmul_exact(first, second):
    return jnp.dot(first, second, precision=exact_mode, preferred_element_type=jnp.float32)


def build_tables(width):
    index = jnp.arange(width, dtype=jnp.int32)
    product = index[:, None] * index[None, :] % width
    angle = product.astype(jnp.float32) * (2.0 * math.pi / width)
    cosine = jnp.cos(angle)
    sine = jnp.sin(angle)
    signed = jnp.where(index < width // 2, index, index - width)
    chirp = -(signed * signed % (4 * width)).astype(jnp.float32) * (2.0 * math.pi / (4 * width))
    chirp_re = jnp.cos(chirp)[None, :]
    chirp_im = jnp.sin(chirp)[None, :]
    scaled_re = cosine * chirp_re - sine * chirp_im
    scaled_im = cosine * chirp_im + sine * chirp_re
    fresnel_re = matmul_exact(scaled_re, cosine) + matmul_exact(scaled_im, sine)
    fresnel_im = matmul_exact(scaled_im, cosine) - matmul_exact(scaled_re, sine)
    fresnel = jnp.stack((fresnel_re, fresnel_im)) / width
    far_field = jnp.stack((cosine, -sine)) / math.sqrt(width)
    return (fresnel, far_field)


def adjoint_of(matrix):
    return jnp.stack((matrix[0].T, -matrix[1].T))


def left_product(matrix, waves, mode):
    return jnp.einsum(
        "ij,bjk->bik", matrix, waves, precision=mode, preferred_element_type=jnp.float32
    )


def right_product(waves, matrix, mode):
    return jnp.einsum(
        "bij,kj->bik", waves, matrix, precision=mode, preferred_element_type=jnp.float32
    )


def propagate(matrix, waves, mode):
    width = matrix.shape[1]
    tall = matrix.reshape(2 * width, width)
    batch = waves.shape[1]
    both = left_product(tall, waves.reshape((2 * batch,) + waves.shape[2:]), mode)
    from_real = both[:batch]
    from_imag = both[batch:]
    inner_re = from_real[:, :width] - from_imag[:, width:]
    inner_im = from_real[:, width:] + from_imag[:, :width]
    right = right_product(jnp.concatenate((inner_re, inner_im)), tall, mode)
    right_re = right[:batch]
    right_im = right[batch:]
    outer_re = right_re[:, :, :width] - right_im[:, :, width:]
    outer_im = right_re[:, :, width:] + right_im[:, :, :width]
    return jnp.stack((outer_re, outer_im))


def forward_layers(wave, slab, matrices):
    moved_list = []
    for layer in range(slab.shape[1]):
        trans_re = slab[0, layer]
        trans_im = slab[1, layer]
        moved = jnp.stack(
            (trans_re * wave[0] - trans_im * wave[1], trans_re * wave[1] + trans_im * wave[0])
        )
        moved_list.append(moved)
        wave = propagate(matrices[layer], moved, exact_mode)
    return (wave, jnp.stack(moved_list, axis=1))


def backward_layers(grad, slab, moved, adjoints):
    layers = slab.shape[1]
    phase_parts = [None] * layers
    absorb_parts = [None] * layers
    for layer in reversed(range(layers)):
        grad_moved = propagate(adjoints[layer], grad, wave_mode)
        moved_re = moved[0, layer]
        moved_im = moved[1, layer]
        phase_parts[layer] = grad_moved[1] * moved_re - grad_moved[0] * moved_im
        absorb_parts[layer] = -(grad_moved[0] * moved_re + grad_moved[1] * moved_im)
        trans_re = slab[0, layer]
        trans_im = slab[1, layer]
        grad = jnp.stack(
            (
                trans_re * grad_moved[0] + trans_im * grad_moved[1],
                trans_re * grad_moved[1] - trans_im * grad_moved[0],
            )
        )
    return (grad, jnp.stack(phase_parts), jnp.stack(absorb_parts))


def pass_rows_all(strip, steps):
    return from_behind(strip, "row", steps)


def pass_cols_all(strip, steps):
    return from_behind(strip, "col", steps)


def fold_rows(grid, rim, mover):
    inner = grid.shape[2] - 2 * rim
    from_above = mover(grid[:, :, inner + rim :], 1)
    from_below = mover(grid[:, :, :rim], -1)
    core = grid[:, :, rim : rim + inner]
    core = core.at[:, :, :rim].add(from_above)
    return core.at[:, :, inner - rim :].add(from_below)


def fold_cols(grid, rim, mover):
    inner = grid.shape[3] - 2 * rim
    from_left = mover(grid[:, :, :, inner + rim :], 1)
    from_right = mover(grid[:, :, :, :rim], -1)
    core = grid[:, :, :, rim : rim + inner]
    core = core.at[:, :, :, :rim].add(from_left)
    return core.at[:, :, :, inner - rim :].add(from_right)


def fold_both(grid, rim, row_mover, col_mover):
    return fold_rows(fold_cols(grid, rim, col_mover), rim, row_mover)


def to_transmit(extended):
    damping = jnp.exp(-extended[1])
    return jnp.stack((damping * jnp.cos(extended[0]), damping * jnp.sin(extended[0])))


def place(patch, row, col, frame):
    height, span = frame
    extra_rows = height - patch.shape[-2]
    extra_cols = span - patch.shape[-1]
    padded = jnp.pad(patch, ((0, 0), (0, 0), (extra_rows, extra_rows), (extra_cols, extra_cols)))
    anchor = jnp.zeros((), jnp.int32)
    start = (anchor, anchor, extra_rows - row, extra_cols - col)
    return lax.dynamic_slice(padded, start, patch.shape[:2] + (height, span))


def per_device(phase, absorption, probe, measured, offsets):
    layers, tile_rows, tile_cols = phase.shape
    width = probe.shape[1]
    rim = width // 2
    probes = offsets.shape[2]
    depth_count = lax.axis_size("depth")
    depth_index = lax.axis_index("depth")
    row_index = lax.axis_index("row")
    col_index = lax.axis_index("col")
    corners = offsets[0, 0]
    row_starts = corners[:, 0] - row_index * tile_rows + rim
    col_starts = corners[:, 1] - col_index * tile_cols + rim
    row_starts = [jnp.clip(row_starts[k], 0, 2 * rim + tile_rows - width) for k in range(probes)]
    col_starts = [jnp.clip(col_starts[k], 0, 2 * rim + tile_cols - width) for k in range(probes)]
    share = probes // depth_count
    source_rows = []
    source_cols = []
    for shift in range(depth_count):
        source = (depth_index - shift) % depth_count
        source_rows.append([lax.select_n(source * share + slot, *row_starts) for slot in range(share)])
        source_cols.append([lax.select_n(source * share + slot, *col_starts) for slot in range(share)])
    stacked = to_transmit(jnp.stack((phase, absorption)))
    row_starts, col_starts, source_rows, source_cols, stacked = lax.optimization_barrier(
        (row_starts, col_starts, source_rows, source_cols, stacked)
    )
    extended = with_halo(stacked, (("row", 2), ("col", 3)), rim)
    anchor = jnp.zeros((), jnp.int32)
    fresnel, far_field = build_tables(width)
    share = probes // depth_count
    first = depth_index * share
    cut = jnp.stack(
        [
            lax.dynamic_slice(
                extended, (anchor, anchor, row_starts[k], col_starts[k]), (2, layers, width, width)
            )
            for k in range(probes)
        ],
        axis=2,
    )
    gathered = lax.all_to_all(cut, "depth", 2, 1, tiled=True)
    windows = gathered
    total_layers = windows.shape[1]
    matrices = [fresnel] * (total_layers - 1) + [far_field]
    adjoints = [adjoint_of(matrix) for matrix in matrices]
    start_wave = probe[:, None]
    far_wave, moved = forward_layers(start_wave, windows, matrices)
    target = lax.dynamic_slice_in_dim(measured[0, 0], first, share)
    power = far_wave[0] ** 2 + far_wave[1] ** 2
    detector = far_wave * (0.25 * (power - target))[None]
    unused, phase_grad, absorb_grad = backward_layers(detector, windows, moved, adjoints)
    parts = jnp.stack((phase_grad, absorb_grad))
    grid = jnp.zeros((2, layers) + extended.shape[2:], jnp.float32)
    for shift in range(depth_count):
        chunk = lax.dynamic_slice_in_dim(
            parts, ((depth_index + shift) % depth_count) * layers, layers, axis=1
        )
        if shift > 0:
            pairs = [(i, (i + shift) % depth_count) for i in range(depth_count)]
            chunk = lax.ppermute(chunk, "depth", pairs)
        for slot in range(share):
            grid = grid + place(
                chunk[:, :, slot], source_rows[shift][slot], source_cols[shift][slot], extended.shape[2:]
            )
    owned = fold_both(grid, rim, pass_rows_all, pass_cols_all)
    return (owned[0], owned[1])


def solution(mesh):
    return jax.shard_map(
        per_device,
        mesh=mesh,
        in_specs=(
            P("depth", "row", "col"),
            P("depth", "row", "col"),
            P(),
            P("row", "col", None, None, None),
            P("row", "col", None, None),
        ),
        out_specs=(P("depth", "row", "col"), P("depth", "row", "col")),
        check_vma=False,
    )
```

```python
import math

import jax
import jax.numpy as jnp
from jax import lax
from jax.sharding import PartitionSpec as P

exact_mode = lax.Precision.HIGHEST
wave_mode = lax.Precision.HIGH


def from_behind(value, axis, steps):
    count = lax.axis_size(axis)
    leading, last = (max(0, -steps), min(count, count - steps))
    return lax.ppermute(value, axis, [(source, source + steps) for source in range(leading, last)])


def outside_filled(strip, edge):
    return jnp.stack((jnp.where(edge, 1.0, strip[0]), jnp.where(edge, 0.0, strip[1])))


def with_halo(block, sides, width):
    for axis, dim in sides:
        count = lax.axis_size(axis)
        index = lax.axis_index(axis)
        forward = [(i, i + 1) for i in range(count - 1)]
        backward = [(target, source) for source, target in forward]
        low = lax.ppermute(
            lax.slice_in_dim(block, block.shape[dim] - width, None, axis=dim), axis, forward
        )
        high = lax.ppermute(lax.slice_in_dim(block, 0, width, axis=dim), axis, backward)
        low = outside_filled(low, index == 0)
        high = outside_filled(high, index == count - 1)
        block = jnp.concatenate([low, block, high], axis=dim)
    return block


def matmul_exact(first, second):
    return jnp.dot(first, second, precision=exact_mode, preferred_element_type=jnp.float32)


def build_tables(width):
    index = jnp.arange(width, dtype=jnp.int32)
    product = index[:, None] * index[None, :] % width
    angle = product.astype(jnp.float32) * (2.0 * math.pi / width)
    cosine = jnp.cos(angle)
    sine = jnp.sin(angle)
    signed = jnp.where(index < width // 2, index, index - width)
    chirp = -(signed * signed % (4 * width)).astype(jnp.float32) * (2.0 * math.pi / (4 * width))
    chirp_re = jnp.cos(chirp)[None, :]
    chirp_im = jnp.sin(chirp)[None, :]
    scaled_re = cosine * chirp_re - sine * chirp_im
    scaled_im = cosine * chirp_im + sine * chirp_re
    fresnel_re = matmul_exact(scaled_re, cosine) + matmul_exact(scaled_im, sine)
    fresnel_im = matmul_exact(scaled_im, cosine) - matmul_exact(scaled_re, sine)
    fresnel = jnp.stack((fresnel_re, fresnel_im)) / width
    far_field = jnp.stack((cosine, -sine)) / math.sqrt(width)
    return (fresnel, far_field)


def adjoint_of(matrix):
    return jnp.stack((matrix[0].T, -matrix[1].T))


def left_product(matrix, waves, mode):
    return jnp.einsum(
        "ij,bjk->bik", matrix, waves, precision=mode, preferred_element_type=jnp.float32
    )


def right_product(waves, matrix, mode):
    return jnp.einsum(
        "bij,kj->bik", waves, matrix, precision=mode, preferred_element_type=jnp.float32
    )


def propagate(matrix, waves, mode):
    width = matrix.shape[1]
    tall = matrix.reshape(2 * width, width)
    batch = waves.shape[1]
    both = left_product(tall, waves.reshape((2 * batch,) + waves.shape[2:]), mode)
    from_real = both[:batch]
    from_imag = both[batch:]
    inner_re = from_real[:, :width] - from_imag[:, width:]
    inner_im = from_real[:, width:] + from_imag[:, :width]
    right = right_product(jnp.concatenate((inner_re, inner_im)), tall, mode)
    right_re = right[:batch]
    right_im = right[batch:]
    outer_re = right_re[:, :, :width] - right_im[:, :, width:]
    outer_im = right_re[:, :, width:] + right_im[:, :, :width]
    return jnp.stack((outer_re, outer_im))


def forward_layers(wave, slab, matrices):
    moved_list = []
    for layer in range(slab.shape[1]):
        trans_re = slab[0, layer]
        trans_im = slab[1, layer]
        moved = jnp.stack(
            (trans_re * wave[0] - trans_im * wave[1], trans_re * wave[1] + trans_im * wave[0])
        )
        moved_list.append(moved)
        wave = propagate(matrices[layer], moved, exact_mode)
    return (wave, jnp.stack(moved_list, axis=1))


def backward_layers(grad, slab, moved, adjoints):
    layers = slab.shape[1]
    phase_parts = [None] * layers
    absorb_parts = [None] * layers
    for layer in reversed(range(layers)):
        grad_moved = propagate(adjoints[layer], grad, wave_mode)
        moved_re = moved[0, layer]
        moved_im = moved[1, layer]
        phase_parts[layer] = grad_moved[1] * moved_re - grad_moved[0] * moved_im
        absorb_parts[layer] = -(grad_moved[0] * moved_re + grad_moved[1] * moved_im)
        trans_re = slab[0, layer]
        trans_im = slab[1, layer]
        grad = jnp.stack(
            (
                trans_re * grad_moved[0] + trans_im * grad_moved[1],
                trans_re * grad_moved[1] - trans_im * grad_moved[0],
            )
        )
    return (grad, jnp.stack(phase_parts), jnp.stack(absorb_parts))


def pass_rows_all(strip, steps):
    return from_behind(strip, "row", steps)


def pass_cols_all(strip, steps):
    return from_behind(strip, "col", steps)


def fold_rows(grid, rim, mover):
    inner = grid.shape[2] - 2 * rim
    from_above = mover(grid[:, :, inner + rim :], 1)
    from_below = mover(grid[:, :, :rim], -1)
    core = grid[:, :, rim : rim + inner]
    core = core.at[:, :, :rim].add(from_above)
    return core.at[:, :, inner - rim :].add(from_below)


def fold_cols(grid, rim, mover):
    inner = grid.shape[3] - 2 * rim
    from_left = mover(grid[:, :, :, inner + rim :], 1)
    from_right = mover(grid[:, :, :, :rim], -1)
    core = grid[:, :, :, rim : rim + inner]
    core = core.at[:, :, :, :rim].add(from_left)
    return core.at[:, :, :, inner - rim :].add(from_right)


def fold_both(grid, rim, row_mover, col_mover):
    return fold_rows(fold_cols(grid, rim, col_mover), rim, row_mover)


def to_transmit(extended):
    damping = jnp.exp(-extended[1])
    return jnp.stack((damping * jnp.cos(extended[0]), damping * jnp.sin(extended[0])))


def place(patch, row, col, frame):
    height, span = frame
    extra_rows = height - patch.shape[-2]
    extra_cols = span - patch.shape[-1]
    padded = jnp.pad(patch, ((0, 0), (0, 0), (extra_rows, extra_rows), (extra_cols, extra_cols)))
    anchor = jnp.zeros((), jnp.int32)
    start = (anchor, anchor, extra_rows - row, extra_cols - col)
    return lax.dynamic_slice(padded, start, patch.shape[:2] + (height, span))


def per_device(phase, absorption, probe, measured, offsets):
    layers, tile_rows, tile_cols = phase.shape
    width = probe.shape[1]
    rim = width // 2
    probes = offsets.shape[2]
    depth_count = lax.axis_size("depth")
    depth_index = lax.axis_index("depth")
    row_index = lax.axis_index("row")
    col_index = lax.axis_index("col")
    stacked = to_transmit(jnp.stack((phase, absorption)))
    tall_slab = with_halo(stacked, (("row", 2),), rim)
    after = (stacked[0, 0, 0, 0] * 0.0).astype(jnp.int32)
    corners = offsets[0, 0] + after
    row_starts = corners[:, 0] - row_index * tile_rows + rim
    col_starts = corners[:, 1] - col_index * tile_cols + rim
    row_starts = [jnp.clip(row_starts[k], 0, 2 * rim + tile_rows - width) for k in range(probes)]
    col_starts = [jnp.clip(col_starts[k], 0, 2 * rim + tile_cols - width) for k in range(probes)]
    share = probes // depth_count
    source_rows = []
    source_cols = []
    for shift in range(depth_count):
        source = (depth_index - shift) % depth_count
        source_rows.append([lax.select_n(source * share + slot, *row_starts) for slot in range(share)])
        source_cols.append([lax.select_n(source * share + slot, *col_starts) for slot in range(share)])
    row_starts, col_starts, source_rows, source_cols, tall_slab = lax.optimization_barrier(
        (row_starts, col_starts, source_rows, source_cols, tall_slab)
    )
    extended = with_halo(tall_slab, (("col", 3),), rim)
    anchor = jnp.zeros((), jnp.int32)
    fresnel, far_field = build_tables(width)
    share = probes // depth_count
    first = depth_index * share
    cut = jnp.stack(
        [
            lax.dynamic_slice(
                extended, (anchor, anchor, row_starts[k], col_starts[k]), (2, layers, width, width)
            )
            for k in range(probes)
        ],
        axis=2,
    )
    gathered = lax.all_to_all(cut, "depth", 2, 1, tiled=True)
    windows = gathered
    total_layers = windows.shape[1]
    matrices = [fresnel] * (total_layers - 1) + [far_field]
    adjoints = [adjoint_of(matrix) for matrix in matrices]
    start_wave = probe[:, None]
    far_wave, moved = forward_layers(start_wave, windows, matrices)
    target = lax.dynamic_slice_in_dim(measured[0, 0], first, share)
    power = far_wave[0] ** 2 + far_wave[1] ** 2
    detector = far_wave * (0.25 * (power - target))[None]
    unused, phase_grad, absorb_grad = backward_layers(detector, windows, moved, adjoints)
    parts = jnp.stack((phase_grad, absorb_grad))
    grid = jnp.zeros((2, layers) + extended.shape[2:], jnp.float32)
    for shift in range(depth_count):
        chunk = lax.dynamic_slice_in_dim(
            parts, ((depth_index + shift) % depth_count) * layers, layers, axis=1
        )
        if shift > 0:
            pairs = [(i, (i + shift) % depth_count) for i in range(depth_count)]
            chunk = lax.ppermute(chunk, "depth", pairs)
        for slot in range(share):
            grid = grid + place(
                chunk[:, :, slot], source_rows[shift][slot], source_cols[shift][slot], extended.shape[2:]
            )
    owned = fold_both(grid, rim, pass_rows_all, pass_cols_all)
    return (owned[0], owned[1])


def solution(mesh):
    return jax.shard_map(
        per_device,
        mesh=mesh,
        in_specs=(
            P("depth", "row", "col"),
            P("depth", "row", "col"),
            P(),
            P("row", "col", None, None, None),
            P("row", "col", None, None),
        ),
        out_specs=(P("depth", "row", "col"), P("depth", "row", "col")),
        check_vma=False,
    )
```

```python
import math

import jax
import jax.numpy as jnp
from jax import lax
from jax.sharding import PartitionSpec as P

exact_mode = lax.Precision.HIGHEST
wave_mode = lax.Precision.HIGH


def from_behind(value, axis, steps):
    count = lax.axis_size(axis)
    leading, last = (max(0, -steps), min(count, count - steps))
    return lax.ppermute(value, axis, [(source, source + steps) for source in range(leading, last)])


def outside_filled(strip, edge):
    return jnp.stack((jnp.where(edge, 1.0, strip[0]), jnp.where(edge, 0.0, strip[1])))


def with_halo(block, sides, width):
    for axis, dim in sides:
        count = lax.axis_size(axis)
        index = lax.axis_index(axis)
        forward = [(i, i + 1) for i in range(count - 1)]
        backward = [(target, source) for source, target in forward]
        low = lax.ppermute(
            lax.slice_in_dim(block, block.shape[dim] - width, None, axis=dim), axis, forward
        )
        high = lax.ppermute(lax.slice_in_dim(block, 0, width, axis=dim), axis, backward)
        low = outside_filled(low, index == 0)
        high = outside_filled(high, index == count - 1)
        block = jnp.concatenate([low, block, high], axis=dim)
    return block


def matmul_exact(first, second):
    return jnp.dot(first, second, precision=exact_mode, preferred_element_type=jnp.float32)


def build_tables(width):
    index = jnp.arange(width, dtype=jnp.int32)
    product = index[:, None] * index[None, :] % width
    angle = product.astype(jnp.float32) * (2.0 * math.pi / width)
    cosine = jnp.cos(angle)
    sine = jnp.sin(angle)
    signed = jnp.where(index < width // 2, index, index - width)
    chirp = -(signed * signed % (4 * width)).astype(jnp.float32) * (2.0 * math.pi / (4 * width))
    chirp_re = jnp.cos(chirp)[None, :]
    chirp_im = jnp.sin(chirp)[None, :]
    scaled_re = cosine * chirp_re - sine * chirp_im
    scaled_im = cosine * chirp_im + sine * chirp_re
    fresnel_re = matmul_exact(scaled_re, cosine) + matmul_exact(scaled_im, sine)
    fresnel_im = matmul_exact(scaled_im, cosine) - matmul_exact(scaled_re, sine)
    fresnel = jnp.stack((fresnel_re, fresnel_im)) / width
    far_field = jnp.stack((cosine, -sine)) / math.sqrt(width)
    return (fresnel, far_field)


def adjoint_of(matrix):
    return jnp.stack((matrix[0].T, -matrix[1].T))


def left_product(matrix, waves, mode):
    return jnp.einsum(
        "ij,bjk->bik", matrix, waves, precision=mode, preferred_element_type=jnp.float32
    )


def right_product(waves, matrix, mode):
    return jnp.einsum(
        "bij,kj->bik", waves, matrix, precision=mode, preferred_element_type=jnp.float32
    )


def propagate(matrix, waves, mode):
    width = matrix.shape[1]
    tall = matrix.reshape(2 * width, width)
    batch = waves.shape[1]
    both = left_product(tall, waves.reshape((2 * batch,) + waves.shape[2:]), mode)
    from_real = both[:batch]
    from_imag = both[batch:]
    inner_re = from_real[:, :width] - from_imag[:, width:]
    inner_im = from_real[:, width:] + from_imag[:, :width]
    right = right_product(jnp.concatenate((inner_re, inner_im)), tall, mode)
    right_re = right[:batch]
    right_im = right[batch:]
    outer_re = right_re[:, :, :width] - right_im[:, :, width:]
    outer_im = right_re[:, :, width:] + right_im[:, :, :width]
    return jnp.stack((outer_re, outer_im))


def propagate_three(matrix, waves, mode):
    first, second = matrix[0], matrix[1]
    factors = jnp.stack((first, second, first + second))
    left = jnp.stack((waves[0], waves[1], waves[0] + waves[1]))
    prod = jnp.einsum(
        "nij,nbjk->nbik", factors, left, precision=mode, preferred_element_type=jnp.float32
    )
    inner_re = prod[0] - prod[1]
    inner_im = prod[2] - prod[0] - prod[1]
    right = jnp.stack((inner_re, inner_im, inner_re + inner_im))
    prod = jnp.einsum(
        "nbij,nkj->nbik", right, factors, precision=mode, preferred_element_type=jnp.float32
    )
    return jnp.stack((prod[0] - prod[1], prod[2] - prod[0] - prod[1]))


def forward_layers(wave, slab, matrices):
    moved_list = []
    for layer in range(slab.shape[1]):
        trans_re = slab[0, layer]
        trans_im = slab[1, layer]
        moved = jnp.stack(
            (trans_re * wave[0] - trans_im * wave[1], trans_re * wave[1] + trans_im * wave[0])
        )
        moved_list.append(moved)
        wave = propagate_three(matrices[layer], moved, exact_mode)
    return (wave, jnp.stack(moved_list, axis=1))


def backward_layers(grad, slab, moved, adjoints):
    layers = slab.shape[1]
    phase_parts = [None] * layers
    absorb_parts = [None] * layers
    for layer in reversed(range(layers)):
        grad_moved = propagate(adjoints[layer], grad, wave_mode)
        moved_re = moved[0, layer]
        moved_im = moved[1, layer]
        phase_parts[layer] = grad_moved[1] * moved_re - grad_moved[0] * moved_im
        absorb_parts[layer] = -(grad_moved[0] * moved_re + grad_moved[1] * moved_im)
        trans_re = slab[0, layer]
        trans_im = slab[1, layer]
        grad = jnp.stack(
            (
                trans_re * grad_moved[0] + trans_im * grad_moved[1],
                trans_re * grad_moved[1] - trans_im * grad_moved[0],
            )
        )
    return (grad, jnp.stack(phase_parts), jnp.stack(absorb_parts))


def pass_rows_all(strip, steps):
    return from_behind(strip, "row", steps)


def pass_cols_all(strip, steps):
    return from_behind(strip, "col", steps)


def fold_rows(grid, rim, mover):
    inner = grid.shape[2] - 2 * rim
    from_above = mover(grid[:, :, inner + rim :], 1)
    from_below = mover(grid[:, :, :rim], -1)
    core = grid[:, :, rim : rim + inner]
    core = core.at[:, :, :rim].add(from_above)
    return core.at[:, :, inner - rim :].add(from_below)


def fold_cols(grid, rim, mover):
    inner = grid.shape[3] - 2 * rim
    from_left = mover(grid[:, :, :, inner + rim :], 1)
    from_right = mover(grid[:, :, :, :rim], -1)
    core = grid[:, :, :, rim : rim + inner]
    core = core.at[:, :, :, :rim].add(from_left)
    return core.at[:, :, :, inner - rim :].add(from_right)


def fold_both(grid, rim, row_mover, col_mover):
    return fold_rows(fold_cols(grid, rim, col_mover), rim, row_mover)


def to_transmit(extended):
    damping = jnp.exp(-extended[1])
    return jnp.stack((damping * jnp.cos(extended[0]), damping * jnp.sin(extended[0])))


def place(patch, row, col, frame):
    height, span = frame
    extra_rows = height - patch.shape[-2]
    extra_cols = span - patch.shape[-1]
    padded = jnp.pad(patch, ((0, 0), (0, 0), (extra_rows, extra_rows), (extra_cols, extra_cols)))
    anchor = jnp.zeros((), jnp.int32)
    start = (anchor, anchor, extra_rows - row, extra_cols - col)
    return lax.dynamic_slice(padded, start, patch.shape[:2] + (height, span))


def per_device(phase, absorption, probe, measured, offsets):
    layers, tile_rows, tile_cols = phase.shape
    width = probe.shape[1]
    rim = width // 2
    probes = offsets.shape[2]
    depth_count = lax.axis_size("depth")
    depth_index = lax.axis_index("depth")
    row_index = lax.axis_index("row")
    col_index = lax.axis_index("col")
    stacked = to_transmit(jnp.stack((phase, absorption)))
    tall_slab = with_halo(stacked, (("row", 2),), rim)
    after = (stacked[0, 0, 0, 0] * 0.0).astype(jnp.int32)
    corners = offsets[0, 0] + after
    row_starts = corners[:, 0] - row_index * tile_rows + rim
    col_starts = corners[:, 1] - col_index * tile_cols + rim
    row_starts = [jnp.clip(row_starts[k], 0, 2 * rim + tile_rows - width) for k in range(probes)]
    col_starts = [jnp.clip(col_starts[k], 0, 2 * rim + tile_cols - width) for k in range(probes)]
    share = probes // depth_count
    source_rows = []
    source_cols = []
    for shift in range(depth_count):
        source = (depth_index - shift) % depth_count
        source_rows.append([lax.select_n(source * share + slot, *row_starts) for slot in range(share)])
        source_cols.append([lax.select_n(source * share + slot, *col_starts) for slot in range(share)])
    row_starts, col_starts, source_rows, source_cols, tall_slab = lax.optimization_barrier(
        (row_starts, col_starts, source_rows, source_cols, tall_slab)
    )
    extended = with_halo(tall_slab, (("col", 3),), rim)
    anchor = jnp.zeros((), jnp.int32)
    fresnel, far_field = build_tables(width)
    share = probes // depth_count
    first = depth_index * share
    cut = jnp.stack(
        [
            lax.dynamic_slice(
                extended, (anchor, anchor, row_starts[k], col_starts[k]), (2, layers, width, width)
            )
            for k in range(probes)
        ],
        axis=2,
    )
    gathered = lax.all_to_all(cut, "depth", 2, 1, tiled=True)
    windows = gathered
    total_layers = windows.shape[1]
    matrices = [fresnel] * (total_layers - 1) + [far_field]
    adjoints = [adjoint_of(matrix) for matrix in matrices]
    start_wave = probe[:, None]
    far_wave, moved = forward_layers(start_wave, windows, matrices)
    target = lax.dynamic_slice_in_dim(measured[0, 0], first, share)
    power = far_wave[0] ** 2 + far_wave[1] ** 2
    detector = far_wave * (0.25 * (power - target))[None]
    unused, phase_grad, absorb_grad = backward_layers(detector, windows, moved, adjoints)
    parts = jnp.stack((phase_grad, absorb_grad))
    grid = jnp.zeros((2, layers) + extended.shape[2:], jnp.float32)
    for shift in range(depth_count):
        chunk = lax.dynamic_slice_in_dim(
            parts, ((depth_index + shift) % depth_count) * layers, layers, axis=1
        )
        if shift > 0:
            pairs = [(i, (i + shift) % depth_count) for i in range(depth_count)]
            chunk = lax.ppermute(chunk, "depth", pairs)
        for slot in range(share):
            grid = grid + place(
                chunk[:, :, slot], source_rows[shift][slot], source_cols[shift][slot], extended.shape[2:]
            )
    owned = fold_both(grid, rim, pass_rows_all, pass_cols_all)
    return (owned[0], owned[1])


def solution(mesh):
    return jax.shard_map(
        per_device,
        mesh=mesh,
        in_specs=(
            P("depth", "row", "col"),
            P("depth", "row", "col"),
            P(),
            P("row", "col", None, None, None),
            P("row", "col", None, None),
        ),
        out_specs=(P("depth", "row", "col"), P("depth", "row", "col")),
        check_vma=False,
    )
```

```python
import math

import jax
import jax.numpy as jnp
from jax import lax
from jax.sharding import PartitionSpec as P

exact_mode = lax.Precision.HIGHEST
wave_mode = lax.Precision.HIGH


def from_behind(value, axis, steps):
    count = lax.axis_size(axis)
    leading, last = (max(0, -steps), min(count, count - steps))
    return lax.ppermute(value, axis, [(source, source + steps) for source in range(leading, last)])


def outside_filled(strip, edge):
    return jnp.stack((jnp.where(edge, 1.0, strip[0]), jnp.where(edge, 0.0, strip[1])))


def with_halo(block, sides, width):
    for axis, dim in sides:
        count = lax.axis_size(axis)
        index = lax.axis_index(axis)
        forward = [(i, i + 1) for i in range(count - 1)]
        backward = [(target, source) for source, target in forward]
        low = lax.ppermute(
            lax.slice_in_dim(block, block.shape[dim] - width, None, axis=dim), axis, forward
        )
        high = lax.ppermute(lax.slice_in_dim(block, 0, width, axis=dim), axis, backward)
        low = outside_filled(low, index == 0)
        high = outside_filled(high, index == count - 1)
        block = jnp.concatenate([low, block, high], axis=dim)
    return block


def matmul_exact(first, second):
    return jnp.dot(first, second, precision=exact_mode, preferred_element_type=jnp.float32)


def build_tables(width):
    index = jnp.arange(width, dtype=jnp.int32)
    product = index[:, None] * index[None, :] % width
    angle = product.astype(jnp.float32) * (2.0 * math.pi / width)
    cosine = jnp.cos(angle)
    sine = jnp.sin(angle)
    signed = jnp.where(index < width // 2, index, index - width)
    chirp = -(signed * signed % (4 * width)).astype(jnp.float32) * (2.0 * math.pi / (4 * width))
    chirp_re = jnp.cos(chirp)[None, :]
    chirp_im = jnp.sin(chirp)[None, :]
    scaled_re = cosine * chirp_re - sine * chirp_im
    scaled_im = cosine * chirp_im + sine * chirp_re
    fresnel_re = matmul_exact(scaled_re, cosine) + matmul_exact(scaled_im, sine)
    fresnel_im = matmul_exact(scaled_im, cosine) - matmul_exact(scaled_re, sine)
    fresnel = jnp.stack((fresnel_re, fresnel_im)) / width
    far_field = jnp.stack((cosine, -sine)) / math.sqrt(width)
    return (fresnel, far_field)


def adjoint_of(matrix):
    return jnp.stack((matrix[0].T, -matrix[1].T))


def left_product(matrix, waves, mode):
    return jnp.einsum(
        "ij,bjk->bik", matrix, waves, precision=mode, preferred_element_type=jnp.float32
    )


def right_product(waves, matrix, mode):
    return jnp.einsum(
        "bij,kj->bik", waves, matrix, precision=mode, preferred_element_type=jnp.float32
    )


def propagate(matrix, waves, mode):
    width = matrix.shape[1]
    tall = matrix.reshape(2 * width, width)
    batch = waves.shape[1]
    both = left_product(tall, waves.reshape((2 * batch,) + waves.shape[2:]), mode)
    from_real = both[:batch]
    from_imag = both[batch:]
    inner_re = from_real[:, :width] - from_imag[:, width:]
    inner_im = from_real[:, width:] + from_imag[:, :width]
    right = right_product(jnp.concatenate((inner_re, inner_im)), tall, mode)
    right_re = right[:batch]
    right_im = right[batch:]
    outer_re = right_re[:, :, :width] - right_im[:, :, width:]
    outer_im = right_re[:, :, width:] + right_im[:, :, :width]
    return jnp.stack((outer_re, outer_im))


def forward_layers(wave, slab, matrices):
    moved_list = []
    for layer in range(slab.shape[1]):
        trans_re = slab[0, layer]
        trans_im = slab[1, layer]
        moved = jnp.stack(
            (trans_re * wave[0] - trans_im * wave[1], trans_re * wave[1] + trans_im * wave[0])
        )
        moved_list.append(moved)
        wave = propagate(matrices[layer], moved, exact_mode)
    return (wave, jnp.stack(moved_list, axis=1))


def backward_layers(grad, slab, moved, adjoints):
    layers = slab.shape[1]
    phase_parts = [None] * layers
    absorb_parts = [None] * layers
    for layer in reversed(range(layers)):
        grad_moved = propagate(adjoints[layer], grad, wave_mode)
        moved_re = moved[0, layer]
        moved_im = moved[1, layer]
        phase_parts[layer] = grad_moved[1] * moved_re - grad_moved[0] * moved_im
        absorb_parts[layer] = -(grad_moved[0] * moved_re + grad_moved[1] * moved_im)
        trans_re = slab[0, layer]
        trans_im = slab[1, layer]
        grad = jnp.stack(
            (
                trans_re * grad_moved[0] + trans_im * grad_moved[1],
                trans_re * grad_moved[1] - trans_im * grad_moved[0],
            )
        )
    return (grad, jnp.stack(phase_parts), jnp.stack(absorb_parts))


def pass_rows_all(strip, steps):
    return from_behind(strip, "row", steps)


def pass_cols_all(strip, steps):
    return from_behind(strip, "col", steps)


def fold_rows(grid, rim, mover):
    inner = grid.shape[2] - 2 * rim
    from_above = mover(grid[:, :, inner + rim :], 1)
    from_below = mover(grid[:, :, :rim], -1)
    core = grid[:, :, rim : rim + inner]
    core = core.at[:, :, :rim].add(from_above)
    return core.at[:, :, inner - rim :].add(from_below)


def fold_cols(grid, rim, mover):
    inner = grid.shape[3] - 2 * rim
    from_left = mover(grid[:, :, :, inner + rim :], 1)
    from_right = mover(grid[:, :, :, :rim], -1)
    core = grid[:, :, :, rim : rim + inner]
    core = core.at[:, :, :, :rim].add(from_left)
    return core.at[:, :, :, inner - rim :].add(from_right)


def fold_both(grid, rim, row_mover, col_mover):
    return fold_rows(fold_cols(grid, rim, col_mover), rim, row_mover)


def to_transmit(extended):
    damping = jnp.exp(-extended[1])
    return jnp.stack((damping * jnp.cos(extended[0]), damping * jnp.sin(extended[0])))


def place(patch, row, col, frame):
    height, span = frame
    extra_rows = height - patch.shape[-2]
    extra_cols = span - patch.shape[-1]
    padded = jnp.pad(patch, ((0, 0), (0, 0), (extra_rows, extra_rows), (extra_cols, extra_cols)))
    anchor = jnp.zeros((), jnp.int32)
    start = (anchor, anchor, extra_rows - row, extra_cols - col)
    return lax.dynamic_slice(padded, start, patch.shape[:2] + (height, span))


def per_device(phase, absorption, probe, measured, offsets):
    layers, tile_rows, tile_cols = phase.shape
    width = probe.shape[1]
    rim = width // 2
    probes = offsets.shape[2]
    depth_count = lax.axis_size("depth")
    depth_index = lax.axis_index("depth")
    row_index = lax.axis_index("row")
    col_index = lax.axis_index("col")
    stacked = to_transmit(jnp.stack((phase, absorption)))
    tall_slab = with_halo(stacked, (("row", 2),), rim)
    after = (stacked[0, 0, 0, 0] * 0.0).astype(jnp.int32)
    corners = offsets[0, 0] + after
    row_starts = corners[:, 0] - row_index * tile_rows + rim
    col_starts = corners[:, 1] - col_index * tile_cols + rim
    row_starts = [jnp.clip(row_starts[k], 0, 2 * rim + tile_rows - width) for k in range(probes)]
    col_starts = [jnp.clip(col_starts[k], 0, 2 * rim + tile_cols - width) for k in range(probes)]
    share = probes // depth_count
    source_rows = []
    source_cols = []
    for shift in range(depth_count):
        source = (depth_index - shift) % depth_count
        source_rows.append([lax.select_n(source * share + slot, *row_starts) for slot in range(share)])
        source_cols.append([lax.select_n(source * share + slot, *col_starts) for slot in range(share)])
    row_starts, col_starts, source_rows, source_cols, tall_slab = lax.optimization_barrier(
        (row_starts, col_starts, source_rows, source_cols, tall_slab)
    )
    extended = with_halo(tall_slab, (("col", 3),), rim)
    anchor = jnp.zeros((), jnp.int32)
    fresnel, far_field = build_tables(width)
    share = probes // depth_count
    first = depth_index * share
    cut = jnp.stack(
        [
            lax.dynamic_slice(
                extended, (anchor, anchor, row_starts[k], col_starts[k]), (2, layers, width, width)
            )
            for k in range(probes)
        ],
        axis=2,
    )
    gathered = lax.all_to_all(cut, "depth", 2, 1, tiled=True)
    windows = gathered
    total_layers = windows.shape[1]
    matrices = [fresnel] * (total_layers - 1) + [far_field]
    adjoints = [adjoint_of(matrix) for matrix in matrices]
    start_wave = probe[:, None]
    far_wave, moved = forward_layers(start_wave, windows, matrices)
    target = lax.dynamic_slice_in_dim(measured[0, 0], first, share)
    power = far_wave[0] ** 2 + far_wave[1] ** 2
    detector = far_wave * (0.25 * (power - target))[None]
    unused, phase_grad, absorb_grad = backward_layers(detector, windows, moved, adjoints)
    parts = jnp.stack((phase_grad, absorb_grad))
    grid = jnp.zeros((2, layers) + extended.shape[2:], jnp.float32)
    for shift in range(depth_count):
        chunk = lax.dynamic_slice_in_dim(
            parts, ((depth_index + shift) % depth_count) * layers, layers, axis=1
        )
        if shift > 0:
            pairs = [(i, (i + shift) % depth_count) for i in range(depth_count)]
            chunk = lax.ppermute(chunk, "depth", pairs)
        for slot in range(share):
            grid = grid + place(
                chunk[:, :, slot], source_rows[shift][slot], source_cols[shift][slot], extended.shape[2:]
            )
        grid = lax.optimization_barrier(grid)
    owned = fold_both(grid, rim, pass_rows_all, pass_cols_all)
    return (owned[0], owned[1])


def solution(mesh):
    return jax.shard_map(
        per_device,
        mesh=mesh,
        in_specs=(
            P("depth", "row", "col"),
            P("depth", "row", "col"),
            P(),
            P("row", "col", None, None, None),
            P("row", "col", None, None),
        ),
        out_specs=(P("depth", "row", "col"), P("depth", "row", "col")),
        check_vma=False,
    )
```

```python
import math

import jax
import jax.numpy as jnp
from jax import lax
from jax.sharding import PartitionSpec as P

exact_mode = lax.Precision.HIGHEST
wave_mode = lax.Precision.HIGH


def from_behind(value, axis, steps):
    count = lax.axis_size(axis)
    leading, last = (max(0, -steps), min(count, count - steps))
    return lax.ppermute(value, axis, [(source, source + steps) for source in range(leading, last)])


def outside_filled(strip, edge):
    return jnp.stack((jnp.where(edge, 1.0, strip[0]), jnp.where(edge, 0.0, strip[1])))


def with_halo(block, sides, width, strips=None):
    for axis, dim in sides:
        count = lax.axis_size(axis)
        index = lax.axis_index(axis)
        forward = [(i, i + 1) for i in range(count - 1)]
        backward = [(target, source) for source, target in forward]
        if strips is None:
            last = lax.slice_in_dim(block, block.shape[dim] - width, None, axis=dim)
            head = lax.slice_in_dim(block, 0, width, axis=dim)
        else:
            head, last = strips
        low = lax.ppermute(last, axis, forward)
        high = lax.ppermute(head, axis, backward)
        low = outside_filled(low, index == 0)
        high = outside_filled(high, index == count - 1)
        block = jnp.concatenate([low, block, high], axis=dim)
    return block


def matmul_exact(first, second):
    return jnp.dot(first, second, precision=exact_mode, preferred_element_type=jnp.float32)


def build_tables(width):
    index = jnp.arange(width, dtype=jnp.int32)
    product = index[:, None] * index[None, :] % width
    angle = product.astype(jnp.float32) * (2.0 * math.pi / width)
    cosine = jnp.cos(angle)
    sine = jnp.sin(angle)
    signed = jnp.where(index < width // 2, index, index - width)
    chirp = -(signed * signed % (4 * width)).astype(jnp.float32) * (2.0 * math.pi / (4 * width))
    chirp_re = jnp.cos(chirp)[None, :]
    chirp_im = jnp.sin(chirp)[None, :]
    scaled_re = cosine * chirp_re - sine * chirp_im
    scaled_im = cosine * chirp_im + sine * chirp_re
    fresnel_re = matmul_exact(scaled_re, cosine) + matmul_exact(scaled_im, sine)
    fresnel_im = matmul_exact(scaled_im, cosine) - matmul_exact(scaled_re, sine)
    fresnel = jnp.stack((fresnel_re, fresnel_im)) / width
    far_field = jnp.stack((cosine, -sine)) / math.sqrt(width)
    return (fresnel, far_field)


def adjoint_of(matrix):
    return jnp.stack((matrix[0].T, -matrix[1].T))


def left_product(matrix, waves, mode):
    return jnp.einsum(
        "ij,bjk->bik", matrix, waves, precision=mode, preferred_element_type=jnp.float32
    )


def right_product(waves, matrix, mode):
    return jnp.einsum(
        "bij,kj->bik", waves, matrix, precision=mode, preferred_element_type=jnp.float32
    )


def propagate(matrix, waves, mode):
    width = matrix.shape[1]
    tall = matrix.reshape(2 * width, width)
    batch = waves.shape[1]
    both = left_product(tall, waves.reshape((2 * batch,) + waves.shape[2:]), mode)
    from_real = both[:batch]
    from_imag = both[batch:]
    inner_re = from_real[:, :width] - from_imag[:, width:]
    inner_im = from_real[:, width:] + from_imag[:, :width]
    right = right_product(jnp.concatenate((inner_re, inner_im)), tall, mode)
    right_re = right[:batch]
    right_im = right[batch:]
    outer_re = right_re[:, :, :width] - right_im[:, :, width:]
    outer_im = right_re[:, :, width:] + right_im[:, :, :width]
    return jnp.stack((outer_re, outer_im))


def forward_layers(wave, slab, matrices):
    moved_list = []
    for layer in range(slab.shape[1]):
        trans_re = slab[0, layer]
        trans_im = slab[1, layer]
        moved = jnp.stack(
            (trans_re * wave[0] - trans_im * wave[1], trans_re * wave[1] + trans_im * wave[0])
        )
        moved_list.append(moved)
        wave = propagate(matrices[layer], moved, exact_mode)
    return (wave, jnp.stack(moved_list, axis=1))


def backward_layers(grad, slab, moved, adjoints):
    layers = slab.shape[1]
    phase_parts = [None] * layers
    absorb_parts = [None] * layers
    for layer in reversed(range(layers)):
        grad_moved = propagate(adjoints[layer], grad, wave_mode)
        moved_re = moved[0, layer]
        moved_im = moved[1, layer]
        phase_parts[layer] = grad_moved[1] * moved_re - grad_moved[0] * moved_im
        absorb_parts[layer] = -(grad_moved[0] * moved_re + grad_moved[1] * moved_im)
        trans_re = slab[0, layer]
        trans_im = slab[1, layer]
        grad = jnp.stack(
            (
                trans_re * grad_moved[0] + trans_im * grad_moved[1],
                trans_re * grad_moved[1] - trans_im * grad_moved[0],
            )
        )
    return (grad, jnp.stack(phase_parts), jnp.stack(absorb_parts))


def pass_rows_all(strip, steps):
    return from_behind(strip, "row", steps)


def pass_cols_all(strip, steps):
    return from_behind(strip, "col", steps)


def fold_rows(grid, rim, mover):
    inner = grid.shape[2] - 2 * rim
    from_above = mover(grid[:, :, inner + rim :], 1)
    from_below = mover(grid[:, :, :rim], -1)
    core = grid[:, :, rim : rim + inner]
    core = core.at[:, :, :rim].add(from_above)
    return core.at[:, :, inner - rim :].add(from_below)


def fold_cols(grid, rim, mover):
    inner = grid.shape[3] - 2 * rim
    from_left = mover(grid[:, :, :, inner + rim :], 1)
    from_right = mover(grid[:, :, :, :rim], -1)
    core = grid[:, :, :, rim : rim + inner]
    core = core.at[:, :, :, :rim].add(from_left)
    return core.at[:, :, :, inner - rim :].add(from_right)


def fold_both(grid, rim, row_mover, col_mover):
    return fold_rows(fold_cols(grid, rim, col_mover), rim, row_mover)


def to_transmit(extended):
    damping = jnp.exp(-extended[1])
    return jnp.stack((damping * jnp.cos(extended[0]), damping * jnp.sin(extended[0])))


def place(patch, row, col, frame):
    height, span = frame
    extra_rows = height - patch.shape[-2]
    extra_cols = span - patch.shape[-1]
    padded = jnp.pad(patch, ((0, 0), (0, 0), (extra_rows, extra_rows), (extra_cols, extra_cols)))
    anchor = jnp.zeros((), jnp.int32)
    start = (anchor, anchor, extra_rows - row, extra_cols - col)
    return lax.dynamic_slice(padded, start, patch.shape[:2] + (height, span))


def per_device(phase, absorption, probe, measured, offsets):
    layers, tile_rows, tile_cols = phase.shape
    width = probe.shape[1]
    rim = width // 2
    probes = offsets.shape[2]
    depth_count = lax.axis_size("depth")
    depth_index = lax.axis_index("depth")
    row_index = lax.axis_index("row")
    col_index = lax.axis_index("col")
    raw = jnp.stack((phase, absorption))
    edges = lax.optimization_barrier(
        (to_transmit(raw[:, :, :rim]), to_transmit(raw[:, :, tile_rows - rim :]))
    )
    stacked = to_transmit(raw)
    tall_slab = with_halo(stacked, (("row", 2),), rim, strips=edges)
    after = (stacked[0, 0, 0, 0] * 0.0).astype(jnp.int32)
    corners = offsets[0, 0] + after
    row_starts = corners[:, 0] - row_index * tile_rows + rim
    col_starts = corners[:, 1] - col_index * tile_cols + rim
    row_starts = [jnp.clip(row_starts[k], 0, 2 * rim + tile_rows - width) for k in range(probes)]
    col_starts = [jnp.clip(col_starts[k], 0, 2 * rim + tile_cols - width) for k in range(probes)]
    share = probes // depth_count
    source_rows = []
    source_cols = []
    for shift in range(depth_count):
        source = (depth_index - shift) % depth_count
        source_rows.append([lax.select_n(source * share + slot, *row_starts) for slot in range(share)])
        source_cols.append([lax.select_n(source * share + slot, *col_starts) for slot in range(share)])
    row_starts, col_starts, source_rows, source_cols, tall_slab = lax.optimization_barrier(
        (row_starts, col_starts, source_rows, source_cols, tall_slab)
    )
    extended = with_halo(tall_slab, (("col", 3),), rim)
    anchor = jnp.zeros((), jnp.int32)
    fresnel, far_field = build_tables(width)
    share = probes // depth_count
    first = depth_index * share
    cut = jnp.stack(
        [
            lax.dynamic_slice(
                extended, (anchor, anchor, row_starts[k], col_starts[k]), (2, layers, width, width)
            )
            for k in range(probes)
        ],
        axis=2,
    )
    gathered = lax.all_to_all(cut, "depth", 2, 1, tiled=True)
    windows = gathered
    total_layers = windows.shape[1]
    matrices = [fresnel] * (total_layers - 1) + [far_field]
    adjoints = [adjoint_of(matrix) for matrix in matrices]
    start_wave = probe[:, None]
    far_wave, moved = forward_layers(start_wave, windows, matrices)
    target = lax.dynamic_slice_in_dim(measured[0, 0], first, share)
    power = far_wave[0] ** 2 + far_wave[1] ** 2
    detector = far_wave * (0.25 * (power - target))[None]
    unused, phase_grad, absorb_grad = backward_layers(detector, windows, moved, adjoints)
    parts = jnp.stack((phase_grad, absorb_grad))
    grid = jnp.zeros((2, layers) + extended.shape[2:], jnp.float32)
    for shift in range(depth_count):
        chunk = lax.dynamic_slice_in_dim(
            parts, ((depth_index + shift) % depth_count) * layers, layers, axis=1
        )
        if shift > 0:
            pairs = [(i, (i + shift) % depth_count) for i in range(depth_count)]
            chunk = lax.ppermute(chunk, "depth", pairs)
        for slot in range(share):
            grid = grid + place(
                chunk[:, :, slot], source_rows[shift][slot], source_cols[shift][slot], extended.shape[2:]
            )
        grid = lax.optimization_barrier(grid)
    owned = fold_both(grid, rim, pass_rows_all, pass_cols_all)
    return (owned[0], owned[1])


def solution(mesh):
    return jax.shard_map(
        per_device,
        mesh=mesh,
        in_specs=(
            P("depth", "row", "col"),
            P("depth", "row", "col"),
            P(),
            P("row", "col", None, None, None),
            P("row", "col", None, None),
        ),
        out_specs=(P("depth", "row", "col"), P("depth", "row", "col")),
        check_vma=False,
    )
```

```python
import math

import jax
import jax.numpy as jnp
from jax import lax
from jax.sharding import PartitionSpec as P

exact_mode = lax.Precision.HIGHEST
wave_mode = lax.Precision.HIGH


def from_behind(value, axis, steps):
    count = lax.axis_size(axis)
    leading, last = (max(0, -steps), min(count, count - steps))
    return lax.ppermute(value, axis, [(source, source + steps) for source in range(leading, last)])


def outside_filled(strip, edge):
    return jnp.stack((jnp.where(edge, 1.0, strip[0]), jnp.where(edge, 0.0, strip[1])))


def with_halo(block, sides, width):
    for axis, dim in sides:
        count = lax.axis_size(axis)
        index = lax.axis_index(axis)
        forward = [(i, i + 1) for i in range(count - 1)]
        backward = [(target, source) for source, target in forward]
        low = lax.ppermute(
            lax.slice_in_dim(block, block.shape[dim] - width, None, axis=dim), axis, forward
        )
        high = lax.ppermute(lax.slice_in_dim(block, 0, width, axis=dim), axis, backward)
        low = outside_filled(low, index == 0)
        high = outside_filled(high, index == count - 1)
        block = jnp.concatenate([low, block, high], axis=dim)
    return block


def matmul_exact(first, second):
    return jnp.dot(first, second, precision=exact_mode, preferred_element_type=jnp.float32)


def build_tables(width):
    index = jnp.arange(width, dtype=jnp.int32)
    product = index[:, None] * index[None, :] % width
    angle = product.astype(jnp.float32) * (2.0 * math.pi / width)
    cosine = jnp.cos(angle)
    sine = jnp.sin(angle)
    signed = jnp.where(index < width // 2, index, index - width)
    chirp = -(signed * signed % (4 * width)).astype(jnp.float32) * (2.0 * math.pi / (4 * width))
    chirp_re = jnp.cos(chirp)[None, :]
    chirp_im = jnp.sin(chirp)[None, :]
    scaled_re = cosine * chirp_re - sine * chirp_im
    scaled_im = cosine * chirp_im + sine * chirp_re
    fresnel_re = matmul_exact(scaled_re, cosine) + matmul_exact(scaled_im, sine)
    fresnel_im = matmul_exact(scaled_im, cosine) - matmul_exact(scaled_re, sine)
    fresnel = jnp.stack((fresnel_re, fresnel_im)) / width
    far_field = jnp.stack((cosine, -sine)) / math.sqrt(width)
    return (fresnel, far_field)


def adjoint_of(matrix):
    return jnp.stack((matrix[0].T, -matrix[1].T))


def left_product(matrix, waves, mode):
    return jnp.einsum(
        "ij,bjk->bik", matrix, waves, precision=mode, preferred_element_type=jnp.float32
    )


def right_product(waves, matrix, mode):
    return jnp.einsum(
        "bij,kj->bik", waves, matrix, precision=mode, preferred_element_type=jnp.float32
    )


def propagate(matrix, waves, mode):
    width = matrix.shape[1]
    tall = matrix.reshape(2 * width, width)
    batch = waves.shape[1]
    both = left_product(tall, waves.reshape((2 * batch,) + waves.shape[2:]), mode)
    from_real = both[:batch]
    from_imag = both[batch:]
    inner_re = from_real[:, :width] - from_imag[:, width:]
    inner_im = from_real[:, width:] + from_imag[:, :width]
    right = right_product(jnp.concatenate((inner_re, inner_im)), tall, mode)
    right_re = right[:batch]
    right_im = right[batch:]
    outer_re = right_re[:, :, :width] - right_im[:, :, width:]
    outer_im = right_re[:, :, width:] + right_im[:, :, :width]
    return jnp.stack((outer_re, outer_im))


def forward_layers(wave, slab, matrices):
    moved_list = []
    for layer in range(slab.shape[1]):
        trans_re = slab[0, layer]
        trans_im = slab[1, layer]
        moved = jnp.stack(
            (trans_re * wave[0] - trans_im * wave[1], trans_re * wave[1] + trans_im * wave[0])
        )
        moved_list.append(moved)
        wave = propagate(matrices[layer], moved, exact_mode)
    return (wave, jnp.stack(moved_list, axis=1))


def backward_layers(grad, slab, moved, adjoints):
    layers = slab.shape[1]
    phase_parts = [None] * layers
    absorb_parts = [None] * layers
    for layer in reversed(range(layers)):
        grad_moved = propagate(adjoints[layer], grad, wave_mode)
        moved_re = moved[0, layer]
        moved_im = moved[1, layer]
        phase_parts[layer] = grad_moved[1] * moved_re - grad_moved[0] * moved_im
        absorb_parts[layer] = -(grad_moved[0] * moved_re + grad_moved[1] * moved_im)
        trans_re = slab[0, layer]
        trans_im = slab[1, layer]
        grad = jnp.stack(
            (
                trans_re * grad_moved[0] + trans_im * grad_moved[1],
                trans_re * grad_moved[1] - trans_im * grad_moved[0],
            )
        )
    return (grad, jnp.stack(phase_parts), jnp.stack(absorb_parts))


def pass_rows_all(strip, steps):
    return from_behind(strip, "row", steps)


def pass_cols_all(strip, steps):
    return from_behind(strip, "col", steps)


def fold_rows(grid, rim, mover):
    inner = grid.shape[2] - 2 * rim
    from_above = mover(grid[:, :, inner + rim :], 1)
    from_below = mover(grid[:, :, :rim], -1)
    core = grid[:, :, rim : rim + inner]
    core = core.at[:, :, :rim].add(from_above)
    return core.at[:, :, inner - rim :].add(from_below)


def fold_cols(grid, rim, mover):
    inner = grid.shape[3] - 2 * rim
    from_left = mover(grid[:, :, :, inner + rim :], 1)
    from_right = mover(grid[:, :, :, :rim], -1)
    core = grid[:, :, :, rim : rim + inner]
    core = core.at[:, :, :, :rim].add(from_left)
    return core.at[:, :, :, inner - rim :].add(from_right)


def fold_both(grid, rim, row_mover, col_mover):
    return fold_rows(fold_cols(grid, rim, col_mover), rim, row_mover)


def to_transmit(extended):
    damping = jnp.exp(-extended[1])
    return jnp.stack((damping * jnp.cos(extended[0]), damping * jnp.sin(extended[0])))


def place(patch, row, col, frame):
    height, span = frame
    extra_rows = height - patch.shape[-2]
    extra_cols = span - patch.shape[-1]
    padded = jnp.pad(patch, ((0, 0), (0, 0), (extra_rows, extra_rows), (extra_cols, extra_cols)))
    anchor = jnp.zeros((), jnp.int32)
    start = (anchor, anchor, extra_rows - row, extra_cols - col)
    return lax.dynamic_slice(padded, start, patch.shape[:2] + (height, span))


def issue_order(count):
    half = count // 2
    rest = [shift for shift in range(1, count) if shift != half]
    return [0, half] + rest if count % 2 == 0 and half > 0 else list(range(count))


def per_device(phase, absorption, probe, measured, offsets):
    layers, tile_rows, tile_cols = phase.shape
    width = probe.shape[1]
    rim = width // 2
    probes = offsets.shape[2]
    depth_count = lax.axis_size("depth")
    depth_index = lax.axis_index("depth")
    row_index = lax.axis_index("row")
    col_index = lax.axis_index("col")
    stacked = to_transmit(jnp.stack((phase, absorption)))
    tall_slab = with_halo(stacked, (("row", 2),), rim)
    after = (stacked[0, 0, 0, 0] * 0.0).astype(jnp.int32)
    corners = offsets[0, 0] + after
    row_starts = corners[:, 0] - row_index * tile_rows + rim
    col_starts = corners[:, 1] - col_index * tile_cols + rim
    row_starts = [jnp.clip(row_starts[k], 0, 2 * rim + tile_rows - width) for k in range(probes)]
    col_starts = [jnp.clip(col_starts[k], 0, 2 * rim + tile_cols - width) for k in range(probes)]
    share = probes // depth_count
    source_rows = []
    source_cols = []
    for shift in range(depth_count):
        source = (depth_index - shift) % depth_count
        source_rows.append([lax.select_n(source * share + slot, *row_starts) for slot in range(share)])
        source_cols.append([lax.select_n(source * share + slot, *col_starts) for slot in range(share)])
    row_starts, col_starts, source_rows, source_cols, tall_slab = lax.optimization_barrier(
        (row_starts, col_starts, source_rows, source_cols, tall_slab)
    )
    extended = with_halo(tall_slab, (("col", 3),), rim)
    anchor = jnp.zeros((), jnp.int32)
    fresnel, far_field = build_tables(width)
    share = probes // depth_count
    first = depth_index * share
    cut = jnp.stack(
        [
            lax.dynamic_slice(
                extended, (anchor, anchor, row_starts[k], col_starts[k]), (2, layers, width, width)
            )
            for k in range(probes)
        ],
        axis=2,
    )
    gathered = lax.all_to_all(cut, "depth", 2, 1, tiled=True)
    windows = gathered
    total_layers = windows.shape[1]
    matrices = [fresnel] * (total_layers - 1) + [far_field]
    adjoints = [adjoint_of(matrix) for matrix in matrices]
    start_wave = probe[:, None]
    far_wave, moved = forward_layers(start_wave, windows, matrices)
    target = lax.dynamic_slice_in_dim(measured[0, 0], first, share)
    power = far_wave[0] ** 2 + far_wave[1] ** 2
    detector = far_wave * (0.25 * (power - target))[None]
    unused, phase_grad, absorb_grad = backward_layers(detector, windows, moved, adjoints)
    parts = jnp.stack((phase_grad, absorb_grad))
    grid = jnp.zeros((2, layers) + extended.shape[2:], jnp.float32)
    for shift in issue_order(depth_count):
        chunk = lax.dynamic_slice_in_dim(
            parts, ((depth_index + shift) % depth_count) * layers, layers, axis=1
        )
        if shift > 0:
            pairs = [(i, (i + shift) % depth_count) for i in range(depth_count)]
            chunk = lax.ppermute(chunk, "depth", pairs)
        for slot in range(share):
            grid = grid + place(
                chunk[:, :, slot], source_rows[shift][slot], source_cols[shift][slot], extended.shape[2:]
            )
        grid = lax.optimization_barrier(grid)
    owned = fold_both(grid, rim, pass_rows_all, pass_cols_all)
    return (owned[0], owned[1])


def solution(mesh):
    return jax.shard_map(
        per_device,
        mesh=mesh,
        in_specs=(
            P("depth", "row", "col"),
            P("depth", "row", "col"),
            P(),
            P("row", "col", None, None, None),
            P("row", "col", None, None),
        ),
        out_specs=(P("depth", "row", "col"), P("depth", "row", "col")),
        check_vma=False,
    )
```

```python
import math

import jax
import jax.numpy as jnp
from jax import lax
from jax.sharding import PartitionSpec as P

exact_mode = lax.Precision.HIGHEST
wave_mode = lax.Precision.HIGH


def from_behind(value, axis, steps):
    count = lax.axis_size(axis)
    leading, last = (max(0, -steps), min(count, count - steps))
    return lax.ppermute(value, axis, [(source, source + steps) for source in range(leading, last)])


def outside_filled(strip, edge):
    return jnp.stack((jnp.where(edge, 1.0, strip[0]), jnp.where(edge, 0.0, strip[1])))


def with_halo(block, sides, width):
    for axis, dim in sides:
        count = lax.axis_size(axis)
        index = lax.axis_index(axis)
        forward = [(i, i + 1) for i in range(count - 1)]
        backward = [(target, source) for source, target in forward]
        low = lax.ppermute(
            lax.slice_in_dim(block, block.shape[dim] - width, None, axis=dim), axis, forward
        )
        high = lax.ppermute(lax.slice_in_dim(block, 0, width, axis=dim), axis, backward)
        low = outside_filled(low, index == 0)
        high = outside_filled(high, index == count - 1)
        block = jnp.concatenate([low, block, high], axis=dim)
    return block


def matmul_exact(first, second):
    return jnp.dot(first, second, precision=exact_mode, preferred_element_type=jnp.float32)


def build_tables(width):
    index = jnp.arange(width, dtype=jnp.int32)
    product = index[:, None] * index[None, :] % width
    angle = product.astype(jnp.float32) * (2.0 * math.pi / width)
    cosine = jnp.cos(angle)
    sine = jnp.sin(angle)
    signed = jnp.where(index < width // 2, index, index - width)
    chirp = -(signed * signed % (4 * width)).astype(jnp.float32) * (2.0 * math.pi / (4 * width))
    chirp_re = jnp.cos(chirp)[None, :]
    chirp_im = jnp.sin(chirp)[None, :]
    scaled_re = cosine * chirp_re - sine * chirp_im
    scaled_im = cosine * chirp_im + sine * chirp_re
    fresnel_re = matmul_exact(scaled_re, cosine) + matmul_exact(scaled_im, sine)
    fresnel_im = matmul_exact(scaled_im, cosine) - matmul_exact(scaled_re, sine)
    fresnel = jnp.stack((fresnel_re, fresnel_im)) / width
    far_field = jnp.stack((cosine, -sine)) / math.sqrt(width)
    return (fresnel, far_field)


def adjoint_of(matrix):
    return jnp.stack((matrix[0].T, -matrix[1].T))


def left_product(matrix, waves, mode):
    return jnp.einsum(
        "ij,bjk->bik", matrix, waves, precision=mode, preferred_element_type=jnp.float32
    )


def right_product(waves, matrix, mode):
    return jnp.einsum(
        "bij,kj->bik", waves, matrix, precision=mode, preferred_element_type=jnp.float32
    )


def propagate(matrix, waves, mode):
    width = matrix.shape[1]
    tall = matrix.reshape(2 * width, width)
    batch = waves.shape[1]
    both = left_product(tall, waves.reshape((2 * batch,) + waves.shape[2:]), mode)
    from_real = both[:batch]
    from_imag = both[batch:]
    inner_re = from_real[:, :width] - from_imag[:, width:]
    inner_im = from_real[:, width:] + from_imag[:, :width]
    right = right_product(jnp.concatenate((inner_re, inner_im)), tall, mode)
    right_re = right[:batch]
    right_im = right[batch:]
    outer_re = right_re[:, :, :width] - right_im[:, :, width:]
    outer_im = right_re[:, :, width:] + right_im[:, :, :width]
    return jnp.stack((outer_re, outer_im))


def forward_layers(wave, slab, matrices):
    moved_list = []
    for layer in range(len(slab)):
        trans_re = slab[layer][0]
        trans_im = slab[layer][1]
        moved = jnp.stack(
            (trans_re * wave[0] - trans_im * wave[1], trans_re * wave[1] + trans_im * wave[0])
        )
        moved_list.append(moved)
        wave = propagate(matrices[layer], moved, exact_mode)
    return (wave, jnp.stack(moved_list, axis=1))


def backward_layers(grad, slab, moved, adjoints):
    layers = len(slab)
    phase_parts = [None] * layers
    absorb_parts = [None] * layers
    for layer in reversed(range(layers)):
        grad_moved = propagate(adjoints[layer], grad, wave_mode)
        moved_re = moved[0, layer]
        moved_im = moved[1, layer]
        phase_parts[layer] = grad_moved[1] * moved_re - grad_moved[0] * moved_im
        absorb_parts[layer] = -(grad_moved[0] * moved_re + grad_moved[1] * moved_im)
        trans_re = slab[layer][0]
        trans_im = slab[layer][1]
        grad = jnp.stack(
            (
                trans_re * grad_moved[0] + trans_im * grad_moved[1],
                trans_re * grad_moved[1] - trans_im * grad_moved[0],
            )
        )
    return (grad, jnp.stack(phase_parts), jnp.stack(absorb_parts))


def pass_rows_all(strip, steps):
    return from_behind(strip, "row", steps)


def pass_cols_all(strip, steps):
    return from_behind(strip, "col", steps)


def fold_rows(grid, rim, mover):
    inner = grid.shape[2] - 2 * rim
    from_above = mover(grid[:, :, inner + rim :], 1)
    from_below = mover(grid[:, :, :rim], -1)
    core = grid[:, :, rim : rim + inner]
    core = core.at[:, :, :rim].add(from_above)
    return core.at[:, :, inner - rim :].add(from_below)


def fold_cols(grid, rim, mover):
    inner = grid.shape[3] - 2 * rim
    from_left = mover(grid[:, :, :, inner + rim :], 1)
    from_right = mover(grid[:, :, :, :rim], -1)
    core = grid[:, :, :, rim : rim + inner]
    core = core.at[:, :, :, :rim].add(from_left)
    return core.at[:, :, :, inner - rim :].add(from_right)


def fold_both(grid, rim, row_mover, col_mover):
    return fold_rows(fold_cols(grid, rim, col_mover), rim, row_mover)


def to_transmit(extended):
    damping = jnp.exp(-extended[1])
    return jnp.stack((damping * jnp.cos(extended[0]), damping * jnp.sin(extended[0])))


def place(patch, row, col, frame):
    height, span = frame
    extra_rows = height - patch.shape[-2]
    extra_cols = span - patch.shape[-1]
    padded = jnp.pad(patch, ((0, 0), (0, 0), (extra_rows, extra_rows), (extra_cols, extra_cols)))
    anchor = jnp.zeros((), jnp.int32)
    start = (anchor, anchor, extra_rows - row, extra_cols - col)
    return lax.dynamic_slice(padded, start, patch.shape[:2] + (height, span))


def issue_order(count):
    half = count // 2
    rest = [shift for shift in range(1, count) if shift != half]
    return [0, half] + rest if count % 2 == 0 and half > 0 else list(range(count))


def per_device(phase, absorption, probe, measured, offsets):
    layers, tile_rows, tile_cols = phase.shape
    width = probe.shape[1]
    rim = width // 2
    probes = offsets.shape[2]
    depth_count = lax.axis_size("depth")
    depth_index = lax.axis_index("depth")
    row_index = lax.axis_index("row")
    col_index = lax.axis_index("col")
    stacked = to_transmit(jnp.stack((phase, absorption)))
    tall_slab = with_halo(stacked, (("row", 2),), rim)
    after = (stacked[0, 0, 0, 0] * 0.0).astype(jnp.int32)
    corners = offsets[0, 0] + after
    row_starts = corners[:, 0] - row_index * tile_rows + rim
    col_starts = corners[:, 1] - col_index * tile_cols + rim
    row_starts = [jnp.clip(row_starts[k], 0, 2 * rim + tile_rows - width) for k in range(probes)]
    col_starts = [jnp.clip(col_starts[k], 0, 2 * rim + tile_cols - width) for k in range(probes)]
    share = probes // depth_count
    source_rows = []
    source_cols = []
    for shift in range(depth_count):
        source = (depth_index - shift) % depth_count
        source_rows.append([lax.select_n(source * share + slot, *row_starts) for slot in range(share)])
        source_cols.append([lax.select_n(source * share + slot, *col_starts) for slot in range(share)])
    row_starts, col_starts, source_rows, source_cols, tall_slab = lax.optimization_barrier(
        (row_starts, col_starts, source_rows, source_cols, tall_slab)
    )
    extended = with_halo(tall_slab, (("col", 3),), rim)
    anchor = jnp.zeros((), jnp.int32)
    fresnel, far_field = build_tables(width)
    share = probes // depth_count
    first = depth_index * share
    cut = jnp.stack(
        [
            lax.dynamic_slice(
                extended, (anchor, anchor, row_starts[k], col_starts[k]), (2, layers, width, width)
            )
            for k in range(probes)
        ],
        axis=2,
    )
    pieces = []
    for shift in range(depth_count):
        chunk = lax.dynamic_slice_in_dim(
            cut, ((depth_index + shift) % depth_count) * share, share, axis=2
        )
        if shift > 0:
            pairs = [(i, (i + shift) % depth_count) for i in range(depth_count)]
            chunk = lax.ppermute(chunk, "depth", pairs)
        pieces.append(chunk)
    windows = []
    for group in range(depth_count):
        which = (depth_index - group) % depth_count
        for layer in range(layers):
            windows.append(lax.select_n(which, *[piece[:, layer] for piece in pieces]))
    total_layers = len(windows)
    matrices = [fresnel] * (total_layers - 1) + [far_field]
    adjoints = [adjoint_of(matrix) for matrix in matrices]
    start_wave = probe[:, None]
    far_wave, moved = forward_layers(start_wave, windows, matrices)
    target = lax.dynamic_slice_in_dim(measured[0, 0], first, share)
    power = far_wave[0] ** 2 + far_wave[1] ** 2
    detector = far_wave * (0.25 * (power - target))[None]
    unused, phase_grad, absorb_grad = backward_layers(detector, windows, moved, adjoints)
    parts = jnp.stack((phase_grad, absorb_grad))
    grid = jnp.zeros((2, layers) + extended.shape[2:], jnp.float32)
    for shift in issue_order(depth_count):
        chunk = lax.dynamic_slice_in_dim(
            parts, ((depth_index + shift) % depth_count) * layers, layers, axis=1
        )
        if shift > 0:
            pairs = [(i, (i + shift) % depth_count) for i in range(depth_count)]
            chunk = lax.ppermute(chunk, "depth", pairs)
        for slot in range(share):
            grid = grid + place(
                chunk[:, :, slot], source_rows[shift][slot], source_cols[shift][slot], extended.shape[2:]
            )
        grid = lax.optimization_barrier(grid)
    owned = fold_both(grid, rim, pass_rows_all, pass_cols_all)
    return (owned[0], owned[1])


def solution(mesh):
    return jax.shard_map(
        per_device,
        mesh=mesh,
        in_specs=(
            P("depth", "row", "col"),
            P("depth", "row", "col"),
            P(),
            P("row", "col", None, None, None),
            P("row", "col", None, None),
        ),
        out_specs=(P("depth", "row", "col"), P("depth", "row", "col")),
        check_vma=False,
    )
```

```python
import math

import jax
import jax.numpy as jnp
from jax import lax
from jax.sharding import PartitionSpec as P

exact_mode = lax.Precision.HIGHEST
wave_mode = lax.Precision.HIGH


def from_behind(value, axis, steps):
    count = lax.axis_size(axis)
    leading, last = (max(0, -steps), min(count, count - steps))
    return lax.ppermute(value, axis, [(source, source + steps) for source in range(leading, last)])


def outside_filled(strip, edge):
    return jnp.stack((jnp.where(edge, 1.0, strip[0]), jnp.where(edge, 0.0, strip[1])))


def with_halo(block, sides, width):
    for axis, dim in sides:
        count = lax.axis_size(axis)
        index = lax.axis_index(axis)
        forward = [(i, i + 1) for i in range(count - 1)]
        backward = [(target, source) for source, target in forward]
        low = lax.ppermute(
            lax.slice_in_dim(block, block.shape[dim] - width, None, axis=dim), axis, forward
        )
        high = lax.ppermute(lax.slice_in_dim(block, 0, width, axis=dim), axis, backward)
        low = outside_filled(low, index == 0)
        high = outside_filled(high, index == count - 1)
        block = jnp.concatenate([low, block, high], axis=dim)
    return block


def matmul_exact(first, second):
    return jnp.dot(first, second, precision=exact_mode, preferred_element_type=jnp.float32)


def build_tables(width):
    index = jnp.arange(width, dtype=jnp.int32)
    product = index[:, None] * index[None, :] % width
    angle = product.astype(jnp.float32) * (2.0 * math.pi / width)
    cosine = jnp.cos(angle)
    sine = jnp.sin(angle)
    signed = jnp.where(index < width // 2, index, index - width)
    chirp = -(signed * signed % (4 * width)).astype(jnp.float32) * (2.0 * math.pi / (4 * width))
    chirp_re = jnp.cos(chirp)[None, :]
    chirp_im = jnp.sin(chirp)[None, :]
    scaled_re = cosine * chirp_re - sine * chirp_im
    scaled_im = cosine * chirp_im + sine * chirp_re
    fresnel_re = matmul_exact(scaled_re, cosine) + matmul_exact(scaled_im, sine)
    fresnel_im = matmul_exact(scaled_im, cosine) - matmul_exact(scaled_re, sine)
    fresnel = jnp.stack((fresnel_re, fresnel_im)) / width
    far_field = jnp.stack((cosine, -sine)) / math.sqrt(width)
    return (fresnel, far_field)


def adjoint_of(matrix):
    return jnp.stack((matrix[0].T, -matrix[1].T))


def left_product(matrix, waves, mode):
    return jnp.einsum(
        "ij,bjk->bik", matrix, waves, precision=mode, preferred_element_type=jnp.float32
    )


def right_product(waves, matrix, mode):
    return jnp.einsum(
        "bij,kj->bik", waves, matrix, precision=mode, preferred_element_type=jnp.float32
    )


def propagate(matrix, waves, mode):
    width = matrix.shape[1]
    tall = matrix.reshape(2 * width, width)
    batch = waves.shape[1]
    both = left_product(tall, waves.reshape((2 * batch,) + waves.shape[2:]), mode)
    from_real = both[:batch]
    from_imag = both[batch:]
    inner_re = from_real[:, :width] - from_imag[:, width:]
    inner_im = from_real[:, width:] + from_imag[:, :width]
    right = right_product(jnp.concatenate((inner_re, inner_im)), tall, mode)
    right_re = right[:batch]
    right_im = right[batch:]
    outer_re = right_re[:, :, :width] - right_im[:, :, width:]
    outer_im = right_re[:, :, width:] + right_im[:, :, :width]
    return jnp.stack((outer_re, outer_im))


def forward_layers(wave, slab, matrices):
    moved_list = []
    for layer in range(slab.shape[1]):
        trans_re = slab[0, layer]
        trans_im = slab[1, layer]
        moved = jnp.stack(
            (trans_re * wave[0] - trans_im * wave[1], trans_re * wave[1] + trans_im * wave[0])
        )
        moved_list.append(moved)
        wave = propagate(matrices[layer], moved, exact_mode if layer == slab.shape[1] - 1 else wave_mode)
    return (wave, jnp.stack(moved_list, axis=1))


def backward_layers(grad, slab, moved, adjoints):
    layers = slab.shape[1]
    phase_parts = [None] * layers
    absorb_parts = [None] * layers
    for layer in reversed(range(layers)):
        grad_moved = propagate(adjoints[layer], grad, wave_mode)
        moved_re = moved[0, layer]
        moved_im = moved[1, layer]
        phase_parts[layer] = grad_moved[1] * moved_re - grad_moved[0] * moved_im
        absorb_parts[layer] = -(grad_moved[0] * moved_re + grad_moved[1] * moved_im)
        trans_re = slab[0, layer]
        trans_im = slab[1, layer]
        grad = jnp.stack(
            (
                trans_re * grad_moved[0] + trans_im * grad_moved[1],
                trans_re * grad_moved[1] - trans_im * grad_moved[0],
            )
        )
    return (grad, jnp.stack(phase_parts), jnp.stack(absorb_parts))


def pass_rows_all(strip, steps):
    return from_behind(strip, "row", steps)


def pass_cols_all(strip, steps):
    return from_behind(strip, "col", steps)


def fold_rows(grid, rim, mover):
    inner = grid.shape[2] - 2 * rim
    from_above = mover(grid[:, :, inner + rim :], 1)
    from_below = mover(grid[:, :, :rim], -1)
    core = grid[:, :, rim : rim + inner]
    core = core.at[:, :, :rim].add(from_above)
    return core.at[:, :, inner - rim :].add(from_below)


def fold_cols(grid, rim, mover):
    inner = grid.shape[3] - 2 * rim
    from_left = mover(grid[:, :, :, inner + rim :], 1)
    from_right = mover(grid[:, :, :, :rim], -1)
    core = grid[:, :, :, rim : rim + inner]
    core = core.at[:, :, :, :rim].add(from_left)
    return core.at[:, :, :, inner - rim :].add(from_right)


def fold_both(grid, rim, row_mover, col_mover):
    return fold_rows(fold_cols(grid, rim, col_mover), rim, row_mover)


def to_transmit(extended):
    damping = jnp.exp(-extended[1])
    return jnp.stack((damping * jnp.cos(extended[0]), damping * jnp.sin(extended[0])))


def place(patch, row, col, frame):
    height, span = frame
    extra_rows = height - patch.shape[-2]
    extra_cols = span - patch.shape[-1]
    padded = jnp.pad(patch, ((0, 0), (0, 0), (extra_rows, extra_rows), (extra_cols, extra_cols)))
    anchor = jnp.zeros((), jnp.int32)
    start = (anchor, anchor, extra_rows - row, extra_cols - col)
    return lax.dynamic_slice(padded, start, patch.shape[:2] + (height, span))


def issue_order(count):
    half = count // 2
    rest = [shift for shift in range(1, count) if shift != half]
    return [0, half] + rest if count % 2 == 0 and half > 0 else list(range(count))


def per_device(phase, absorption, probe, measured, offsets):
    layers, tile_rows, tile_cols = phase.shape
    width = probe.shape[1]
    rim = width // 2
    probes = offsets.shape[2]
    depth_count = lax.axis_size("depth")
    depth_index = lax.axis_index("depth")
    row_index = lax.axis_index("row")
    col_index = lax.axis_index("col")
    stacked = to_transmit(jnp.stack((phase, absorption)))
    tall_slab = with_halo(stacked, (("row", 2),), rim)
    after = (stacked[0, 0, 0, 0] * 0.0).astype(jnp.int32)
    corners = offsets[0, 0] + after
    row_starts = corners[:, 0] - row_index * tile_rows + rim
    col_starts = corners[:, 1] - col_index * tile_cols + rim
    row_starts = [jnp.clip(row_starts[k], 0, 2 * rim + tile_rows - width) for k in range(probes)]
    col_starts = [jnp.clip(col_starts[k], 0, 2 * rim + tile_cols - width) for k in range(probes)]
    share = probes // depth_count
    source_rows = []
    source_cols = []
    for shift in range(depth_count):
        source = (depth_index - shift) % depth_count
        source_rows.append([lax.select_n(source * share + slot, *row_starts) for slot in range(share)])
        source_cols.append([lax.select_n(source * share + slot, *col_starts) for slot in range(share)])
    row_starts, col_starts, source_rows, source_cols, tall_slab = lax.optimization_barrier(
        (row_starts, col_starts, source_rows, source_cols, tall_slab)
    )
    extended = with_halo(tall_slab, (("col", 3),), rim)
    anchor = jnp.zeros((), jnp.int32)
    fresnel, far_field = build_tables(width)
    share = probes // depth_count
    first = depth_index * share
    cut = jnp.stack(
        [
            lax.dynamic_slice(
                extended, (anchor, anchor, row_starts[k], col_starts[k]), (2, layers, width, width)
            )
            for k in range(probes)
        ],
        axis=2,
    )
    gathered = lax.all_to_all(cut, "depth", 2, 1, tiled=True)
    windows = gathered
    total_layers = windows.shape[1]
    matrices = [fresnel] * (total_layers - 1) + [far_field]
    adjoints = [adjoint_of(matrix) for matrix in matrices]
    start_wave = probe[:, None]
    far_wave, moved = forward_layers(start_wave, windows, matrices)
    target = lax.dynamic_slice_in_dim(measured[0, 0], first, share)
    power = far_wave[0] ** 2 + far_wave[1] ** 2
    detector = far_wave * (0.25 * (power - target))[None]
    unused, phase_grad, absorb_grad = backward_layers(detector, windows, moved, adjoints)
    parts = jnp.stack((phase_grad, absorb_grad))
    grid = jnp.zeros((2, layers) + extended.shape[2:], jnp.float32)
    for shift in issue_order(depth_count):
        chunk = lax.dynamic_slice_in_dim(
            parts, ((depth_index + shift) % depth_count) * layers, layers, axis=1
        )
        if shift > 0:
            pairs = [(i, (i + shift) % depth_count) for i in range(depth_count)]
            chunk = lax.ppermute(chunk, "depth", pairs)
        for slot in range(share):
            grid = grid + place(
                chunk[:, :, slot], source_rows[shift][slot], source_cols[shift][slot], extended.shape[2:]
            )
        grid = lax.optimization_barrier(grid)
    owned = fold_both(grid, rim, pass_rows_all, pass_cols_all)
    return (owned[0], owned[1])


def solution(mesh):
    return jax.shard_map(
        per_device,
        mesh=mesh,
        in_specs=(
            P("depth", "row", "col"),
            P("depth", "row", "col"),
            P(),
            P("row", "col", None, None, None),
            P("row", "col", None, None),
        ),
        out_specs=(P("depth", "row", "col"), P("depth", "row", "col")),
        check_vma=False,
    )
```

```python
import math

import jax
import jax.numpy as jnp
from jax import lax
from jax.sharding import PartitionSpec as P

exact_mode = lax.Precision.HIGHEST
wave_mode = lax.Precision.HIGH


def from_behind(value, axis, steps):
    count = lax.axis_size(axis)
    leading, last = (max(0, -steps), min(count, count - steps))
    return lax.ppermute(value, axis, [(source, source + steps) for source in range(leading, last)])


def outside_filled(strip, edge):
    return jnp.stack((jnp.where(edge, 1.0, strip[0]), jnp.where(edge, 0.0, strip[1])))


def with_halo(block, sides, width):
    for axis, dim in sides:
        count = lax.axis_size(axis)
        index = lax.axis_index(axis)
        forward = [(i, i + 1) for i in range(count - 1)]
        backward = [(target, source) for source, target in forward]
        low = lax.ppermute(
            lax.slice_in_dim(block, block.shape[dim] - width, None, axis=dim), axis, forward
        )
        high = lax.ppermute(lax.slice_in_dim(block, 0, width, axis=dim), axis, backward)
        low = outside_filled(low, index == 0)
        high = outside_filled(high, index == count - 1)
        block = jnp.concatenate([low, block, high], axis=dim)
    return block


def matmul_exact(first, second):
    return jnp.dot(first, second, precision=exact_mode, preferred_element_type=jnp.float32)


def build_tables(width):
    index = jnp.arange(width, dtype=jnp.int32)
    product = index[:, None] * index[None, :] % width
    angle = product.astype(jnp.float32) * (2.0 * math.pi / width)
    cosine = jnp.cos(angle)
    sine = jnp.sin(angle)
    signed = jnp.where(index < width // 2, index, index - width)
    chirp = -(signed * signed % (4 * width)).astype(jnp.float32) * (2.0 * math.pi / (4 * width))
    chirp_re = jnp.cos(chirp)[None, :]
    chirp_im = jnp.sin(chirp)[None, :]
    scaled_re = cosine * chirp_re - sine * chirp_im
    scaled_im = cosine * chirp_im + sine * chirp_re
    fresnel_re = matmul_exact(scaled_re, cosine) + matmul_exact(scaled_im, sine)
    fresnel_im = matmul_exact(scaled_im, cosine) - matmul_exact(scaled_re, sine)
    fresnel = jnp.stack((fresnel_re, fresnel_im)) / width
    far_field = jnp.stack((cosine, -sine)) / math.sqrt(width)
    return (fresnel, far_field)


def adjoint_of(matrix):
    return jnp.stack((matrix[0].T, -matrix[1].T))


def left_product(matrix, waves, mode):
    return jnp.einsum(
        "ij,bjk->bik", matrix, waves, precision=mode, preferred_element_type=jnp.float32
    )


def right_product(waves, matrix, mode):
    return jnp.einsum(
        "bij,kj->bik", waves, matrix, precision=mode, preferred_element_type=jnp.float32
    )


def propagate(matrix, waves, mode):
    width = matrix.shape[1]
    tall = matrix.reshape(2 * width, width)
    batch = waves.shape[1]
    both = left_product(tall, waves.reshape((2 * batch,) + waves.shape[2:]), mode)
    from_real = both[:batch]
    from_imag = both[batch:]
    inner_re = from_real[:, :width] - from_imag[:, width:]
    inner_im = from_real[:, width:] + from_imag[:, :width]
    right = right_product(jnp.concatenate((inner_re, inner_im)), tall, mode)
    right_re = right[:batch]
    right_im = right[batch:]
    outer_re = right_re[:, :, :width] - right_im[:, :, width:]
    outer_im = right_re[:, :, width:] + right_im[:, :, :width]
    return jnp.stack((outer_re, outer_im))


def forward_layers(wave, slab, matrices):
    moved_list = []
    for layer in range(slab.shape[1]):
        trans_re = slab[0, layer]
        trans_im = slab[1, layer]
        moved = jnp.stack(
            (trans_re * wave[0] - trans_im * wave[1], trans_re * wave[1] + trans_im * wave[0])
        )
        moved_list.append(moved)
        wave = propagate(matrices[layer], moved, exact_mode)
    return (wave, jnp.stack(moved_list, axis=1))


def backward_layers(grad, slab, moved, adjoints):
    layers = slab.shape[1]
    phase_parts = [None] * layers
    absorb_parts = [None] * layers
    for layer in reversed(range(layers)):
        grad_moved = propagate(adjoints[layer], grad, wave_mode)
        moved_re = moved[0, layer]
        moved_im = moved[1, layer]
        phase_parts[layer] = grad_moved[1] * moved_re - grad_moved[0] * moved_im
        absorb_parts[layer] = -(grad_moved[0] * moved_re + grad_moved[1] * moved_im)
        trans_re = slab[0, layer]
        trans_im = slab[1, layer]
        grad = jnp.stack(
            (
                trans_re * grad_moved[0] + trans_im * grad_moved[1],
                trans_re * grad_moved[1] - trans_im * grad_moved[0],
            )
        )
    return (grad, jnp.stack(phase_parts), jnp.stack(absorb_parts))


def pass_rows_all(strip, steps):
    return from_behind(strip, "row", steps)


def pass_cols_all(strip, steps):
    return from_behind(strip, "col", steps)


def fold_rows(grid, rim, mover):
    inner = grid.shape[2] - 2 * rim
    from_above = mover(grid[:, :, inner + rim :], 1)
    from_below = mover(grid[:, :, :rim], -1)
    core = grid[:, :, rim : rim + inner]
    core = core.at[:, :, :rim].add(from_above)
    return core.at[:, :, inner - rim :].add(from_below)


def fold_cols(grid, rim, mover):
    inner = grid.shape[3] - 2 * rim
    from_left = mover(grid[:, :, :, inner + rim :], 1)
    from_right = mover(grid[:, :, :, :rim], -1)
    core = grid[:, :, :, rim : rim + inner]
    core = core.at[:, :, :, :rim].add(from_left)
    return core.at[:, :, :, inner - rim :].add(from_right)


def fold_both(grid, rim, row_mover, col_mover):
    return fold_rows(fold_cols(grid, rim, col_mover), rim, row_mover)


def to_transmit(extended):
    damping = jnp.exp(-extended[1])
    return jnp.stack((damping * jnp.cos(extended[0]), damping * jnp.sin(extended[0])))


def place(patch, row, col, frame):
    height, span = frame
    extra_rows = height - patch.shape[-2]
    extra_cols = span - patch.shape[-1]
    padded = jnp.pad(patch, ((0, 0), (0, 0), (extra_rows, extra_rows), (extra_cols, extra_cols)))
    anchor = jnp.zeros((), jnp.int32)
    start = (anchor, anchor, extra_rows - row, extra_cols - col)
    return lax.dynamic_slice(padded, start, patch.shape[:2] + (height, span))


def issue_order(count):
    half = count // 2
    rest = [shift for shift in range(1, count) if shift != half]
    return [0, half] + rest if count % 2 == 0 and half > 0 else list(range(count))


def per_device(phase, absorption, probe, measured, offsets):
    layers, tile_rows, tile_cols = phase.shape
    width = probe.shape[1]
    rim = width // 2
    probes = offsets.shape[2]
    depth_count = lax.axis_size("depth")
    depth_index = lax.axis_index("depth")
    row_index = lax.axis_index("row")
    col_index = lax.axis_index("col")
    stacked = to_transmit(jnp.stack((phase, absorption)))
    tall_slab = with_halo(stacked, (("row", 2),), rim)
    col_count = lax.axis_size("col")
    col_forward = [(i, i + 1) for i in range(col_count - 1)]
    col_backward = [(target, source) for source, target in col_forward]
    from_left = outside_filled(
        lax.ppermute(stacked[:, :, :, tile_cols - rim :], "col", col_forward), col_index == 0
    )
    from_right = outside_filled(
        lax.ppermute(stacked[:, :, :, :rim], "col", col_backward), col_index == col_count - 1
    )
    after = (stacked[0, 0, 0, 0] * 0.0).astype(jnp.int32)
    corners = offsets[0, 0] + after
    row_starts = corners[:, 0] - row_index * tile_rows + rim
    col_starts = corners[:, 1] - col_index * tile_cols + rim
    row_starts = [jnp.clip(row_starts[k], 0, 2 * rim + tile_rows - width) for k in range(probes)]
    col_starts = [jnp.clip(col_starts[k], 0, 2 * rim + tile_cols - width) for k in range(probes)]
    share = probes // depth_count
    source_rows = []
    source_cols = []
    for shift in range(depth_count):
        source = (depth_index - shift) % depth_count
        source_rows.append([lax.select_n(source * share + slot, *row_starts) for slot in range(share)])
        source_cols.append([lax.select_n(source * share + slot, *col_starts) for slot in range(share)])
    row_starts, col_starts, source_rows, source_cols, tall_slab = lax.optimization_barrier(
        (row_starts, col_starts, source_rows, source_cols, tall_slab)
    )
    above = tall_slab[:, :, :rim]
    below = tall_slab[:, :, rim + tile_rows :]
    corner_left = outside_filled(
        lax.ppermute(
            jnp.concatenate((above[:, :, :, tile_cols - rim :], below[:, :, :, tile_cols - rim :]), axis=2),
            "col",
            col_forward,
        ),
        col_index == 0,
    )
    corner_right = outside_filled(
        lax.ppermute(
            jnp.concatenate((above[:, :, :, :rim], below[:, :, :, :rim]), axis=2), "col", col_backward
        ),
        col_index == col_count - 1,
    )
    left_side = jnp.concatenate((corner_left[:, :, :rim], from_left, corner_left[:, :, rim:]), axis=2)
    right_side = jnp.concatenate((corner_right[:, :, :rim], from_right, corner_right[:, :, rim:]), axis=2)
    extended = jnp.concatenate((left_side, tall_slab, right_side), axis=3)
    anchor = jnp.zeros((), jnp.int32)
    fresnel, far_field = build_tables(width)
    share = probes // depth_count
    first = depth_index * share
    cut = jnp.stack(
        [
            lax.dynamic_slice(
                extended, (anchor, anchor, row_starts[k], col_starts[k]), (2, layers, width, width)
            )
            for k in range(probes)
        ],
        axis=2,
    )
    gathered = lax.all_to_all(cut, "depth", 2, 1, tiled=True)
    windows = gathered
    total_layers = windows.shape[1]
    matrices = [fresnel] * (total_layers - 1) + [far_field]
    adjoints = [adjoint_of(matrix) for matrix in matrices]
    start_wave = probe[:, None]
    far_wave, moved = forward_layers(start_wave, windows, matrices)
    target = lax.dynamic_slice_in_dim(measured[0, 0], first, share)
    power = far_wave[0] ** 2 + far_wave[1] ** 2
    detector = far_wave * (0.25 * (power - target))[None]
    unused, phase_grad, absorb_grad = backward_layers(detector, windows, moved, adjoints)
    parts = jnp.stack((phase_grad, absorb_grad))
    grid = jnp.zeros((2, layers) + extended.shape[2:], jnp.float32)
    for shift in issue_order(depth_count):
        chunk = lax.dynamic_slice_in_dim(
            parts, ((depth_index + shift) % depth_count) * layers, layers, axis=1
        )
        if shift > 0:
            pairs = [(i, (i + shift) % depth_count) for i in range(depth_count)]
            chunk = lax.ppermute(chunk, "depth", pairs)
        for slot in range(share):
            grid = grid + place(
                chunk[:, :, slot], source_rows[shift][slot], source_cols[shift][slot], extended.shape[2:]
            )
        grid = lax.optimization_barrier(grid)
    owned = fold_both(grid, rim, pass_rows_all, pass_cols_all)
    return (owned[0], owned[1])


def solution(mesh):
    return jax.shard_map(
        per_device,
        mesh=mesh,
        in_specs=(
            P("depth", "row", "col"),
            P("depth", "row", "col"),
            P(),
            P("row", "col", None, None, None),
            P("row", "col", None, None),
        ),
        out_specs=(P("depth", "row", "col"), P("depth", "row", "col")),
        check_vma=False,
    )
```

```python
import math

import jax
import jax.numpy as jnp
from jax import lax
from jax.sharding import PartitionSpec as P

exact_mode = lax.Precision.HIGHEST
wave_mode = lax.Precision.HIGH


def from_behind(value, axis, steps):
    count = lax.axis_size(axis)
    leading, last = (max(0, -steps), min(count, count - steps))
    return lax.ppermute(value, axis, [(source, source + steps) for source in range(leading, last)])


def outside_filled(strip, edge):
    return jnp.stack((jnp.where(edge, 1.0, strip[0]), jnp.where(edge, 0.0, strip[1])))


def with_halo(block, sides, width):
    for axis, dim in sides:
        count = lax.axis_size(axis)
        index = lax.axis_index(axis)
        forward = [(i, i + 1) for i in range(count - 1)]
        backward = [(target, source) for source, target in forward]
        low = lax.ppermute(
            lax.slice_in_dim(block, block.shape[dim] - width, None, axis=dim), axis, forward
        )
        high = lax.ppermute(lax.slice_in_dim(block, 0, width, axis=dim), axis, backward)
        low = outside_filled(low, index == 0)
        high = outside_filled(high, index == count - 1)
        block = jnp.concatenate([low, block, high], axis=dim)
    return block


def matmul_exact(first, second):
    return jnp.dot(first, second, precision=exact_mode, preferred_element_type=jnp.float32)


def build_tables(width):
    index = jnp.arange(width, dtype=jnp.int32)
    product = index[:, None] * index[None, :] % width
    angle = product.astype(jnp.float32) * (2.0 * math.pi / width)
    cosine = jnp.cos(angle)
    sine = jnp.sin(angle)
    signed = jnp.where(index < width // 2, index, index - width)
    chirp = -(signed * signed % (4 * width)).astype(jnp.float32) * (2.0 * math.pi / (4 * width))
    chirp_re = jnp.cos(chirp)[None, :]
    chirp_im = jnp.sin(chirp)[None, :]
    scaled_re = cosine * chirp_re - sine * chirp_im
    scaled_im = cosine * chirp_im + sine * chirp_re
    fresnel_re = matmul_exact(scaled_re, cosine) + matmul_exact(scaled_im, sine)
    fresnel_im = matmul_exact(scaled_im, cosine) - matmul_exact(scaled_re, sine)
    fresnel = jnp.stack((fresnel_re, fresnel_im)) / width
    far_field = jnp.stack((cosine, -sine)) / math.sqrt(width)
    return (fresnel, far_field)


def adjoint_of(matrix):
    return jnp.stack((matrix[0].T, -matrix[1].T))


def left_product(matrix, waves, mode):
    return jnp.einsum(
        "ij,bjk->bik", matrix, waves, precision=mode, preferred_element_type=jnp.float32
    )


def right_product(waves, matrix, mode):
    return jnp.einsum(
        "bij,kj->bik", waves, matrix, precision=mode, preferred_element_type=jnp.float32
    )


def propagate(matrix, waves, mode):
    width = matrix.shape[1]
    tall = matrix.reshape(2 * width, width)
    batch = waves.shape[1]
    both = left_product(tall, waves.reshape((2 * batch,) + waves.shape[2:]), mode)
    from_real = both[:batch]
    from_imag = both[batch:]
    inner_re = from_real[:, :width] - from_imag[:, width:]
    inner_im = from_real[:, width:] + from_imag[:, :width]
    right = right_product(jnp.concatenate((inner_re, inner_im)), tall, mode)
    right_re = right[:batch]
    right_im = right[batch:]
    outer_re = right_re[:, :, :width] - right_im[:, :, width:]
    outer_im = right_re[:, :, width:] + right_im[:, :, :width]
    return jnp.stack((outer_re, outer_im))


def forward_layers(wave, slab, matrices):
    moved_list = []
    for layer in range(slab.shape[1]):
        trans_re = slab[0, layer]
        trans_im = slab[1, layer]
        moved = jnp.stack(
            (trans_re * wave[0] - trans_im * wave[1], trans_re * wave[1] + trans_im * wave[0])
        )
        moved_list.append(moved)
        wave = propagate(matrices[layer], moved, exact_mode)
    return (wave, jnp.stack(moved_list, axis=1))


def backward_layers(grad, slab, moved, adjoints):
    layers = slab.shape[1]
    phase_parts = [None] * layers
    absorb_parts = [None] * layers
    for layer in reversed(range(layers)):
        grad_moved = propagate(adjoints[layer], grad, wave_mode)
        moved_re = moved[0, layer]
        moved_im = moved[1, layer]
        phase_parts[layer] = grad_moved[1] * moved_re - grad_moved[0] * moved_im
        absorb_parts[layer] = -(grad_moved[0] * moved_re + grad_moved[1] * moved_im)
        trans_re = slab[0, layer]
        trans_im = slab[1, layer]
        grad = jnp.stack(
            (
                trans_re * grad_moved[0] + trans_im * grad_moved[1],
                trans_re * grad_moved[1] - trans_im * grad_moved[0],
            )
        )
    return (grad, jnp.stack(phase_parts), jnp.stack(absorb_parts))


def pass_rows_all(strip, steps):
    return from_behind(strip, "row", steps)


def pass_cols_all(strip, steps):
    return from_behind(strip, "col", steps)


def fold_rows(grid, rim, mover):
    inner = grid.shape[2] - 2 * rim
    from_above = mover(grid[:, :, inner + rim :], 1)
    from_below = mover(grid[:, :, :rim], -1)
    core = grid[:, :, rim : rim + inner]
    core = core.at[:, :, :rim].add(from_above)
    return core.at[:, :, inner - rim :].add(from_below)


def fold_cols(grid, rim, mover):
    inner = grid.shape[3] - 2 * rim
    from_left = mover(grid[:, :, :, inner + rim :], 1)
    from_right = mover(grid[:, :, :, :rim], -1)
    core = grid[:, :, :, rim : rim + inner]
    core = core.at[:, :, :, :rim].add(from_left)
    return core.at[:, :, :, inner - rim :].add(from_right)


def fold_both(grid, rim, row_mover, col_mover):
    return fold_rows(fold_cols(grid, rim, col_mover), rim, row_mover)


def to_transmit(extended):
    damping = jnp.exp(-extended[1])
    return jnp.stack((damping * jnp.cos(extended[0]), damping * jnp.sin(extended[0])))


def place(patch, row, col, frame):
    height, span = frame
    extra_rows = height - patch.shape[-2]
    extra_cols = span - patch.shape[-1]
    padded = jnp.pad(patch, ((0, 0), (0, 0), (extra_rows, extra_rows), (extra_cols, extra_cols)))
    anchor = jnp.zeros((), jnp.int32)
    start = (anchor, anchor, extra_rows - row, extra_cols - col)
    return lax.dynamic_slice(padded, start, patch.shape[:2] + (height, span))


def issue_order(count):
    half = count // 2
    rest = [shift for shift in range(1, count) if shift != half]
    return [0, half] + rest if count % 2 == 0 and half > 0 else list(range(count))


def per_device(phase, absorption, probe, measured, offsets):
    layers, tile_rows, tile_cols = phase.shape
    width = probe.shape[1]
    rim = width // 2
    probes = offsets.shape[2]
    depth_count = lax.axis_size("depth")
    depth_index = lax.axis_index("depth")
    row_index = lax.axis_index("row")
    col_index = lax.axis_index("col")
    stacked = to_transmit(jnp.stack((phase, absorption)))
    tall_slab = with_halo(stacked, (("row", 2),), rim)
    after = (stacked[0, 0, 0, 0] * 0.0).astype(jnp.int32)
    corners = offsets[0, 0] + after
    row_starts = corners[:, 0] - row_index * tile_rows + rim
    col_starts = corners[:, 1] - col_index * tile_cols + rim
    row_starts = [jnp.clip(row_starts[k], 0, 2 * rim + tile_rows - width) for k in range(probes)]
    col_starts = [jnp.clip(col_starts[k], 0, 2 * rim + tile_cols - width) for k in range(probes)]
    share = probes // depth_count
    source_rows = []
    source_cols = []
    for shift in range(depth_count):
        source = (depth_index - shift) % depth_count
        source_rows.append([lax.select_n(source * share + slot, *row_starts) for slot in range(share)])
        source_cols.append([lax.select_n(source * share + slot, *col_starts) for slot in range(share)])
    row_starts, col_starts, source_rows, source_cols, tall_slab = lax.optimization_barrier(
        (row_starts, col_starts, source_rows, source_cols, tall_slab)
    )
    extended = with_halo(tall_slab, (("col", 3),), rim)
    anchor = jnp.zeros((), jnp.int32)
    fresnel, far_field = build_tables(width)
    share = probes // depth_count
    first = depth_index * share
    cut = jnp.stack(
        [
            lax.dynamic_slice(
                extended, (anchor, anchor, row_starts[k], col_starts[k]), (2, layers, width, width)
            )
            for k in range(probes)
        ],
        axis=2,
    )
    gathered = lax.all_to_all(cut, "depth", 2, 1, tiled=True)
    windows = jnp.swapaxes(gathered, -1, -2)
    total_layers = windows.shape[1]
    matrices = [fresnel] * (total_layers - 1) + [far_field]
    adjoints = [adjoint_of(matrix) for matrix in matrices]
    start_wave = jnp.swapaxes(probe, -1, -2)[:, None]
    far_wave, moved = forward_layers(start_wave, windows, matrices)
    target = jnp.swapaxes(lax.dynamic_slice_in_dim(measured[0, 0], first, share), -1, -2)
    power = far_wave[0] ** 2 + far_wave[1] ** 2
    detector = far_wave * (0.25 * (power - target))[None]
    unused, phase_grad, absorb_grad = backward_layers(detector, windows, moved, adjoints)
    parts = jnp.swapaxes(jnp.stack((phase_grad, absorb_grad)), -1, -2)
    grid = jnp.zeros((2, layers) + extended.shape[2:], jnp.float32)
    for shift in issue_order(depth_count):
        chunk = lax.dynamic_slice_in_dim(
            parts, ((depth_index + shift) % depth_count) * layers, layers, axis=1
        )
        if shift > 0:
            pairs = [(i, (i + shift) % depth_count) for i in range(depth_count)]
            chunk = lax.ppermute(chunk, "depth", pairs)
        for slot in range(share):
            grid = grid + place(
                chunk[:, :, slot], source_rows[shift][slot], source_cols[shift][slot], extended.shape[2:]
            )
        grid = lax.optimization_barrier(grid)
    owned = fold_both(grid, rim, pass_rows_all, pass_cols_all)
    return (owned[0], owned[1])


def solution(mesh):
    return jax.shard_map(
        per_device,
        mesh=mesh,
        in_specs=(
            P("depth", "row", "col"),
            P("depth", "row", "col"),
            P(),
            P("row", "col", None, None, None),
            P("row", "col", None, None),
        ),
        out_specs=(P("depth", "row", "col"), P("depth", "row", "col")),
        check_vma=False,
    )
```

```python
import math

import jax
import jax.numpy as jnp
from jax import lax
from jax.sharding import PartitionSpec as P

exact_mode = lax.Precision.HIGHEST
wave_mode = lax.Precision.HIGH


def from_behind(value, axis, steps):
    count = lax.axis_size(axis)
    leading, last = (max(0, -steps), min(count, count - steps))
    return lax.ppermute(value, axis, [(source, source + steps) for source in range(leading, last)])


def outside_filled(strip, edge):
    return jnp.stack((jnp.where(edge, 1.0, strip[0]), jnp.where(edge, 0.0, strip[1])))


def with_halo(block, sides, width):
    for axis, dim in sides:
        count = lax.axis_size(axis)
        index = lax.axis_index(axis)
        forward = [(i, i + 1) for i in range(count - 1)]
        backward = [(target, source) for source, target in forward]
        low = lax.ppermute(
            lax.slice_in_dim(block, block.shape[dim] - width, None, axis=dim), axis, forward
        )
        high = lax.ppermute(lax.slice_in_dim(block, 0, width, axis=dim), axis, backward)
        low = outside_filled(low, index == 0)
        high = outside_filled(high, index == count - 1)
        block = jnp.concatenate([low, block, high], axis=dim)
    return block


def matmul_exact(first, second):
    return jnp.dot(first, second, precision=exact_mode, preferred_element_type=jnp.float32)


def build_tables(width):
    index = jnp.arange(width, dtype=jnp.int32)
    product = index[:, None] * index[None, :] % width
    angle = product.astype(jnp.float32) * (2.0 * math.pi / width)
    cosine = jnp.cos(angle)
    sine = jnp.sin(angle)
    signed = jnp.where(index < width // 2, index, index - width)
    chirp = -(signed * signed % (4 * width)).astype(jnp.float32) * (2.0 * math.pi / (4 * width))
    chirp_re = jnp.cos(chirp)[None, :]
    chirp_im = jnp.sin(chirp)[None, :]
    scaled_re = cosine * chirp_re - sine * chirp_im
    scaled_im = cosine * chirp_im + sine * chirp_re
    fresnel_re = matmul_exact(scaled_re, cosine) + matmul_exact(scaled_im, sine)
    fresnel_im = matmul_exact(scaled_im, cosine) - matmul_exact(scaled_re, sine)
    fresnel = jnp.stack((fresnel_re, fresnel_im)) / width
    far_field = jnp.stack((cosine, -sine)) / math.sqrt(width)
    return (fresnel, far_field)


def adjoint_of(matrix):
    return jnp.stack((matrix[0].T, -matrix[1].T))


def left_product(matrix, waves, mode):
    return jnp.einsum(
        "ij,bjk->bik", matrix, waves, precision=mode, preferred_element_type=jnp.float32
    )


def right_product(waves, matrix, mode):
    return jnp.einsum(
        "bij,kj->bik", waves, matrix, precision=mode, preferred_element_type=jnp.float32
    )


def propagate(matrix, waves, mode):
    width = matrix.shape[1]
    tall = matrix.reshape(2 * width, width)
    batch = waves.shape[1]
    both = left_product(tall, waves.reshape((2 * batch,) + waves.shape[2:]), mode)
    from_real = both[:batch]
    from_imag = both[batch:]
    inner_re = from_real[:, :width] - from_imag[:, width:]
    inner_im = from_real[:, width:] + from_imag[:, :width]
    right = right_product(jnp.concatenate((inner_re, inner_im)), tall, mode)
    right_re = right[:batch]
    right_im = right[batch:]
    outer_re = right_re[:, :, :width] - right_im[:, :, width:]
    outer_im = right_re[:, :, width:] + right_im[:, :, :width]
    return jnp.stack((outer_re, outer_im))


def forward_layers(wave, slab, matrices):
    moved_list = []
    for layer in range(slab.shape[1]):
        trans_re = slab[0, layer]
        trans_im = slab[1, layer]
        if layer == 0:
            moved = jnp.stack((trans_re, trans_im))
        else:
            moved = jnp.stack(
                (trans_re * wave[0] - trans_im * wave[1], trans_re * wave[1] + trans_im * wave[0])
            )
        moved_list.append(moved)
        wave = propagate(matrices[layer], moved, exact_mode)
    return (wave, jnp.stack(moved_list, axis=1))


def backward_layers(grad, slab, moved, adjoints):
    layers = slab.shape[1]
    phase_parts = [None] * layers
    absorb_parts = [None] * layers
    for layer in reversed(range(layers)):
        grad_moved = propagate(adjoints[layer], grad, wave_mode)
        moved_re = moved[0, layer]
        moved_im = moved[1, layer]
        phase_parts[layer] = grad_moved[1] * moved_re - grad_moved[0] * moved_im
        absorb_parts[layer] = -(grad_moved[0] * moved_re + grad_moved[1] * moved_im)
        trans_re = slab[0, layer]
        trans_im = slab[1, layer]
        grad = jnp.stack(
            (
                trans_re * grad_moved[0] + trans_im * grad_moved[1],
                trans_re * grad_moved[1] - trans_im * grad_moved[0],
            )
        )
    return (grad, jnp.stack(phase_parts), jnp.stack(absorb_parts))


def pass_rows_all(strip, steps):
    return from_behind(strip, "row", steps)


def pass_cols_all(strip, steps):
    return from_behind(strip, "col", steps)


def fold_rows(grid, rim, mover):
    inner = grid.shape[2] - 2 * rim
    from_above = mover(grid[:, :, inner + rim :], 1)
    from_below = mover(grid[:, :, :rim], -1)
    core = grid[:, :, rim : rim + inner]
    core = core.at[:, :, :rim].add(from_above)
    return core.at[:, :, inner - rim :].add(from_below)


def fold_cols(grid, rim, mover):
    inner = grid.shape[3] - 2 * rim
    from_left = mover(grid[:, :, :, inner + rim :], 1)
    from_right = mover(grid[:, :, :, :rim], -1)
    core = grid[:, :, :, rim : rim + inner]
    core = core.at[:, :, :, :rim].add(from_left)
    return core.at[:, :, :, inner - rim :].add(from_right)


def fold_both(grid, rim, row_mover, col_mover):
    return fold_rows(fold_cols(grid, rim, col_mover), rim, row_mover)


def to_transmit(extended):
    damping = jnp.exp(-extended[1])
    return jnp.stack((damping * jnp.cos(extended[0]), damping * jnp.sin(extended[0])))


def place(patch, row, col, frame):
    height, span = frame
    extra_rows = height - patch.shape[-2]
    extra_cols = span - patch.shape[-1]
    padded = jnp.pad(patch, ((0, 0), (0, 0), (extra_rows, extra_rows), (extra_cols, extra_cols)))
    anchor = jnp.zeros((), jnp.int32)
    start = (anchor, anchor, extra_rows - row, extra_cols - col)
    return lax.dynamic_slice(padded, start, patch.shape[:2] + (height, span))


def issue_order(count):
    half = count // 2
    rest = [shift for shift in range(1, count) if shift != half]
    return [0, half] + rest if count % 2 == 0 and half > 0 else list(range(count))


def per_device(phase, absorption, probe, measured, offsets):
    layers, tile_rows, tile_cols = phase.shape
    width = probe.shape[1]
    rim = width // 2
    probes = offsets.shape[2]
    depth_count = lax.axis_size("depth")
    depth_index = lax.axis_index("depth")
    row_index = lax.axis_index("row")
    col_index = lax.axis_index("col")
    stacked = to_transmit(jnp.stack((phase, absorption)))
    tall_slab = with_halo(stacked, (("row", 2),), rim)
    after = (stacked[0, 0, 0, 0] * 0.0).astype(jnp.int32)
    corners = offsets[0, 0] + after
    row_starts = corners[:, 0] - row_index * tile_rows + rim
    col_starts = corners[:, 1] - col_index * tile_cols + rim
    row_starts = [jnp.clip(row_starts[k], 0, 2 * rim + tile_rows - width) for k in range(probes)]
    col_starts = [jnp.clip(col_starts[k], 0, 2 * rim + tile_cols - width) for k in range(probes)]
    share = probes // depth_count
    source_rows = []
    source_cols = []
    for shift in range(depth_count):
        source = (depth_index - shift) % depth_count
        source_rows.append([lax.select_n(source * share + slot, *row_starts) for slot in range(share)])
        source_cols.append([lax.select_n(source * share + slot, *col_starts) for slot in range(share)])
    row_starts, col_starts, source_rows, source_cols, tall_slab = lax.optimization_barrier(
        (row_starts, col_starts, source_rows, source_cols, tall_slab)
    )
    extended = with_halo(tall_slab, (("col", 3),), rim)
    anchor = jnp.zeros((), jnp.int32)
    fresnel, far_field = build_tables(width)
    share = probes // depth_count
    first = depth_index * share
    cut = jnp.stack(
        [
            lax.dynamic_slice(
                extended, (anchor, anchor, row_starts[k], col_starts[k]), (2, layers, width, width)
            )
            for k in range(probes)
        ],
        axis=2,
    )
    lead = cut[:, 0]
    lit = jnp.stack(
        (
            lead[0] * probe[0] - lead[1] * probe[1],
            lead[0] * probe[1] + lead[1] * probe[0],
        )
    )
    lead = jnp.where(depth_index == 0, lit, lead)
    cut = jnp.concatenate((lead[:, None], cut[:, 1:]), axis=1)
    gathered = lax.all_to_all(cut, "depth", 2, 1, tiled=True)
    windows = jnp.swapaxes(gathered, -1, -2)
    total_layers = windows.shape[1]
    matrices = [fresnel] * (total_layers - 1) + [far_field]
    adjoints = [adjoint_of(matrix) for matrix in matrices]
    start_wave = None
    far_wave, moved = forward_layers(start_wave, windows, matrices)
    target = jnp.swapaxes(lax.dynamic_slice_in_dim(measured[0, 0], first, share), -1, -2)
    power = far_wave[0] ** 2 + far_wave[1] ** 2
    detector = far_wave * (0.25 * (power - target))[None]
    unused, phase_grad, absorb_grad = backward_layers(detector, windows, moved, adjoints)
    parts = jnp.swapaxes(jnp.stack((phase_grad, absorb_grad)), -1, -2)
    grid = jnp.zeros((2, layers) + extended.shape[2:], jnp.float32)
    for shift in issue_order(depth_count):
        chunk = lax.dynamic_slice_in_dim(
            parts, ((depth_index + shift) % depth_count) * layers, layers, axis=1
        )
        if shift > 0:
            pairs = [(i, (i + shift) % depth_count) for i in range(depth_count)]
            chunk = lax.ppermute(chunk, "depth", pairs)
        for slot in range(share):
            grid = grid + place(
                chunk[:, :, slot], source_rows[shift][slot], source_cols[shift][slot], extended.shape[2:]
            )
        grid = lax.optimization_barrier(grid)
    owned = fold_both(grid, rim, pass_rows_all, pass_cols_all)
    return (owned[0], owned[1])


def solution(mesh):
    return jax.shard_map(
        per_device,
        mesh=mesh,
        in_specs=(
            P("depth", "row", "col"),
            P("depth", "row", "col"),
            P(),
            P("row", "col", None, None, None),
            P("row", "col", None, None),
        ),
        out_specs=(P("depth", "row", "col"), P("depth", "row", "col")),
        check_vma=False,
    )
```

```python
import math

import jax
import jax.numpy as jnp
from jax import lax
from jax.sharding import PartitionSpec as P

exact_mode = lax.Precision.HIGHEST
wave_mode = lax.Precision.HIGH


def from_behind(value, axis, steps):
    count = lax.axis_size(axis)
    leading, last = (max(0, -steps), min(count, count - steps))
    return lax.ppermute(value, axis, [(source, source + steps) for source in range(leading, last)])


def outside_filled(strip, edge):
    return jnp.stack((jnp.where(edge, 1.0, strip[0]), jnp.where(edge, 0.0, strip[1])))


def with_halo(block, sides, width):
    for axis, dim in sides:
        count = lax.axis_size(axis)
        index = lax.axis_index(axis)
        forward = [(i, i + 1) for i in range(count - 1)]
        backward = [(target, source) for source, target in forward]
        low = lax.ppermute(
            lax.slice_in_dim(block, block.shape[dim] - width, None, axis=dim), axis, forward
        )
        high = lax.ppermute(lax.slice_in_dim(block, 0, width, axis=dim), axis, backward)
        low = outside_filled(low, index == 0)
        high = outside_filled(high, index == count - 1)
        block = jnp.concatenate([low, block, high], axis=dim)
    return block


def matmul_exact(first, second):
    return jnp.dot(first, second, precision=exact_mode, preferred_element_type=jnp.float32)


def build_tables(width):
    index = jnp.arange(width, dtype=jnp.int32)
    product = index[:, None] * index[None, :] % width
    angle = product.astype(jnp.float32) * (2.0 * math.pi / width)
    cosine = jnp.cos(angle)
    sine = jnp.sin(angle)
    signed = jnp.where(index < width // 2, index, index - width)
    chirp = -(signed * signed % (4 * width)).astype(jnp.float32) * (2.0 * math.pi / (4 * width))
    chirp_re = jnp.cos(chirp)[None, :]
    chirp_im = jnp.sin(chirp)[None, :]
    scaled_re = cosine * chirp_re - sine * chirp_im
    scaled_im = cosine * chirp_im + sine * chirp_re
    fresnel_re = matmul_exact(scaled_re, cosine) + matmul_exact(scaled_im, sine)
    fresnel_im = matmul_exact(scaled_im, cosine) - matmul_exact(scaled_re, sine)
    fresnel = jnp.stack((fresnel_re, fresnel_im)) / width
    far_field = jnp.stack((cosine, -sine)) / math.sqrt(width)
    return (fresnel, far_field)


def adjoint_of(matrix):
    return jnp.stack((matrix[0].T, -matrix[1].T))


def left_product(matrix, waves, mode):
    return jnp.einsum(
        "ij,bjk->bik", matrix, waves, precision=mode, preferred_element_type=jnp.float32
    )


def right_product(waves, matrix, mode):
    return jnp.einsum(
        "bij,kj->bik", waves, matrix, precision=mode, preferred_element_type=jnp.float32
    )


def propagate(matrix, waves, mode):
    width = matrix.shape[1]
    tall = matrix.reshape(2 * width, width)
    batch = waves.shape[1]
    both = left_product(tall, waves.reshape((2 * batch,) + waves.shape[2:]), mode)
    from_real = both[:batch]
    from_imag = both[batch:]
    inner_re = from_real[:, :width] - from_imag[:, width:]
    inner_im = from_real[:, width:] + from_imag[:, :width]
    right = right_product(jnp.concatenate((inner_re, inner_im)), tall, mode)
    right_re = right[:batch]
    right_im = right[batch:]
    outer_re = right_re[:, :, :width] - right_im[:, :, width:]
    outer_im = right_re[:, :, width:] + right_im[:, :, :width]
    return jnp.stack((outer_re, outer_im))


def forward_layers(wave, slab, matrices):
    moved_list = []
    for layer in range(slab.shape[1]):
        trans_re = slab[0, layer]
        trans_im = slab[1, layer]
        moved = jnp.stack(
            (trans_re * wave[0] - trans_im * wave[1], trans_re * wave[1] + trans_im * wave[0])
        )
        moved_list.append(moved)
        wave = propagate(matrices[layer], moved, exact_mode)
    return (wave, jnp.stack(moved_list, axis=1))


def backward_layers(grad, slab, moved, adjoints):
    layers = slab.shape[1]
    phase_parts = [None] * layers
    absorb_parts = [None] * layers
    for layer in reversed(range(layers)):
        grad_moved = propagate(adjoints[layer], grad, wave_mode)
        moved_re = moved[0, layer]
        moved_im = moved[1, layer]
        phase_parts[layer] = grad_moved[1] * moved_re - grad_moved[0] * moved_im
        absorb_parts[layer] = -(grad_moved[0] * moved_re + grad_moved[1] * moved_im)
        trans_re = slab[0, layer]
        trans_im = slab[1, layer]
        grad = jnp.stack(
            (
                trans_re * grad_moved[0] + trans_im * grad_moved[1],
                trans_re * grad_moved[1] - trans_im * grad_moved[0],
            )
        )
    return (grad, jnp.stack(phase_parts), jnp.stack(absorb_parts))


def pass_rows_all(strip, steps):
    return from_behind(strip, "row", steps)


def pass_cols_all(strip, steps):
    return from_behind(strip, "col", steps)


def fold_rows(grid, rim, mover):
    inner = grid.shape[2] - 2 * rim
    from_above = mover(grid[:, :, inner + rim :], 1)
    from_below = mover(grid[:, :, :rim], -1)
    core = grid[:, :, rim : rim + inner]
    core = core.at[:, :, :rim].add(from_above)
    return core.at[:, :, inner - rim :].add(from_below)


def fold_cols(grid, rim, mover):
    inner = grid.shape[3] - 2 * rim
    from_left = mover(grid[:, :, :, inner + rim :], 1)
    from_right = mover(grid[:, :, :, :rim], -1)
    core = grid[:, :, :, rim : rim + inner]
    core = core.at[:, :, :, :rim].add(from_left)
    return core.at[:, :, :, inner - rim :].add(from_right)


def fold_both(grid, rim, row_mover, col_mover):
    return fold_rows(fold_cols(grid, rim, col_mover), rim, row_mover)


def to_transmit(extended):
    damping = jnp.exp(-extended[1])
    return jnp.stack((damping * jnp.cos(extended[0]), damping * jnp.sin(extended[0])))


def place(patch, row, col, frame):
    height, span = frame
    extra_rows = height - patch.shape[-2]
    extra_cols = span - patch.shape[-1]
    padded = jnp.pad(patch, ((0, 0), (0, 0), (extra_rows, extra_rows), (extra_cols, extra_cols)))
    anchor = jnp.zeros((), jnp.int32)
    start = (anchor, anchor, extra_rows - row, extra_cols - col)
    return lax.dynamic_slice(padded, start, patch.shape[:2] + (height, span))


def issue_order(count):
    half = count // 2
    rest = [shift for shift in range(1, count) if shift != half]
    return [0, half] + rest if count % 2 == 0 and half > 0 else list(range(count))


def place_region(patch, row, col, rows, cols):
    height = rows[0] + rows[1]
    span = cols[0] + cols[1] + 2 * patch.shape[-1]
    padded = jnp.pad(patch, ((0, 0), (0, 0), (height, height), (span, span)))
    anchor = jnp.zeros((), jnp.int32)
    start = (anchor, anchor, height - row + rows[0], span - col + cols[0])
    return lax.dynamic_slice(padded, start, patch.shape[:2] + (rows[1], cols[1]))


def per_device(phase, absorption, probe, measured, offsets):
    layers, tile_rows, tile_cols = phase.shape
    width = probe.shape[1]
    rim = width // 2
    probes = offsets.shape[2]
    depth_count = lax.axis_size("depth")
    depth_index = lax.axis_index("depth")
    row_index = lax.axis_index("row")
    col_index = lax.axis_index("col")
    stacked = to_transmit(jnp.stack((phase, absorption)))
    tall_slab = with_halo(stacked, (("row", 2),), rim)
    after = (stacked[0, 0, 0, 0] * 0.0).astype(jnp.int32)
    corners = offsets[0, 0] + after
    row_starts = corners[:, 0] - row_index * tile_rows + rim
    col_starts = corners[:, 1] - col_index * tile_cols + rim
    row_starts = [jnp.clip(row_starts[k], 0, 2 * rim + tile_rows - width) for k in range(probes)]
    col_starts = [jnp.clip(col_starts[k], 0, 2 * rim + tile_cols - width) for k in range(probes)]
    share = probes // depth_count
    source_rows = []
    source_cols = []
    for shift in range(depth_count):
        source = (depth_index - shift) % depth_count
        source_rows.append([lax.select_n(source * share + slot, *row_starts) for slot in range(share)])
        source_cols.append([lax.select_n(source * share + slot, *col_starts) for slot in range(share)])
    row_starts, col_starts, source_rows, source_cols, tall_slab = lax.optimization_barrier(
        (row_starts, col_starts, source_rows, source_cols, tall_slab)
    )
    extended = with_halo(tall_slab, (("col", 3),), rim)
    anchor = jnp.zeros((), jnp.int32)
    fresnel, far_field = build_tables(width)
    share = probes // depth_count
    first = depth_index * share
    cut = jnp.stack(
        [
            lax.dynamic_slice(
                extended, (anchor, anchor, row_starts[k], col_starts[k]), (2, layers, width, width)
            )
            for k in range(probes)
        ],
        axis=2,
    )
    gathered = lax.all_to_all(cut, "depth", 2, 1, tiled=True)
    windows = jnp.swapaxes(gathered, -1, -2)
    total_layers = windows.shape[1]
    matrices = [fresnel] * (total_layers - 1) + [far_field]
    adjoints = [adjoint_of(matrix) for matrix in matrices]
    start_wave = jnp.swapaxes(probe, -1, -2)[:, None]
    far_wave, moved = forward_layers(start_wave, windows, matrices)
    target = jnp.swapaxes(lax.dynamic_slice_in_dim(measured[0, 0], first, share), -1, -2)
    power = far_wave[0] ** 2 + far_wave[1] ** 2
    detector = far_wave * (0.25 * (power - target))[None]
    unused, phase_grad, absorb_grad = backward_layers(detector, windows, moved, adjoints)
    parts = jnp.swapaxes(jnp.stack((phase_grad, absorb_grad)), -1, -2)
    frame_rows, frame_cols = extended.shape[2:]
    regions = [(0, rim), (rim, frame_cols - 2 * rim), (frame_cols - rim, rim)]
    pieces = [jnp.zeros((2, layers, frame_rows, wide), jnp.float32) for start, wide in regions]
    for shift in issue_order(depth_count):
        chunk = lax.dynamic_slice_in_dim(
            parts, ((depth_index + shift) % depth_count) * layers, layers, axis=1
        )
        if shift > 0:
            pairs = [(i, (i + shift) % depth_count) for i in range(depth_count)]
            chunk = lax.ppermute(chunk, "depth", pairs)
        for slot in range(share):
            pieces = [
                piece
                + place_region(
                    chunk[:, :, slot],
                    source_rows[shift][slot],
                    source_cols[shift][slot],
                    (0, frame_rows),
                    region,
                )
                for piece, region in zip(pieces, regions)
            ]
        if shift == 0:
            pieces = list(lax.optimization_barrier(tuple(pieces)))
    left_strip, core, right_strip = pieces
    from_left = pass_cols_all(right_strip, 1)
    from_right = pass_cols_all(left_strip, -1)
    core = core.at[:, :, :, :rim].add(from_left)
    core = core.at[:, :, :, frame_cols - 3 * rim :].add(from_right)
    owned = fold_rows(core, rim, pass_rows_all)
    return (owned[0], owned[1])


def solution(mesh):
    return jax.shard_map(
        per_device,
        mesh=mesh,
        in_specs=(
            P("depth", "row", "col"),
            P("depth", "row", "col"),
            P(),
            P("row", "col", None, None, None),
            P("row", "col", None, None),
        ),
        out_specs=(P("depth", "row", "col"), P("depth", "row", "col")),
        check_vma=False,
    )
```

```python
import math

import jax
import jax.numpy as jnp
from jax import lax
from jax.sharding import PartitionSpec as P

exact_mode = lax.Precision.HIGHEST
wave_mode = lax.Precision.HIGH


def from_behind(value, axis, steps):
    count = lax.axis_size(axis)
    leading, last = (max(0, -steps), min(count, count - steps))
    return lax.ppermute(value, axis, [(source, source + steps) for source in range(leading, last)])


def outside_filled(strip, edge):
    return jnp.stack((jnp.where(edge, 1.0, strip[0]), jnp.where(edge, 0.0, strip[1])))


def with_halo(block, sides, width):
    for axis, dim in sides:
        count = lax.axis_size(axis)
        index = lax.axis_index(axis)
        forward = [(i, i + 1) for i in range(count - 1)]
        backward = [(target, source) for source, target in forward]
        low = lax.ppermute(
            lax.slice_in_dim(block, block.shape[dim] - width, None, axis=dim), axis, forward
        )
        high = lax.ppermute(lax.slice_in_dim(block, 0, width, axis=dim), axis, backward)
        low = outside_filled(low, index == 0)
        high = outside_filled(high, index == count - 1)
        block = jnp.concatenate([low, block, high], axis=dim)
    return block


def matmul_exact(first, second):
    return jnp.dot(first, second, precision=exact_mode, preferred_element_type=jnp.float32)


def build_tables(width):
    index = jnp.arange(width, dtype=jnp.int32)
    product = index[:, None] * index[None, :] % width
    angle = product.astype(jnp.float32) * (2.0 * math.pi / width)
    cosine = jnp.cos(angle)
    sine = jnp.sin(angle)
    signed = jnp.where(index < width // 2, index, index - width)
    chirp = -(signed * signed % (4 * width)).astype(jnp.float32) * (2.0 * math.pi / (4 * width))
    chirp_re = jnp.cos(chirp)[None, :]
    chirp_im = jnp.sin(chirp)[None, :]
    scaled_re = cosine * chirp_re - sine * chirp_im
    scaled_im = cosine * chirp_im + sine * chirp_re
    fresnel_re = matmul_exact(scaled_re, cosine) + matmul_exact(scaled_im, sine)
    fresnel_im = matmul_exact(scaled_im, cosine) - matmul_exact(scaled_re, sine)
    fresnel = jnp.stack((fresnel_re, fresnel_im)) / width
    far_field = jnp.stack((cosine, -sine)) / math.sqrt(width)
    return (fresnel, far_field)


def adjoint_of(matrix):
    return jnp.stack((matrix[0].T, -matrix[1].T))


def left_product(matrix, waves, mode):
    return jnp.einsum(
        "ij,bjk->bik", matrix, waves, precision=mode, preferred_element_type=jnp.float32
    )


def right_product(waves, matrix, mode):
    return jnp.einsum(
        "bij,kj->bik", waves, matrix, precision=mode, preferred_element_type=jnp.float32
    )


def propagate(matrix, waves, mode):
    width = matrix.shape[1]
    tall = matrix.reshape(2 * width, width)
    batch = waves.shape[1]
    both = left_product(tall, waves.reshape((2 * batch,) + waves.shape[2:]), mode)
    from_real = both[:batch]
    from_imag = both[batch:]
    inner_re = from_real[:, :width] - from_imag[:, width:]
    inner_im = from_real[:, width:] + from_imag[:, :width]
    right = right_product(jnp.concatenate((inner_re, inner_im)), tall, mode)
    right_re = right[:batch]
    right_im = right[batch:]
    outer_re = right_re[:, :, :width] - right_im[:, :, width:]
    outer_im = right_re[:, :, width:] + right_im[:, :, :width]
    return jnp.stack((outer_re, outer_im))


def forward_layers(wave, slab, matrices):
    moved_list = []
    for layer in range(slab.shape[1]):
        trans_re = slab[0, layer]
        trans_im = slab[1, layer]
        moved = jnp.stack(
            (trans_re * wave[0] - trans_im * wave[1], trans_re * wave[1] + trans_im * wave[0])
        )
        moved_list.append(moved)
        wave = propagate(matrices[layer], moved, exact_mode)
    return (wave, jnp.stack(moved_list, axis=1))


def backward_layers(grad, slab, moved, adjoints):
    layers = slab.shape[1]
    phase_parts = [None] * layers
    absorb_parts = [None] * layers
    for layer in reversed(range(layers)):
        grad_moved = propagate(adjoints[layer], grad, wave_mode)
        moved_re = moved[0, layer]
        moved_im = moved[1, layer]
        phase_parts[layer] = grad_moved[1] * moved_re - grad_moved[0] * moved_im
        absorb_parts[layer] = -(grad_moved[0] * moved_re + grad_moved[1] * moved_im)
        trans_re = slab[0, layer]
        trans_im = slab[1, layer]
        grad = jnp.stack(
            (
                trans_re * grad_moved[0] + trans_im * grad_moved[1],
                trans_re * grad_moved[1] - trans_im * grad_moved[0],
            )
        )
    return (grad, jnp.stack(phase_parts), jnp.stack(absorb_parts))


def pass_rows_all(strip, steps):
    return from_behind(strip, "row", steps)


def pass_cols_all(strip, steps):
    return from_behind(strip, "col", steps)


def fold_rows(grid, rim, mover):
    inner = grid.shape[2] - 2 * rim
    from_above = mover(grid[:, :, inner + rim :], 1)
    from_below = mover(grid[:, :, :rim], -1)
    core = grid[:, :, rim : rim + inner]
    core = core.at[:, :, :rim].add(from_above)
    return core.at[:, :, inner - rim :].add(from_below)


def fold_cols(grid, rim, mover):
    inner = grid.shape[3] - 2 * rim
    from_left = mover(grid[:, :, :, inner + rim :], 1)
    from_right = mover(grid[:, :, :, :rim], -1)
    core = grid[:, :, :, rim : rim + inner]
    core = core.at[:, :, :, :rim].add(from_left)
    return core.at[:, :, :, inner - rim :].add(from_right)


def fold_both(grid, rim, row_mover, col_mover):
    return fold_rows(fold_cols(grid, rim, col_mover), rim, row_mover)


def to_transmit(extended):
    damping = jnp.exp(-extended[1])
    return jnp.stack((damping * jnp.cos(extended[0]), damping * jnp.sin(extended[0])))


def place(patch, row, col, frame):
    height, span = frame
    extra_rows = height - patch.shape[-2]
    extra_cols = span - patch.shape[-1]
    padded = jnp.pad(patch, ((0, 0), (0, 0), (extra_rows, extra_rows), (extra_cols, extra_cols)))
    anchor = jnp.zeros((), jnp.int32)
    start = (anchor, anchor, extra_rows - row, extra_cols - col)
    return lax.dynamic_slice(padded, start, patch.shape[:2] + (height, span))


def issue_order(count):
    half = count // 2
    rest = [shift for shift in range(1, count) if shift != half]
    return [0, half] + rest if count % 2 == 0 and half > 0 else list(range(count))


def per_device(phase, absorption, probe, measured, offsets):
    layers, tile_rows, tile_cols = phase.shape
    width = probe.shape[1]
    rim = width // 2
    probes = offsets.shape[2]
    depth_count = lax.axis_size("depth")
    depth_index = lax.axis_index("depth")
    row_index = lax.axis_index("row")
    col_index = lax.axis_index("col")
    stacked = to_transmit(jnp.stack((phase, absorption)))
    tall_slab = with_halo(stacked, (("row", 2),), rim)
    after = (stacked[0, 0, 0, 0] * 0.0).astype(jnp.int32)
    corners = offsets[0, 0] + after
    row_starts = corners[:, 0] - row_index * tile_rows + rim
    col_starts = corners[:, 1] - col_index * tile_cols + rim
    row_starts = [jnp.clip(row_starts[k], 0, 2 * rim + tile_rows - width) for k in range(probes)]
    col_starts = [jnp.clip(col_starts[k], 0, 2 * rim + tile_cols - width) for k in range(probes)]
    share = probes // depth_count
    source_rows = []
    source_cols = []
    for shift in range(depth_count):
        source = (depth_index - shift) % depth_count
        source_rows.append([lax.select_n(source * share + slot, *row_starts) for slot in range(share)])
        source_cols.append([lax.select_n(source * share + slot, *col_starts) for slot in range(share)])
    row_starts, col_starts, source_rows, source_cols, tall_slab = lax.optimization_barrier(
        (row_starts, col_starts, source_rows, source_cols, tall_slab)
    )
    extended = with_halo(tall_slab, (("col", 3),), rim)
    anchor = jnp.zeros((), jnp.int32)
    fresnel, far_field = build_tables(width)
    share = probes // depth_count
    first = depth_index * share
    cut = jnp.stack(
        [
            lax.dynamic_slice(
                extended, (anchor, anchor, row_starts[k], col_starts[k]), (2, layers, width, width)
            )
            for k in range(probes)
        ],
        axis=2,
    )
    gathered = lax.all_to_all(cut, "depth", 2, 1, tiled=True)
    windows = jnp.swapaxes(gathered, -1, -2)
    total_layers = windows.shape[1]
    matrices = [fresnel] * (total_layers - 1) + [far_field]
    adjoints = [adjoint_of(matrix) for matrix in matrices]
    start_wave = jnp.swapaxes(probe, -1, -2)[:, None]
    far_wave, moved = forward_layers(start_wave, windows, matrices)
    target = jnp.swapaxes(lax.dynamic_slice_in_dim(measured[0, 0], first, share), -1, -2)
    power = far_wave[0] ** 2 + far_wave[1] ** 2
    detector = far_wave * (0.25 * (power - target))[None]
    unused, phase_grad, absorb_grad = backward_layers(detector, windows, moved, adjoints)
    parts = jnp.swapaxes(jnp.stack((phase_grad, absorb_grad)), -1, -2)
    grid = jnp.zeros((2, layers) + extended.shape[2:], jnp.float32)
    for shift in range(depth_count):
        chunk = lax.dynamic_slice_in_dim(
            parts, ((depth_index + shift) % depth_count) * layers, layers, axis=1
        )
        if shift > 0:
            pairs = [(i, (i + shift) % depth_count) for i in range(depth_count)]
            chunk = lax.ppermute(chunk, "depth", pairs)
        for slot in range(share):
            grid = grid + place(
                chunk[:, :, slot], source_rows[shift][slot], source_cols[shift][slot], extended.shape[2:]
            )
        grid = lax.optimization_barrier(grid)
    owned = fold_both(grid, rim, pass_rows_all, pass_cols_all)
    return (owned[0], owned[1])


def solution(mesh):
    return jax.shard_map(
        per_device,
        mesh=mesh,
        in_specs=(
            P("depth", "row", "col"),
            P("depth", "row", "col"),
            P(),
            P("row", "col", None, None, None),
            P("row", "col", None, None),
        ),
        out_specs=(P("depth", "row", "col"), P("depth", "row", "col")),
        check_vma=False,
    )
```

```python
import math

import jax
import jax.numpy as jnp
from jax import lax
from jax.sharding import PartitionSpec as P

exact_mode = lax.Precision.HIGHEST
wave_mode = lax.Precision.HIGH


def from_behind(value, axis, steps):
    count = lax.axis_size(axis)
    leading, last = (max(0, -steps), min(count, count - steps))
    return lax.ppermute(value, axis, [(source, source + steps) for source in range(leading, last)])


def outside_filled(strip, edge):
    return jnp.stack((jnp.where(edge, 1.0, strip[0]), jnp.where(edge, 0.0, strip[1])))


def with_halo(block, sides, width):
    for axis, dim in sides:
        count = lax.axis_size(axis)
        index = lax.axis_index(axis)
        forward = [(i, i + 1) for i in range(count - 1)]
        backward = [(target, source) for source, target in forward]
        low = lax.ppermute(
            lax.slice_in_dim(block, block.shape[dim] - width, None, axis=dim), axis, forward
        )
        high = lax.ppermute(lax.slice_in_dim(block, 0, width, axis=dim), axis, backward)
        low = outside_filled(low, index == 0)
        high = outside_filled(high, index == count - 1)
        block = jnp.concatenate([low, block, high], axis=dim)
    return block


def matmul_exact(first, second):
    return jnp.dot(first, second, precision=exact_mode, preferred_element_type=jnp.float32)


def build_tables(width):
    index = jnp.arange(width, dtype=jnp.int32)
    product = index[:, None] * index[None, :] % width
    angle = product.astype(jnp.float32) * (2.0 * math.pi / width)
    cosine = jnp.cos(angle)
    sine = jnp.sin(angle)
    signed = jnp.where(index < width // 2, index, index - width)
    chirp = -(signed * signed % (4 * width)).astype(jnp.float32) * (2.0 * math.pi / (4 * width))
    chirp_re = jnp.cos(chirp)[None, :]
    chirp_im = jnp.sin(chirp)[None, :]
    scaled_re = cosine * chirp_re - sine * chirp_im
    scaled_im = cosine * chirp_im + sine * chirp_re
    fresnel_re = matmul_exact(scaled_re, cosine) + matmul_exact(scaled_im, sine)
    fresnel_im = matmul_exact(scaled_im, cosine) - matmul_exact(scaled_re, sine)
    fresnel = jnp.stack((fresnel_re, fresnel_im)) / width
    far_field = jnp.stack((cosine, -sine)) / math.sqrt(width)
    return (fresnel, far_field)


def adjoint_of(matrix):
    return jnp.stack((matrix[0].T, -matrix[1].T))


def left_product(matrix, waves, mode):
    return jnp.einsum(
        "ij,bjk->bik", matrix, waves, precision=mode, preferred_element_type=jnp.float32
    )


def right_product(waves, matrix, mode):
    return jnp.einsum(
        "bij,kj->bik", waves, matrix, precision=mode, preferred_element_type=jnp.float32
    )


def propagate(matrix, waves, mode):
    width = matrix.shape[1]
    tall = matrix.reshape(2 * width, width)
    batch = waves.shape[1]
    both = left_product(tall, waves.reshape((2 * batch,) + waves.shape[2:]), mode)
    from_real = both[:batch]
    from_imag = both[batch:]
    inner_re = from_real[:, :width] - from_imag[:, width:]
    inner_im = from_real[:, width:] + from_imag[:, :width]
    right = right_product(jnp.concatenate((inner_re, inner_im)), tall, mode)
    right_re = right[:batch]
    right_im = right[batch:]
    outer_re = right_re[:, :, :width] - right_im[:, :, width:]
    outer_im = right_re[:, :, width:] + right_im[:, :, :width]
    return jnp.stack((outer_re, outer_im))


def forward_layers(wave, slab, matrices):
    moved_list = []
    for layer in range(slab.shape[1]):
        trans_re = slab[0, layer]
        trans_im = slab[1, layer]
        moved = jnp.stack(
            (trans_re * wave[0] - trans_im * wave[1], trans_re * wave[1] + trans_im * wave[0])
        )
        moved_list.append(moved)
        wave = propagate(matrices[layer], moved, exact_mode)
    return (wave, jnp.stack(moved_list, axis=1))


def backward_layers(grad, slab, moved, adjoints):
    layers = slab.shape[1]
    phase_parts = [None] * layers
    absorb_parts = [None] * layers
    for layer in reversed(range(layers)):
        grad_moved = propagate(adjoints[layer], grad, wave_mode)
        moved_re = moved[0, layer]
        moved_im = moved[1, layer]
        phase_parts[layer] = grad_moved[1] * moved_re - grad_moved[0] * moved_im
        absorb_parts[layer] = -(grad_moved[0] * moved_re + grad_moved[1] * moved_im)
        trans_re = slab[0, layer]
        trans_im = slab[1, layer]
        grad = jnp.stack(
            (
                trans_re * grad_moved[0] + trans_im * grad_moved[1],
                trans_re * grad_moved[1] - trans_im * grad_moved[0],
            )
        )
    return (grad, jnp.stack(phase_parts), jnp.stack(absorb_parts))


def pass_rows_all(strip, steps):
    return from_behind(strip, "row", steps)


def pass_cols_all(strip, steps):
    return from_behind(strip, "col", steps)


def fold_rows(grid, rim, mover):
    inner = grid.shape[2] - 2 * rim
    from_above = mover(grid[:, :, inner + rim :], 1)
    from_below = mover(grid[:, :, :rim], -1)
    core = grid[:, :, rim : rim + inner]
    core = core.at[:, :, :rim].add(from_above)
    return core.at[:, :, inner - rim :].add(from_below)


def fold_cols(grid, rim, mover):
    inner = grid.shape[3] - 2 * rim
    from_left = mover(grid[:, :, :, inner + rim :], 1)
    from_right = mover(grid[:, :, :, :rim], -1)
    core = grid[:, :, :, rim : rim + inner]
    core = core.at[:, :, :, :rim].add(from_left)
    return core.at[:, :, :, inner - rim :].add(from_right)


def fold_both(grid, rim, row_mover, col_mover):
    return fold_rows(fold_cols(grid, rim, col_mover), rim, row_mover)


def to_transmit(extended):
    damping = jnp.exp(-extended[1])
    return jnp.stack((damping * jnp.cos(extended[0]), damping * jnp.sin(extended[0])))


def place(patch, row, col, frame):
    height, span = frame
    extra_rows = height - patch.shape[-2]
    extra_cols = span - patch.shape[-1]
    padded = jnp.pad(patch, ((0, 0), (0, 0), (extra_rows, extra_rows), (extra_cols, extra_cols)))
    anchor = jnp.zeros((), jnp.int32)
    start = (anchor, anchor, extra_rows - row, extra_cols - col)
    return lax.dynamic_slice(padded, start, patch.shape[:2] + (height, span))


def issue_order(count):
    half = count // 2
    rest = [shift for shift in range(1, count) if shift != half]
    return [0, half] + rest if count % 2 == 0 and half > 0 else list(range(count))


def per_device(phase, absorption, probe, measured, offsets):
    layers, tile_rows, tile_cols = phase.shape
    width = probe.shape[1]
    rim = width // 2
    probes = offsets.shape[2]
    depth_count = lax.axis_size("depth")
    depth_index = lax.axis_index("depth")
    row_index = lax.axis_index("row")
    col_index = lax.axis_index("col")
    stacked = to_transmit(jnp.stack((phase, absorption)))
    tall_slab = with_halo(stacked, (("row", 2),), rim)
    after = (stacked[0, 0, 0, 0] * 0.0).astype(jnp.int32)
    corners = offsets[0, 0] + after
    row_starts = corners[:, 0] - row_index * tile_rows + rim
    col_starts = corners[:, 1] - col_index * tile_cols + rim
    row_starts = [jnp.clip(row_starts[k], 0, 2 * rim + tile_rows - width) for k in range(probes)]
    col_starts = [jnp.clip(col_starts[k], 0, 2 * rim + tile_cols - width) for k in range(probes)]
    share = probes // depth_count
    source_rows = []
    source_cols = []
    for shift in range(depth_count):
        source = (depth_index - shift) % depth_count
        source_rows.append([lax.select_n(source * share + slot, *row_starts) for slot in range(share)])
        source_cols.append([lax.select_n(source * share + slot, *col_starts) for slot in range(share)])
    row_starts, col_starts, source_rows, source_cols, tall_slab = lax.optimization_barrier(
        (row_starts, col_starts, source_rows, source_cols, tall_slab)
    )
    extended = with_halo(tall_slab, (("col", 3),), rim)
    anchor = jnp.zeros((), jnp.int32)
    fresnel, far_field = build_tables(width)
    share = probes // depth_count
    first = depth_index * share
    cut = jnp.stack(
        [
            lax.dynamic_slice(
                extended, (anchor, anchor, row_starts[k], col_starts[k]), (2, layers, width, width)
            )
            for k in range(probes)
        ],
        axis=2,
    )
    gathered = lax.all_to_all(cut, "depth", 2, 1, tiled=True)
    windows = jnp.swapaxes(gathered, -1, -2)
    total_layers = windows.shape[1]
    matrices = [fresnel] * (total_layers - 1) + [far_field]
    adjoints = [adjoint_of(matrix) for matrix in matrices]
    start_wave = jnp.swapaxes(probe, -1, -2)[:, None]
    far_wave, moved = forward_layers(start_wave, windows, matrices)
    target = jnp.swapaxes(lax.dynamic_slice_in_dim(measured[0, 0], first, share), -1, -2)
    power = far_wave[0] ** 2 + far_wave[1] ** 2
    detector = far_wave * (0.25 * (power - target))[None]
    unused, phase_grad, absorb_grad = backward_layers(detector, windows, moved, adjoints)
    parts = jnp.swapaxes(jnp.stack((phase_grad, absorb_grad)), -1, -2)
    grid = jnp.zeros((2, layers) + extended.shape[2:], jnp.float32)
    for shift in issue_order(depth_count):
        chunk = lax.dynamic_slice_in_dim(
            parts, ((depth_index + shift) % depth_count) * layers, layers, axis=1
        )
        if shift > 0:
            pairs = [(i, (i + shift) % depth_count) for i in range(depth_count)]
            chunk = lax.ppermute(chunk, "depth", pairs)
        for slot in range(share):
            grid = grid + place(
                chunk[:, :, slot], source_rows[shift][slot], source_cols[shift][slot], extended.shape[2:]
            )
        if shift == 0:
            grid = lax.optimization_barrier(grid)
    owned = fold_both(grid, rim, pass_rows_all, pass_cols_all)
    return (owned[0], owned[1])


def solution(mesh):
    return jax.shard_map(
        per_device,
        mesh=mesh,
        in_specs=(
            P("depth", "row", "col"),
            P("depth", "row", "col"),
            P(),
            P("row", "col", None, None, None),
            P("row", "col", None, None),
        ),
        out_specs=(P("depth", "row", "col"), P("depth", "row", "col")),
        check_vma=False,
    )
```
